32 devices in a mesh: gx: 4 (over z), gy: 2 (over y), gz: 4 (over x, core).
Axes of the slice: x: 2, y: 2, z: 4, core: 2. Of those that a mesh axis runs over, the one named last changes fastest.
Arguments:
- residuals: bfloat16 [32, 16, 32, 512], P('gx', 'gy', 'gz'), may hold values from -6 to 6
- patch_box: int32 [3, 2, 512], replicated, may hold values from 0 to 32, as said below
- tile_pairs: int32 [4, 2], replicated, may hold values from 0 to 3, as said below
- inv_tiles: float32 [4, 128, 128], P('gx')
Outputs:
- mixed: bfloat16 [32, 16, 32, 512], P('gx', 'gy', 'gz')
The draws below stay inside these ranges and needn't reach their ends.
Inputs may be any that keep to these rules, and one draw needn't show every extreme that they name: patch_box[a, 0, k] < patch_box[a, 1, k], the box spans at least a quarter and at most three quarters of dimension a's cells, and ends within the grid. `tile_pairs`: rows are distinct pairs of blocks, and every (b, b) is among them.
All inputs are finite; a program needn't handle non-finite values.
Results may differ from the reference program's by a relative error of at most 0.001.
Values sent between devices are 32-bit elements; how exact they have to be, the bound alone decides.
No kernel may reach another device: no remote copies, remote signals or barrier semaphores. Data moves between devices by JAX's collectives and lax.ppermute only.
A program may use at most 64 MiB of HBM per device.

```python
import jax
import jax.numpy as jnp
from jax import lax

ORBS = 512
TB = 128
LEVELS = 4
COARSE = 4
NX = 32
NY = 16
NZ = 32
BLOCKS = 4
NTILES = 4


def pair_table(key):
    base_key = jax.random.fold_in(key, 11)
    key_off = jax.random.fold_in(base_key, 1)
    key_order = jax.random.fold_in(base_key, 2)
    diag_ids = jnp.arange(BLOCKS, dtype=jnp.int32)
    diag_pairs = jnp.stack([diag_ids, diag_ids], axis=1)
    picks = jax.random.permutation(key_off, BLOCKS * (BLOCKS - 1))[:NTILES - BLOCKS].astype(jnp.int32)
    row_ids = picks // (BLOCKS - 1)
    col_part = picks % (BLOCKS - 1)
    col_ids = col_part + (col_part >= row_ids).astype(jnp.int32)
    off_pairs = jnp.stack([row_ids, col_ids], axis=1)
    all_pairs = jnp.concatenate([diag_pairs, off_pairs], axis=0)
    order = jax.random.permutation(key_order, NTILES)
    return all_pairs[order]


def draw_tile_pairs(key, part):
    return pair_table(key)


def draw_inv_tiles(key, part):
    pairs = pair_table(key)
    noise_key = jax.random.fold_in(key, 23)
    noise = jax.random.normal(noise_key, (NTILES, TB, TB), jnp.float32) * 0.05
    on_diag = (pairs[:, 0] == pairs[:, 1]).astype(jnp.float32)
    return noise + on_diag[:, None, None] * jnp.eye(TB, dtype=jnp.float32)[None, :, :]


def draw_patch_box(key, part):
    rows = []
    for dim_id, extent in enumerate([NX, NY, NZ]):
        key_width = jax.random.fold_in(key, 100 + dim_id)
        key_start = jax.random.fold_in(key, 200 + dim_id)
        widths = jax.random.randint(key_width, (ORBS,), extent // 4, 3 * extent // 4 + 1, dtype=jnp.int32)
        starts = jax.random.randint(key_start, (ORBS,), 0, extent - widths + 1, dtype=jnp.int32)
        rows.append(jnp.stack([starts, starts + widths], axis=0))
    return jnp.stack(rows, axis=0)


def level_of(own_key, shape, split, low, largest):
    level = 1.0
    for dim, shards_of in split:
        heights = jax.random.uniform(jax.random.fold_in(jax.random.fold_in(own_key, 6), dim), (shards_of,), jnp.float32, low / len(split), largest / len(split))
        level = level * jnp.repeat(jnp.exp(heights), shape[dim] // shards_of).reshape((-1,) + (1,) * (len(shape) - 1 - dim))
    return level


def centred(key, shape, deviation, limit, cuts=(), kind=jnp.bfloat16):
    result = deviation * jax.random.normal(key, shape, jnp.float32)
    if cuts:
        result = result * level_of(key, shape, cuts, -0.22, 0.18)
    return jnp.clip(result, -limit, limit).astype(kind)


def setup_inputs(seed: int = 0) -> dict:
    keys = jax.random.split(jax.random.key(seed), 5)
    residuals = centred(keys[0], (NX, NY, NZ, ORBS), 1.0, 6.0, ((0, 4), (1, 2), (2, 4)))
    patch_box = draw_patch_box(jax.random.fold_in(keys[4], 71), 0)
    tile_pairs = draw_tile_pairs(jax.random.fold_in(keys[4], 71), 0)
    inv_tiles = draw_inv_tiles(jax.random.fold_in(keys[4], 71), 0)
    return dict(residuals=residuals, patch_box=patch_box, tile_pairs=tile_pairs, inv_tiles=inv_tiles)


omega = 0.8
shift_sigma = 0.01


def level_coeffs(level_id):
    coupling = 0.5 / (4.0 ** level_id)
    return 6.0 * coupling + shift_sigma, coupling


def stencil(padded, level_id):
    center, coupling = level_coeffs(level_id)
    middle = padded[1:-1, 1:-1, 1:-1]
    beside = padded[2:, 1:-1, 1:-1] + padded[:-2, 1:-1, 1:-1]
    beside = beside + padded[1:-1, 2:, 1:-1] + padded[1:-1, :-2, 1:-1]
    beside = beside + padded[1:-1, 1:-1, 2:] + padded[1:-1, 1:-1, :-2]
    return center * middle - coupling * beside


def wrap_pad(field):
    return jnp.pad(field, ((1, 1), (1, 1), (1, 1), (0, 0)), mode="wrap")


def restrict(field):
    size_a, size_b, size_c, width = field.shape
    return field.reshape(size_a // 2, 2, size_b // 2, 2, size_c // 2, 2, width).mean(axis=(1, 3, 5))


def prolong(field):
    return jnp.repeat(jnp.repeat(jnp.repeat(field, 2, 0), 2, 1), 2, 2)


def vcycle(current):
    rhs_list = []
    corr_list = []
    for level_id in range(LEVELS - 1):
        center, coupling = level_coeffs(level_id)
        correct = omega * current / center
        remain = current - stencil(wrap_pad(correct), level_id)
        rhs_list.append(current)
        corr_list.append(correct)
        current = restrict(remain)
    top_level = LEVELS - 1
    center, coupling = level_coeffs(top_level)
    correct = omega * current / center
    for sweep_id in range(COARSE - 1):
        correct = correct + omega * (current - stencil(wrap_pad(correct), top_level)) / center
    for level_id in reversed(range(LEVELS - 1)):
        center, coupling = level_coeffs(level_id)
        updated = corr_list[level_id] + prolong(correct)
        correct = updated + omega * (rhs_list[level_id] - stencil(wrap_pad(updated), level_id)) / center
    return correct


def dim_mask(box_part, extent):
    cells = jnp.arange(extent, dtype=jnp.int32)[:, None]
    return ((box_part[0][None, :] <= cells) & (cells < box_part[1][None, :])).astype(jnp.float32)


def reference(residuals, patch_box, tile_pairs, inv_tiles):
    block_res = residuals.reshape(NX, NY, NZ, BLOCKS, TB).transpose(3, 0, 1, 2, 4)
    block_box = patch_box.reshape(3, 2, BLOCKS, TB).transpose(2, 0, 1, 3)

    def one_block(items):
        res_block, box_block = items
        correct = vcycle(res_block.astype(jnp.float32))
        mask_first = dim_mask(box_block[0], NX)
        mask_second = dim_mask(box_block[1], NY)
        mask_third = dim_mask(box_block[2], NZ)
        return correct * (mask_first[:, None, None, :] * mask_second[None, :, None, :] * mask_third[None, None, :, :])

    precond = lax.map(one_block, (block_res, block_box))

    def column_block(col_id):
        def add_tile(tile_id, total):
            def with_tile(acc_val):
                source = precond[tile_pairs[tile_id, 0]]
                return acc_val + jnp.einsum("xyzk,kj->xyzj", source, inv_tiles[tile_id], precision=lax.Precision.HIGHEST)
            return lax.cond(tile_pairs[tile_id, 1] == col_id, with_tile, lambda acc_val: acc_val, total)
        start_val = jnp.zeros((NX, NY, NZ, TB), jnp.float32)
        return lax.fori_loop(0, NTILES, add_tile, start_val).astype(jnp.bfloat16)

    columns = lax.map(column_block, jnp.arange(BLOCKS, dtype=jnp.int32))
    return columns.transpose(1, 2, 3, 0, 4).reshape(NX, NY, NZ, ORBS)
```

```python
import jax
import jax.numpy as jnp
from jax import lax
from jax.sharding import PartitionSpec as P

LEVELS = 4
COARSE = 4


omega = 0.8
shift_sigma = 0.01

GRID_AXES = (("gx", 0), ("gy", 1), ("gz", 2))


def axis_faces(block, axis, dim):
    count = lax.axis_size(axis)
    first = lax.slice_in_dim(block, 0, 1, axis=dim)
    last = lax.slice_in_dim(block, block.shape[dim] - 1, None, axis=dim)
    if count == 1:
        return last, first
    if count == 2:
        both = lax.ppermute(jnp.concatenate([first, last], axis=dim), axis, [(0, 1), (1, 0)])
        hi = lax.slice_in_dim(both, 0, 1, axis=dim)
        lo = lax.slice_in_dim(both, 1, 2, axis=dim)
        return lo, hi
    forward = [(i, (i + 1) % count) for i in range(count)]
    backward = [((i + 1) % count, i) for i in range(count)]
    lo = lax.ppermute(last, axis, forward)
    hi = lax.ppermute(first, axis, backward)
    return lo, hi


def all_faces(block):
    return [axis_faces(block, axis, dim) for axis, dim in GRID_AXES]


def level_coeffs(level_id):
    coupling = 0.5 / 4.0**level_id
    return (6.0 * coupling + shift_sigma, coupling)


def stencil(block, faces, level_id):
    center, coupling = level_coeffs(level_id)
    beside = None
    for dim, (lo, hi) in enumerate(faces):
        size = block.shape[dim]
        plus = jnp.concatenate([lax.slice_in_dim(block, 1, size, axis=dim), hi], axis=dim)
        minus = jnp.concatenate([lo, lax.slice_in_dim(block, 0, size - 1, axis=dim)], axis=dim)
        pair = plus + minus
        beside = pair if beside is None else beside + pair
    return center * block - coupling * beside


def restrict(field):
    size_a, size_b, size_c, width = field.shape
    return field.reshape(size_a // 2, 2, size_b // 2, 2, size_c // 2, 2, width).mean(axis=(1, 3, 5))


def prolong(field):
    return jnp.repeat(jnp.repeat(jnp.repeat(field, 2, 0), 2, 1), 2, 2)


def dim_mask(box_part, offset, extent):
    cells = offset + jnp.arange(extent, dtype=jnp.int32)[:, None]
    return ((box_part[0][None, :] <= cells) & (cells < box_part[1][None, :])).astype(jnp.float32)


def gram_matrix(inv_tiles, tile_pairs, orb_count):
    count = lax.axis_size("gx")
    local = inv_tiles.shape[0]
    tile_edge = inv_tiles.shape[1]
    me = lax.axis_index("gx")
    total = jnp.zeros((orb_count, orb_count), jnp.float32)
    for shift in range(count):
        if shift == 0:
            piece = inv_tiles
        else:
            piece = lax.ppermute(inv_tiles, "gx", [(i, (i + shift) % count) for i in range(count)])
        owner = (me - shift) % count
        for slot in range(local):
            tile_id = owner * local + slot
            row = tile_pairs[tile_id, 0] * tile_edge
            col = tile_pairs[tile_id, 1] * tile_edge
            total = lax.dynamic_update_slice(total, piece[slot], (row, col))
    return total


def body(residuals, patch_box, tile_pairs, inv_tiles):
    size_a, size_b, size_c, orb_count = residuals.shape
    gram = gram_matrix(inv_tiles, tile_pairs, orb_count)
    current = residuals.astype(jnp.float32)
    rhs_list = []
    corr_list = []
    for level_id in range(LEVELS - 1):
        center, coupling = level_coeffs(level_id)
        correct = omega * current / center
        faces = all_faces(correct)
        remain = current - stencil(correct, faces, level_id)
        rhs_list.append(current)
        corr_list.append(correct)
        current = restrict(remain)
    top_level = LEVELS - 1
    center, coupling = level_coeffs(top_level)
    correct = omega * current / center
    for sweep_id in range(COARSE - 1):
        faces = all_faces(correct)
        correct = correct + omega * (current - stencil(correct, faces, top_level)) / center
    for level_id in reversed(range(LEVELS - 1)):
        center, coupling = level_coeffs(level_id)
        updated = corr_list[level_id] + prolong(correct)
        faces = all_faces(updated)
        correct = updated + omega * (rhs_list[level_id] - stencil(updated, faces, level_id)) / center
    mask_first = dim_mask(patch_box[0], lax.axis_index("gx") * size_a, size_a)
    mask_second = dim_mask(patch_box[1], lax.axis_index("gy") * size_b, size_b)
    mask_third = dim_mask(patch_box[2], lax.axis_index("gz") * size_c, size_c)
    precond = correct * (
        mask_first[:, None, None, :] * mask_second[None, :, None, :] * mask_third[None, None, :, :]
    )
    cell_count = size_a * size_b * size_c
    rows = precond.reshape(cell_count, orb_count)
    mixed = jnp.dot(rows, gram, precision=lax.Precision.HIGHEST, preferred_element_type=jnp.float32)
    return mixed.reshape(size_a, size_b, size_c, orb_count).astype(jnp.bfloat16)


def solution(mesh):
    return jax.shard_map(
        body,
        mesh=mesh,
        in_specs=(P("gx", "gy", "gz", None), P(), P(), P("gx", None, None)),
        out_specs=P("gx", "gy", "gz", None),
        check_vma=False,
    )
```

```python
import jax
import jax.numpy as jnp
from jax import lax
from jax.sharding import PartitionSpec as P

LEVELS = 4
COARSE = 4


omega = 0.8
shift_sigma = 0.01

GRID_AXES = (("gx", 0), ("gy", 1), ("gz", 2))
COARSE_HALO = 10
CHUNK_BYTES = 1 << 21


def shifted(block, axis, offset):
    count = lax.axis_size(axis)
    step = offset % count
    if step == 0:
        return block
    return lax.ppermute(block, axis, [(j, (j - step) % count) for j in range(count)])


def axis_faces(block, axis, dim):
    count = lax.axis_size(axis)
    first = lax.slice_in_dim(block, 0, 1, axis=dim)
    last = lax.slice_in_dim(block, block.shape[dim] - 1, None, axis=dim)
    if count == 1:
        return last, first
    if count == 2:
        both = lax.ppermute(jnp.concatenate([first, last], axis=dim), axis, [(0, 1), (1, 0)])
        hi = lax.slice_in_dim(both, 0, 1, axis=dim)
        lo = lax.slice_in_dim(both, 1, 2, axis=dim)
        return lo, hi
    lo = shifted(last, axis, -1)
    hi = shifted(first, axis, 1)
    return lo, hi


def all_faces(block):
    return [axis_faces(block, axis, dim) for axis, dim in GRID_AXES]


def extend_axis(block, axis, dim, halo):
    count = lax.axis_size(axis)
    size = block.shape[dim]
    reach = -(-halo // size)
    if 2 * reach + 1 >= count:
        offsets = list(range(count))
        start = 0
    else:
        offsets = list(range(-reach, reach + 1))
        start = reach * size
    cache = {}
    pieces = []
    for offset in offsets:
        step = offset % count
        if step not in cache:
            cache[step] = shifted(block, axis, step)
        pieces.append(cache[step])
    return jnp.concatenate(pieces, axis=dim), start


def level_coeffs(level_id):
    coupling = 0.5 / 4.0**level_id
    return (6.0 * coupling + shift_sigma, coupling)


def stencil(block, faces, level_id):
    center, coupling = level_coeffs(level_id)
    beside = None
    for dim, (lo, hi) in enumerate(faces):
        size = block.shape[dim]
        plus = jnp.concatenate([lax.slice_in_dim(block, 1, size, axis=dim), hi], axis=dim)
        minus = jnp.concatenate([lo, lax.slice_in_dim(block, 0, size - 1, axis=dim)], axis=dim)
        pair = plus + minus
        beside = pair if beside is None else beside + pair
    return center * block - coupling * beside


def wrap_faces(block):
    faces = []
    for dim in range(3):
        size = block.shape[dim]
        faces.append(
            (lax.slice_in_dim(block, size - 1, size, axis=dim), lax.slice_in_dim(block, 0, 1, axis=dim))
        )
    return faces


def restrict(field):
    size_a, size_b, size_c, width = field.shape
    return field.reshape(size_a // 2, 2, size_b // 2, 2, size_c // 2, 2, width).mean(axis=(1, 3, 5))


def prolong(field):
    return jnp.repeat(jnp.repeat(jnp.repeat(field, 2, 0), 2, 1), 2, 2)


def periodic_take(field, dim, first, count):
    size = field.shape[dim]
    index = [(first + k) % size for k in range(count)]
    parts = [lax.slice_in_dim(field, i, i + 1, axis=dim) for i in index]
    return jnp.concatenate(parts, axis=dim)


def coarse_solve(rhs_two):
    extended = rhs_two
    starts = []
    for axis, dim in GRID_AXES:
        extended, start = extend_axis(extended, axis, dim, COARSE_HALO)
        starts.append(start)
    width = extended.shape[3]
    chunks = 1
    while extended.size * 4 // chunks > CHUNK_BYTES and width % (2 * chunks * 128) == 0:
        chunks *= 2
    if chunks == 1:
        return coarse_levels(extended, starts, rhs_two.shape)
    part = width // chunks

    def one_chunk(k):
        piece = lax.dynamic_slice_in_dim(extended, k * part, part, axis=3)
        return coarse_levels(piece, starts, rhs_two.shape)

    outs = lax.map(one_chunk, jnp.arange(chunks))
    outs = jnp.moveaxis(outs, 0, 3)
    return outs.reshape(outs.shape[:3] + (width,))


def coarse_levels(extended, starts, block_shape):
    level_two = LEVELS - 2
    center, coupling = level_coeffs(level_two)
    correct_two = omega * extended / center
    remain = extended - stencil(correct_two, wrap_faces(correct_two), level_two)
    current = restrict(remain)
    top_level = LEVELS - 1
    center_top, coupling_top = level_coeffs(top_level)
    correct = omega * current / center_top
    for sweep_id in range(COARSE - 1):
        correct = correct + omega * (current - stencil(correct, wrap_faces(correct), top_level)) / center_top
    updated = correct_two + prolong(correct)
    post = updated + omega * (extended - stencil(updated, wrap_faces(updated), level_two)) / center
    for dim, start in enumerate(starts):
        post = periodic_take(post, dim, start - 1, block_shape[dim] + 2)
    return post


def prolong_face(face, dim):
    for other in range(3):
        if other != dim:
            face = jnp.repeat(face, 2, other)
    return face


def coarse_faces(halo_block, dim):
    inner = halo_block
    for other in range(3):
        if other != dim:
            inner = lax.slice_in_dim(inner, 1, inner.shape[other] - 1, axis=other)
    size = inner.shape[dim]
    lo = lax.slice_in_dim(inner, 0, 1, axis=dim)
    hi = lax.slice_in_dim(inner, size - 1, size, axis=dim)
    return lo, hi


def post_smooth(level_id, corr, corr_faces, rhs, coarse_inner, coarse_face_list):
    center, coupling = level_coeffs(level_id)
    updated = corr + prolong(coarse_inner)
    faces = []
    for dim in range(3):
        lo = corr_faces[dim][0] + prolong_face(coarse_face_list[dim][0], dim)
        hi = corr_faces[dim][1] + prolong_face(coarse_face_list[dim][1], dim)
        faces.append((lo, hi))
    return updated + omega * (rhs - stencil(updated, faces, level_id)) / center


def dim_mask(box_part, offset, extent):
    cells = offset + jnp.arange(extent, dtype=jnp.int32)[:, None]
    return ((box_part[0][None, :] <= cells) & (cells < box_part[1][None, :])).astype(jnp.float32)


def gram_matrix(inv_tiles, tile_pairs, orb_count):
    count = lax.axis_size("gx")
    local = inv_tiles.shape[0]
    tile_edge = inv_tiles.shape[1]
    me = lax.axis_index("gx")
    total = jnp.zeros((orb_count, orb_count), jnp.float32)
    for shift in range(count):
        piece = shifted(inv_tiles, "gx", -shift)
        owner = (me - shift) % count
        for slot in range(local):
            tile_id = owner * local + slot
            row = tile_pairs[tile_id, 0] * tile_edge
            col = tile_pairs[tile_id, 1] * tile_edge
            total = lax.dynamic_update_slice(total, piece[slot], (row, col))
    return total


def vcycle(residuals):
    rhs_zero = residuals.astype(jnp.float32)
    center, coupling = level_coeffs(0)
    corr_zero = omega * rhs_zero / center
    faces_zero = all_faces(corr_zero)
    rhs_one = restrict(rhs_zero - stencil(corr_zero, faces_zero, 0))
    center, coupling = level_coeffs(1)
    corr_one = omega * rhs_one / center
    faces_one = all_faces(corr_one)
    rhs_two = restrict(rhs_one - stencil(corr_one, faces_one, 1))
    post_two = coarse_solve(rhs_two)
    inner_two = post_two[1:-1, 1:-1, 1:-1]
    post_one = post_smooth(
        1, corr_one, faces_one, rhs_one, inner_two, [coarse_faces(post_two, dim) for dim in range(3)]
    )
    return post_smooth(0, corr_zero, faces_zero, rhs_zero, post_one, all_faces(post_one))


def body(residuals, patch_box, tile_pairs, inv_tiles):
    size_a, size_b, size_c, orb_count = residuals.shape
    gram = gram_matrix(inv_tiles, tile_pairs, orb_count)
    correct = vcycle(residuals)
    mask_first = dim_mask(patch_box[0], lax.axis_index("gx") * size_a, size_a)
    mask_second = dim_mask(patch_box[1], lax.axis_index("gy") * size_b, size_b)
    mask_third = dim_mask(patch_box[2], lax.axis_index("gz") * size_c, size_c)
    precond = correct * (
        mask_first[:, None, None, :] * mask_second[None, :, None, :] * mask_third[None, None, :, :]
    )
    cell_count = size_a * size_b * size_c
    rows = precond.reshape(cell_count, orb_count)
    mixed = jnp.dot(rows, gram, precision=lax.Precision.HIGHEST, preferred_element_type=jnp.float32)
    return mixed.reshape(size_a, size_b, size_c, orb_count).astype(jnp.bfloat16)


def solution(mesh):
    return jax.shard_map(
        body,
        mesh=mesh,
        in_specs=(P("gx", "gy", "gz", None), P(), P(), P("gx", None, None)),
        out_specs=P("gx", "gy", "gz", None),
        check_vma=False,
    )
```

```python
import jax
import jax.numpy as jnp
from jax import lax
from jax.sharding import PartitionSpec as P

LEVELS = 4
COARSE = 4


omega = 0.8
shift_sigma = 0.01

GRID_AXES = (("gx", 0), ("gy", 1), ("gz", 2))
COARSE_HALO = 10
CHUNK_BYTES = 1 << 21


def shifted(block, axis, offset):
    count = lax.axis_size(axis)
    step = offset % count
    if step == 0:
        return block
    return lax.ppermute(block, axis, [(j, (j - step) % count) for j in range(count)])


def axis_faces(block, axis, dim):
    count = lax.axis_size(axis)
    first = lax.slice_in_dim(block, 0, 1, axis=dim)
    last = lax.slice_in_dim(block, block.shape[dim] - 1, None, axis=dim)
    if count == 1:
        return last, first
    if count == 2:
        both = lax.ppermute(jnp.concatenate([first, last], axis=dim), axis, [(0, 1), (1, 0)])
        hi = lax.slice_in_dim(both, 0, 1, axis=dim)
        lo = lax.slice_in_dim(both, 1, 2, axis=dim)
        return lo, hi
    lo = shifted(last, axis, -1)
    hi = shifted(first, axis, 1)
    return lo, hi


def all_faces(block):
    return [axis_faces(block, axis, dim) for axis, dim in GRID_AXES]


def extend_axis(block, axis, dim, halo):
    count = lax.axis_size(axis)
    size = block.shape[dim]
    reach = -(-halo // size)
    if 2 * reach + 1 >= count:
        offsets = list(range(count))
        start = 0
    else:
        offsets = list(range(-reach, reach + 1))
        start = reach * size
    cache = {}
    pieces = []
    for offset in offsets:
        step = offset % count
        if step not in cache:
            cache[step] = shifted(block, axis, step)
        pieces.append(cache[step])
    return jnp.concatenate(pieces, axis=dim), start


def level_coeffs(level_id):
    coupling = 0.5 / 4.0**level_id
    return (6.0 * coupling + shift_sigma, coupling)


def pad_with(block, faces):
    padded = block
    for dim, (lo, hi) in enumerate(faces):
        widths = [(0, 0)] * 4
        for other in range(dim):
            widths[other] = (1, 1)
        lo = jnp.pad(lo, widths)
        hi = jnp.pad(hi, widths)
        padded = jnp.concatenate([lo, padded, hi], axis=dim)
    return padded


def stencil(block, faces, level_id):
    center, coupling = level_coeffs(level_id)
    padded = pad_with(block, faces)
    middle = padded[1:-1, 1:-1, 1:-1]
    beside = padded[2:, 1:-1, 1:-1] + padded[:-2, 1:-1, 1:-1]
    beside = beside + padded[1:-1, 2:, 1:-1] + padded[1:-1, :-2, 1:-1]
    beside = beside + padded[1:-1, 1:-1, 2:] + padded[1:-1, 1:-1, :-2]
    return center * middle - coupling * beside


def wrap_faces(block):
    faces = []
    for dim in range(3):
        size = block.shape[dim]
        faces.append(
            (lax.slice_in_dim(block, size - 1, size, axis=dim), lax.slice_in_dim(block, 0, 1, axis=dim))
        )
    return faces


def restrict(field):
    size_a, size_b, size_c, width = field.shape
    return field.reshape(size_a // 2, 2, size_b // 2, 2, size_c // 2, 2, width).mean(axis=(1, 3, 5))


def prolong(field):
    return jnp.repeat(jnp.repeat(jnp.repeat(field, 2, 0), 2, 1), 2, 2)


def periodic_take(field, dim, first, count):
    size = field.shape[dim]
    index = [(first + k) % size for k in range(count)]
    parts = [lax.slice_in_dim(field, i, i + 1, axis=dim) for i in index]
    return jnp.concatenate(parts, axis=dim)


def coarse_solve(rhs_two):
    extended = rhs_two
    starts = []
    for axis, dim in GRID_AXES:
        extended, start = extend_axis(extended, axis, dim, COARSE_HALO)
        starts.append(start)
    width = extended.shape[3]
    chunks = 1
    while extended.size * 4 // chunks > CHUNK_BYTES and width % (2 * chunks * 128) == 0:
        chunks *= 2
    if chunks == 1:
        return coarse_levels(extended, starts, rhs_two.shape)
    part = width // chunks

    def one_chunk(k):
        piece = lax.dynamic_slice_in_dim(extended, k * part, part, axis=3)
        return coarse_levels(piece, starts, rhs_two.shape)

    outs = lax.map(one_chunk, jnp.arange(chunks))
    outs = jnp.moveaxis(outs, 0, 3)
    return outs.reshape(outs.shape[:3] + (width,))


def coarse_levels(extended, starts, block_shape):
    level_two = LEVELS - 2
    center, coupling = level_coeffs(level_two)
    correct_two = omega * extended / center
    remain = extended - stencil(correct_two, wrap_faces(correct_two), level_two)
    current = restrict(remain)
    top_level = LEVELS - 1
    center_top, coupling_top = level_coeffs(top_level)
    correct = omega * current / center_top
    for sweep_id in range(COARSE - 1):
        correct = correct + omega * (current - stencil(correct, wrap_faces(correct), top_level)) / center_top
    updated = correct_two + prolong(correct)
    post = updated + omega * (extended - stencil(updated, wrap_faces(updated), level_two)) / center
    for dim, start in enumerate(starts):
        post = periodic_take(post, dim, start - 1, block_shape[dim] + 2)
    return post


def prolong_face(face, dim):
    for other in range(3):
        if other != dim:
            face = jnp.repeat(face, 2, other)
    return face


def coarse_faces(halo_block, dim):
    inner = halo_block
    for other in range(3):
        if other != dim:
            inner = lax.slice_in_dim(inner, 1, inner.shape[other] - 1, axis=other)
    size = inner.shape[dim]
    lo = lax.slice_in_dim(inner, 0, 1, axis=dim)
    hi = lax.slice_in_dim(inner, size - 1, size, axis=dim)
    return lo, hi


def post_smooth(level_id, corr, corr_faces, rhs, coarse_inner, coarse_face_list):
    center, coupling = level_coeffs(level_id)
    updated = corr + prolong(coarse_inner)
    faces = []
    for dim in range(3):
        lo = corr_faces[dim][0] + prolong_face(coarse_face_list[dim][0], dim)
        hi = corr_faces[dim][1] + prolong_face(coarse_face_list[dim][1], dim)
        faces.append((lo, hi))
    return updated + omega * (rhs - stencil(updated, faces, level_id)) / center


def dim_mask(box_part, offset, extent):
    cells = offset + jnp.arange(extent, dtype=jnp.int32)[:, None]
    return ((box_part[0][None, :] <= cells) & (cells < box_part[1][None, :])).astype(jnp.float32)


def gram_matrix(inv_tiles, tile_pairs, orb_count):
    count = lax.axis_size("gx")
    local = inv_tiles.shape[0]
    tile_edge = inv_tiles.shape[1]
    me = lax.axis_index("gx")
    total = jnp.zeros((orb_count, orb_count), jnp.float32)
    for shift in range(count):
        piece = shifted(inv_tiles, "gx", -shift)
        owner = (me - shift) % count
        for slot in range(local):
            tile_id = owner * local + slot
            row = tile_pairs[tile_id, 0] * tile_edge
            col = tile_pairs[tile_id, 1] * tile_edge
            total = lax.dynamic_update_slice(total, piece[slot], (row, col))
    return total


def vcycle(residuals):
    rhs_zero = residuals.astype(jnp.float32)
    center, coupling = level_coeffs(0)
    corr_zero = omega * rhs_zero / center
    faces_zero = all_faces(corr_zero)
    rhs_one = restrict(rhs_zero - stencil(corr_zero, faces_zero, 0))
    center, coupling = level_coeffs(1)
    corr_one = omega * rhs_one / center
    faces_one = all_faces(corr_one)
    rhs_two = restrict(rhs_one - stencil(corr_one, faces_one, 1))
    post_two = coarse_solve(rhs_two)
    inner_two = post_two[1:-1, 1:-1, 1:-1]
    post_one = post_smooth(
        1, corr_one, faces_one, rhs_one, inner_two, [coarse_faces(post_two, dim) for dim in range(3)]
    )
    return post_smooth(0, corr_zero, faces_zero, rhs_zero, post_one, all_faces(post_one))


def body(residuals, patch_box, tile_pairs, inv_tiles):
    size_a, size_b, size_c, orb_count = residuals.shape
    gram = gram_matrix(inv_tiles, tile_pairs, orb_count)
    correct = vcycle(residuals)
    mask_first = dim_mask(patch_box[0], lax.axis_index("gx") * size_a, size_a)
    mask_second = dim_mask(patch_box[1], lax.axis_index("gy") * size_b, size_b)
    mask_third = dim_mask(patch_box[2], lax.axis_index("gz") * size_c, size_c)
    precond = correct * (
        mask_first[:, None, None, :] * mask_second[None, :, None, :] * mask_third[None, None, :, :]
    )
    cell_count = size_a * size_b * size_c
    rows = precond.reshape(cell_count, orb_count)
    mixed = jnp.dot(rows, gram, precision=lax.Precision.HIGHEST, preferred_element_type=jnp.float32)
    return mixed.reshape(size_a, size_b, size_c, orb_count).astype(jnp.bfloat16)


def solution(mesh):
    return jax.shard_map(
        body,
        mesh=mesh,
        in_specs=(P("gx", "gy", "gz", None), P(), P(), P("gx", None, None)),
        out_specs=P("gx", "gy", "gz", None),
        check_vma=False,
    )
```

```python
import jax
import jax.numpy as jnp
from jax import lax
from jax.sharding import PartitionSpec as P

LEVELS = 4
COARSE = 4


omega = 0.8
shift_sigma = 0.01

GRID_AXES = (("gx", 0), ("gy", 1), ("gz", 2))
COARSE_HALO = 10
CHUNK_BYTES = 1 << 21


def shifted(block, axis, offset):
    count = lax.axis_size(axis)
    step = offset % count
    if step == 0:
        return block
    return lax.ppermute(block, axis, [(j, (j - step) % count) for j in range(count)])


def axis_faces(block, axis, dim):
    count = lax.axis_size(axis)
    first = lax.slice_in_dim(block, 0, 1, axis=dim)
    last = lax.slice_in_dim(block, block.shape[dim] - 1, None, axis=dim)
    if count == 1:
        return last, first
    if count == 2:
        both = lax.ppermute(jnp.concatenate([first, last], axis=dim), axis, [(0, 1), (1, 0)])
        hi = lax.slice_in_dim(both, 0, 1, axis=dim)
        lo = lax.slice_in_dim(both, 1, 2, axis=dim)
        return lo, hi
    lo = shifted(last, axis, -1)
    hi = shifted(first, axis, 1)
    return lo, hi


def all_faces(block):
    return [axis_faces(block, axis, dim) for axis, dim in GRID_AXES]


def extend_axis(block, axis, dim, halo, extra=None):
    count = lax.axis_size(axis)
    size = block.shape[dim]
    reach = -(-halo // size)
    if 2 * reach + 1 >= count:
        offsets = list(range(count))
        start = 0
    else:
        offsets = list(range(-reach, reach + 1))
        start = reach * size
    cache = {}
    extras = {}
    pieces = []
    for offset in offsets:
        step = offset % count
        if step not in cache:
            if extra is None or step == 0:
                cache[step] = shifted(block, axis, step)
                extras[step] = extra
            else:
                both = jnp.concatenate([block.reshape(-1), extra.reshape(-1)])
                both = shifted(both, axis, step)
                cache[step] = both[: block.size].reshape(block.shape)
                extras[step] = both[block.size :].reshape(extra.shape)
        pieces.append(cache[step])
    return jnp.concatenate(pieces, axis=dim), start, extras


def level_coeffs(level_id):
    coupling = 0.5 / 4.0**level_id
    return (6.0 * coupling + shift_sigma, coupling)


def pad_with(block, faces):
    padded = block
    for dim, (lo, hi) in enumerate(faces):
        widths = [(0, 0)] * 4
        for other in range(dim):
            widths[other] = (1, 1)
        lo = jnp.pad(lo, widths)
        hi = jnp.pad(hi, widths)
        padded = jnp.concatenate([lo, padded, hi], axis=dim)
    return padded


def stencil(block, faces, level_id):
    center, coupling = level_coeffs(level_id)
    padded = pad_with(block, faces)
    middle = padded[1:-1, 1:-1, 1:-1]
    beside = padded[2:, 1:-1, 1:-1] + padded[:-2, 1:-1, 1:-1]
    beside = beside + padded[1:-1, 2:, 1:-1] + padded[1:-1, :-2, 1:-1]
    beside = beside + padded[1:-1, 1:-1, 2:] + padded[1:-1, 1:-1, :-2]
    return center * middle - coupling * beside


def wrap_faces(block):
    faces = []
    for dim in range(3):
        size = block.shape[dim]
        faces.append(
            (lax.slice_in_dim(block, size - 1, size, axis=dim), lax.slice_in_dim(block, 0, 1, axis=dim))
        )
    return faces


def restrict(field):
    size_a, size_b, size_c, width = field.shape
    return field.reshape(size_a // 2, 2, size_b // 2, 2, size_c // 2, 2, width).mean(axis=(1, 3, 5))


def prolong(field):
    return jnp.repeat(jnp.repeat(jnp.repeat(field, 2, 0), 2, 1), 2, 2)


def periodic_take(field, dim, first, count):
    size = field.shape[dim]
    index = [(first + k) % size for k in range(count)]
    parts = [lax.slice_in_dim(field, i, i + 1, axis=dim) for i in index]
    return jnp.concatenate(parts, axis=dim)


def coarse_solve(rhs_two, tiles):
    extended = rhs_two
    starts = []
    tiles_by_step = {}
    for axis, dim in GRID_AXES:
        extra = tiles if axis == "gx" else None
        extended, start, extras = extend_axis(extended, axis, dim, COARSE_HALO, extra)
        if axis == "gx":
            tiles_by_step = extras
        starts.append(start)
    width = extended.shape[3]
    chunks = 1
    while extended.size * 4 // chunks > CHUNK_BYTES and width % (2 * chunks * 128) == 0:
        chunks *= 2
    if chunks == 1:
        return coarse_levels(extended, starts, rhs_two.shape), tiles_by_step
    part = width // chunks

    def one_chunk(k):
        piece = lax.dynamic_slice_in_dim(extended, k * part, part, axis=3)
        return coarse_levels(piece, starts, rhs_two.shape)

    outs = lax.map(one_chunk, jnp.arange(chunks))
    outs = jnp.moveaxis(outs, 0, 3)
    return outs.reshape(outs.shape[:3] + (width,)), tiles_by_step


def coarse_levels(extended, starts, block_shape):
    level_two = LEVELS - 2
    center, coupling = level_coeffs(level_two)
    correct_two = omega * extended / center
    remain = extended - stencil(correct_two, wrap_faces(correct_two), level_two)
    current = restrict(remain)
    top_level = LEVELS - 1
    center_top, coupling_top = level_coeffs(top_level)
    correct = omega * current / center_top
    for sweep_id in range(COARSE - 1):
        correct = correct + omega * (current - stencil(correct, wrap_faces(correct), top_level)) / center_top
    updated = correct_two + prolong(correct)
    post = updated + omega * (extended - stencil(updated, wrap_faces(updated), level_two)) / center
    for dim, start in enumerate(starts):
        post = periodic_take(post, dim, start - 1, block_shape[dim] + 2)
    return post


def prolong_face(face, dim):
    for other in range(3):
        if other != dim:
            face = jnp.repeat(face, 2, other)
    return face


def coarse_faces(halo_block, dim):
    inner = halo_block
    for other in range(3):
        if other != dim:
            inner = lax.slice_in_dim(inner, 1, inner.shape[other] - 1, axis=other)
    size = inner.shape[dim]
    lo = lax.slice_in_dim(inner, 0, 1, axis=dim)
    hi = lax.slice_in_dim(inner, size - 1, size, axis=dim)
    return lo, hi


def post_smooth(level_id, corr, corr_faces, rhs, coarse_inner, coarse_face_list):
    center, coupling = level_coeffs(level_id)
    updated = corr + prolong(coarse_inner)
    faces = []
    for dim in range(3):
        lo = corr_faces[dim][0] + prolong_face(coarse_face_list[dim][0], dim)
        hi = corr_faces[dim][1] + prolong_face(coarse_face_list[dim][1], dim)
        faces.append((lo, hi))
    return updated + omega * (rhs - stencil(updated, faces, level_id)) / center


def dim_mask(box_part, offset, extent):
    cells = offset + jnp.arange(extent, dtype=jnp.int32)[:, None]
    return ((box_part[0][None, :] <= cells) & (cells < box_part[1][None, :])).astype(jnp.float32)


def gram_matrix(tiles_by_step, inv_tiles, tile_pairs, orb_count):
    count = lax.axis_size("gx")
    local = inv_tiles.shape[0]
    tile_edge = inv_tiles.shape[1]
    me = lax.axis_index("gx")
    total = jnp.zeros((orb_count, orb_count), jnp.float32)
    for step in range(count):
        piece = tiles_by_step.get(step)
        if piece is None:
            piece = inv_tiles if step == 0 else shifted(inv_tiles, "gx", step)
        owner = (me + step) % count
        for slot in range(local):
            tile_id = owner * local + slot
            row = tile_pairs[tile_id, 0] * tile_edge
            col = tile_pairs[tile_id, 1] * tile_edge
            total = lax.dynamic_update_slice(total, piece[slot], (row, col))
    return total


def vcycle(residuals, inv_tiles):
    rhs_zero = residuals.astype(jnp.float32)
    center, coupling = level_coeffs(0)
    corr_zero = omega * rhs_zero / center
    faces_zero = all_faces(corr_zero)
    rhs_one = restrict(rhs_zero - stencil(corr_zero, faces_zero, 0))
    center, coupling = level_coeffs(1)
    corr_one = omega * rhs_one / center
    faces_one = all_faces(corr_one)
    rhs_two = restrict(rhs_one - stencil(corr_one, faces_one, 1))
    post_two, tiles_by_step = coarse_solve(rhs_two, inv_tiles)
    inner_two = post_two[1:-1, 1:-1, 1:-1]
    post_one = post_smooth(
        1, corr_one, faces_one, rhs_one, inner_two, [coarse_faces(post_two, dim) for dim in range(3)]
    )
    return post_smooth(0, corr_zero, faces_zero, rhs_zero, post_one, all_faces(post_one)), tiles_by_step


def body(residuals, patch_box, tile_pairs, inv_tiles):
    size_a, size_b, size_c, orb_count = residuals.shape
    correct, tiles_by_step = vcycle(residuals, inv_tiles)
    gram = gram_matrix(tiles_by_step, inv_tiles, tile_pairs, orb_count)
    mask_first = dim_mask(patch_box[0], lax.axis_index("gx") * size_a, size_a)
    mask_second = dim_mask(patch_box[1], lax.axis_index("gy") * size_b, size_b)
    mask_third = dim_mask(patch_box[2], lax.axis_index("gz") * size_c, size_c)
    precond = correct * (
        mask_first[:, None, None, :] * mask_second[None, :, None, :] * mask_third[None, None, :, :]
    )
    cell_count = size_a * size_b * size_c
    rows = precond.reshape(cell_count, orb_count)
    mixed = jnp.dot(rows, gram, precision=lax.Precision.HIGH, preferred_element_type=jnp.float32)
    return mixed.reshape(size_a, size_b, size_c, orb_count).astype(jnp.bfloat16)


def solution(mesh):
    return jax.shard_map(
        body,
        mesh=mesh,
        in_specs=(P("gx", "gy", "gz", None), P(), P(), P("gx", None, None)),
        out_specs=P("gx", "gy", "gz", None),
        check_vma=False,
    )
```

```python
import jax
import jax.numpy as jnp
from jax import lax
from jax.sharding import PartitionSpec as P

LEVELS = 4
COARSE = 4


omega = 0.8
shift_sigma = 0.01

GRID_AXES = (("gx", 0), ("gy", 1), ("gz", 2))
COARSE_HALO = 10
CHUNK_BYTES = 1 << 21


def shifted(block, axis, offset):
    count = lax.axis_size(axis)
    step = offset % count
    if step == 0:
        return block
    return lax.ppermute(block, axis, [(j, (j - step) % count) for j in range(count)])


def axis_faces(block, axis, dim):
    count = lax.axis_size(axis)
    first = lax.slice_in_dim(block, 0, 1, axis=dim)
    last = lax.slice_in_dim(block, block.shape[dim] - 1, None, axis=dim)
    if count == 1:
        return last, first
    if count == 2:
        both = lax.ppermute(jnp.concatenate([first, last], axis=dim), axis, [(0, 1), (1, 0)])
        hi = lax.slice_in_dim(both, 0, 1, axis=dim)
        lo = lax.slice_in_dim(both, 1, 2, axis=dim)
        return lo, hi
    lo = shifted(last, axis, -1)
    hi = shifted(first, axis, 1)
    return lo, hi


def all_faces(block):
    return [axis_faces(block, axis, dim) for axis, dim in GRID_AXES]


def extend_axis(block, axis, dim, halo, extra=None):
    count = lax.axis_size(axis)
    size = block.shape[dim]
    reach = -(-halo // size)
    if 2 * reach + 1 >= count:
        offsets = list(range(count))
        start = 0
    else:
        offsets = list(range(-reach, reach + 1))
        start = reach * size
    cache = {}
    extras = {}
    pieces = []
    for offset in offsets:
        step = offset % count
        if step not in cache:
            if extra is None or step == 0:
                cache[step] = shifted(block, axis, step)
                extras[step] = extra
            else:
                both = jnp.concatenate([block.reshape(-1), extra.reshape(-1)])
                both = shifted(both, axis, step)
                cache[step] = both[: block.size].reshape(block.shape)
                extras[step] = both[block.size :].reshape(extra.shape)
        pieces.append(cache[step])
    return jnp.concatenate(pieces, axis=dim), start, extras


def axis_offsets(count, size, halo):
    reach = -(-halo // size)
    if 2 * reach + 1 >= count:
        return list(range(count)), 0
    return list(range(-reach, reach + 1)), reach * size


def extend_joint(block, axes, dims, halo):
    counts = [lax.axis_size(axis) for axis in axes]
    plans = [axis_offsets(count, block.shape[dim], halo) for count, dim in zip(counts, dims)]
    cache = {}

    def fetch(offset):
        steps = tuple(o % c for o, c in zip(offset, counts))
        if steps not in cache:
            if not any(steps):
                cache[steps] = block
            else:
                pairs = []
                for target in range(_prod(counts)):
                    coords = _unravel(target, counts)
                    source = _ravel([(c + s) % n for c, s, n in zip(coords, steps, counts)], counts)
                    pairs.append((source, target))
                cache[steps] = lax.ppermute(block, tuple(axes), pairs)
        return cache[steps]

    def assemble(level, prefix):
        offsets, start = plans[level]
        if level == len(axes) - 1:
            pieces = [fetch(prefix + (o,)) for o in offsets]
        else:
            pieces = [assemble(level + 1, prefix + (o,)) for o in offsets]
        return jnp.concatenate(pieces, axis=dims[level])

    return assemble(0, ()), [start for offsets, start in plans]


def _prod(values):
    total = 1
    for v in values:
        total *= v
    return total


def _unravel(index, counts):
    coords = []
    for n in reversed(counts):
        coords.append(index % n)
        index //= n
    return list(reversed(coords))


def _ravel(coords, counts):
    index = 0
    for c, n in zip(coords, counts):
        index = index * n + c
    return index


def level_coeffs(level_id):
    coupling = 0.5 / 4.0**level_id
    return (6.0 * coupling + shift_sigma, coupling)


def pad_with(block, faces):
    padded = block
    for dim, (lo, hi) in enumerate(faces):
        widths = [(0, 0)] * 4
        for other in range(dim):
            widths[other] = (1, 1)
        lo = jnp.pad(lo, widths)
        hi = jnp.pad(hi, widths)
        padded = jnp.concatenate([lo, padded, hi], axis=dim)
    return padded


def stencil(block, faces, level_id):
    center, coupling = level_coeffs(level_id)
    padded = pad_with(block, faces)
    middle = padded[1:-1, 1:-1, 1:-1]
    beside = padded[2:, 1:-1, 1:-1] + padded[:-2, 1:-1, 1:-1]
    beside = beside + padded[1:-1, 2:, 1:-1] + padded[1:-1, :-2, 1:-1]
    beside = beside + padded[1:-1, 1:-1, 2:] + padded[1:-1, 1:-1, :-2]
    return center * middle - coupling * beside


def wrap_faces(block):
    faces = []
    for dim in range(3):
        size = block.shape[dim]
        faces.append(
            (lax.slice_in_dim(block, size - 1, size, axis=dim), lax.slice_in_dim(block, 0, 1, axis=dim))
        )
    return faces


def restrict(field):
    size_a, size_b, size_c, width = field.shape
    return field.reshape(size_a // 2, 2, size_b // 2, 2, size_c // 2, 2, width).mean(axis=(1, 3, 5))


def prolong(field):
    return jnp.repeat(jnp.repeat(jnp.repeat(field, 2, 0), 2, 1), 2, 2)


def periodic_take(field, dim, first, count):
    size = field.shape[dim]
    index = [(first + k) % size for k in range(count)]
    parts = [lax.slice_in_dim(field, i, i + 1, axis=dim) for i in index]
    return jnp.concatenate(parts, axis=dim)


def coarse_solve(rhs_two, tiles):
    extended = rhs_two
    starts = []
    tiles_by_step = {}
    extended, start, tiles_by_step = extend_axis(extended, "gx", 0, COARSE_HALO, tiles)
    starts.append(start)
    extended, joint_starts = extend_joint(extended, ("gy", "gz"), (1, 2), COARSE_HALO)
    starts.extend(joint_starts)
    width = extended.shape[3]
    chunks = 1
    while extended.size * 4 // chunks > CHUNK_BYTES and width % (2 * chunks * 128) == 0:
        chunks *= 2
    if chunks == 1:
        return coarse_levels(extended, starts, rhs_two.shape), tiles_by_step
    part = width // chunks

    def one_chunk(k):
        piece = lax.dynamic_slice_in_dim(extended, k * part, part, axis=3)
        return coarse_levels(piece, starts, rhs_two.shape)

    outs = lax.map(one_chunk, jnp.arange(chunks))
    outs = jnp.moveaxis(outs, 0, 3)
    return outs.reshape(outs.shape[:3] + (width,)), tiles_by_step


def coarse_levels(extended, starts, block_shape):
    level_two = LEVELS - 2
    center, coupling = level_coeffs(level_two)
    correct_two = omega * extended / center
    remain = extended - stencil(correct_two, wrap_faces(correct_two), level_two)
    current = restrict(remain)
    top_level = LEVELS - 1
    center_top, coupling_top = level_coeffs(top_level)
    correct = omega * current / center_top
    for sweep_id in range(COARSE - 1):
        correct = correct + omega * (current - stencil(correct, wrap_faces(correct), top_level)) / center_top
    updated = correct_two + prolong(correct)
    post = updated + omega * (extended - stencil(updated, wrap_faces(updated), level_two)) / center
    for dim, start in enumerate(starts):
        post = periodic_take(post, dim, start - 1, block_shape[dim] + 2)
    return post


def prolong_face(face, dim):
    for other in range(3):
        if other != dim:
            face = jnp.repeat(face, 2, other)
    return face


def coarse_faces(halo_block, dim):
    inner = halo_block
    for other in range(3):
        if other != dim:
            inner = lax.slice_in_dim(inner, 1, inner.shape[other] - 1, axis=other)
    size = inner.shape[dim]
    lo = lax.slice_in_dim(inner, 0, 1, axis=dim)
    hi = lax.slice_in_dim(inner, size - 1, size, axis=dim)
    return lo, hi


def post_smooth(level_id, corr, corr_faces, rhs, coarse_inner, coarse_face_list):
    center, coupling = level_coeffs(level_id)
    updated = corr + prolong(coarse_inner)
    faces = []
    for dim in range(3):
        lo = corr_faces[dim][0] + prolong_face(coarse_face_list[dim][0], dim)
        hi = corr_faces[dim][1] + prolong_face(coarse_face_list[dim][1], dim)
        faces.append((lo, hi))
    return updated + omega * (rhs - stencil(updated, faces, level_id)) / center


def dim_mask(box_part, offset, extent):
    cells = offset + jnp.arange(extent, dtype=jnp.int32)[:, None]
    return ((box_part[0][None, :] <= cells) & (cells < box_part[1][None, :])).astype(jnp.float32)


def gram_matrix(tiles_by_step, inv_tiles, tile_pairs, orb_count):
    count = lax.axis_size("gx")
    local = inv_tiles.shape[0]
    tile_edge = inv_tiles.shape[1]
    me = lax.axis_index("gx")
    total = jnp.zeros((orb_count, orb_count), jnp.float32)
    for step in range(count):
        piece = tiles_by_step.get(step)
        if piece is None:
            piece = inv_tiles if step == 0 else shifted(inv_tiles, "gx", step)
        owner = (me + step) % count
        for slot in range(local):
            tile_id = owner * local + slot
            row = tile_pairs[tile_id, 0] * tile_edge
            col = tile_pairs[tile_id, 1] * tile_edge
            total = lax.dynamic_update_slice(total, piece[slot], (row, col))
    return total


def vcycle(residuals, inv_tiles):
    rhs_zero = residuals.astype(jnp.float32)
    center, coupling = level_coeffs(0)
    corr_zero = omega * rhs_zero / center
    faces_zero = all_faces(corr_zero)
    rhs_one = restrict(rhs_zero - stencil(corr_zero, faces_zero, 0))
    center, coupling = level_coeffs(1)
    corr_one = omega * rhs_one / center
    faces_one = all_faces(corr_one)
    rhs_two = restrict(rhs_one - stencil(corr_one, faces_one, 1))
    post_two, tiles_by_step = coarse_solve(rhs_two, inv_tiles)
    inner_two = post_two[1:-1, 1:-1, 1:-1]
    post_one = post_smooth(
        1, corr_one, faces_one, rhs_one, inner_two, [coarse_faces(post_two, dim) for dim in range(3)]
    )
    return post_smooth(0, corr_zero, faces_zero, rhs_zero, post_one, all_faces(post_one)), tiles_by_step


def body(residuals, patch_box, tile_pairs, inv_tiles):
    size_a, size_b, size_c, orb_count = residuals.shape
    correct, tiles_by_step = vcycle(residuals, inv_tiles)
    gram = gram_matrix(tiles_by_step, inv_tiles, tile_pairs, orb_count)
    mask_first = dim_mask(patch_box[0], lax.axis_index("gx") * size_a, size_a)
    mask_second = dim_mask(patch_box[1], lax.axis_index("gy") * size_b, size_b)
    mask_third = dim_mask(patch_box[2], lax.axis_index("gz") * size_c, size_c)
    precond = correct * (
        mask_first[:, None, None, :] * mask_second[None, :, None, :] * mask_third[None, None, :, :]
    )
    cell_count = size_a * size_b * size_c
    rows = precond.reshape(cell_count, orb_count)
    mixed = jnp.dot(rows, gram, precision=lax.Precision.HIGH, preferred_element_type=jnp.float32)
    return mixed.reshape(size_a, size_b, size_c, orb_count).astype(jnp.bfloat16)


def solution(mesh):
    return jax.shard_map(
        body,
        mesh=mesh,
        in_specs=(P("gx", "gy", "gz", None), P(), P(), P("gx", None, None)),
        out_specs=P("gx", "gy", "gz", None),
        check_vma=False,
    )
```

```python
import jax
import jax.numpy as jnp
from jax import lax
from jax.sharding import PartitionSpec as P

LEVELS = 4
COARSE = 4


omega = 0.8
shift_sigma = 0.01

GRID_AXES = (("gx", 0), ("gy", 1), ("gz", 2))
COARSE_HALO = 10
CHUNK_BYTES = 1 << 21
LANES = 128


def shifted(block, axis, offset):
    count = lax.axis_size(axis)
    step = offset % count
    if step == 0:
        return block
    return lax.ppermute(block, axis, [(j, (j - step) % count) for j in range(count)])


def axis_faces(block, axis, dim):
    count = lax.axis_size(axis)
    first = lax.slice_in_dim(block, 0, 1, axis=dim)
    last = lax.slice_in_dim(block, block.shape[dim] - 1, None, axis=dim)
    if count == 1:
        return last, first
    if count == 2:
        both = lax.ppermute(jnp.concatenate([first, last], axis=dim), axis, [(0, 1), (1, 0)])
        hi = lax.slice_in_dim(both, 0, 1, axis=dim)
        lo = lax.slice_in_dim(both, 1, 2, axis=dim)
        return lo, hi
    lo = shifted(last, axis, -1)
    hi = shifted(first, axis, 1)
    return lo, hi


def all_faces(block):
    return [axis_faces(block, axis, dim) for axis, dim in GRID_AXES]


def extend_axis(block, axis, dim, halo, extra=None):
    count = lax.axis_size(axis)
    size = block.shape[dim]
    reach = -(-halo // size)
    if 2 * reach + 1 >= count:
        offsets = list(range(count))
        start = 0
    else:
        offsets = list(range(-reach, reach + 1))
        start = reach * size
    cache = {}
    extras = {}
    pieces = []
    for offset in offsets:
        step = offset % count
        if step not in cache:
            if extra is None or step == 0:
                cache[step] = shifted(block, axis, step)
                extras[step] = extra
            else:
                both = jnp.concatenate([block.reshape(-1), extra.reshape(-1)])
                both = shifted(both, axis, step)
                cache[step] = both[: block.size].reshape(block.shape)
                extras[step] = both[block.size :].reshape(extra.shape)
        pieces.append(cache[step])
    return jnp.concatenate(pieces, axis=dim), start, extras


def axis_offsets(count, size, halo):
    reach = -(-halo // size)
    if 2 * reach + 1 >= count:
        return list(range(count)), 0
    return list(range(-reach, reach + 1)), reach * size


def extend_joint(block, axes, dims, halo):
    counts = [lax.axis_size(axis) for axis in axes]
    plans = [axis_offsets(count, block.shape[dim], halo) for count, dim in zip(counts, dims)]
    cache = {}

    def fetch(offset):
        steps = tuple(o % c for o, c in zip(offset, counts))
        if steps not in cache:
            if not any(steps):
                cache[steps] = block
            else:
                pairs = []
                for target in range(_prod(counts)):
                    coords = _unravel(target, counts)
                    source = _ravel([(c + s) % n for c, s, n in zip(coords, steps, counts)], counts)
                    pairs.append((source, target))
                cache[steps] = lax.ppermute(block, tuple(axes), pairs)
        return cache[steps]

    def assemble(level, prefix):
        offsets, start = plans[level]
        if level == len(axes) - 1:
            pieces = [fetch(prefix + (o,)) for o in offsets]
        else:
            pieces = [assemble(level + 1, prefix + (o,)) for o in offsets]
        return jnp.concatenate(pieces, axis=dims[level])

    return assemble(0, ()), [start for offsets, start in plans]


def _prod(values):
    total = 1
    for v in values:
        total *= v
    return total


def _unravel(index, counts):
    coords = []
    for n in reversed(counts):
        coords.append(index % n)
        index //= n
    return list(reversed(coords))


def _ravel(coords, counts):
    index = 0
    for c, n in zip(coords, counts):
        index = index * n + c
    return index


def level_coeffs(level_id):
    coupling = 0.5 / 4.0**level_id
    return (6.0 * coupling + shift_sigma, coupling)


def pad_with(block, faces):
    padded = block
    for dim, (lo, hi) in enumerate(faces):
        widths = [(0, 0)] * block.ndim
        for other in range(dim):
            widths[other] = (1, 1)
        lo = jnp.pad(lo, widths)
        hi = jnp.pad(hi, widths)
        padded = jnp.concatenate([lo, padded, hi], axis=dim)
    return padded


def stencil(block, faces, level_id):
    center, coupling = level_coeffs(level_id)
    padded = pad_with(block, faces)
    middle = padded[1:-1, 1:-1, 1:-1]
    beside = padded[2:, 1:-1, 1:-1] + padded[:-2, 1:-1, 1:-1]
    beside = beside + padded[1:-1, 2:, 1:-1] + padded[1:-1, :-2, 1:-1]
    beside = beside + padded[1:-1, 1:-1, 2:] + padded[1:-1, 1:-1, :-2]
    return center * middle - coupling * beside


def wrap_faces(block):
    faces = []
    for dim in range(3):
        size = block.shape[dim]
        faces.append(
            (lax.slice_in_dim(block, size - 1, size, axis=dim), lax.slice_in_dim(block, 0, 1, axis=dim))
        )
    return faces


def restrict(field):
    size_a, size_b, size_c = field.shape[:3]
    rest = field.shape[3:]
    return field.reshape((size_a // 2, 2, size_b // 2, 2, size_c // 2, 2) + rest).mean(axis=(1, 3, 5))


def prolong(field):
    return jnp.repeat(jnp.repeat(jnp.repeat(field, 2, 0), 2, 1), 2, 2)


def periodic_take(field, dim, first, count):
    size = field.shape[dim]
    index = [(first + k) % size for k in range(count)]
    parts = [lax.slice_in_dim(field, i, i + 1, axis=dim) for i in index]
    return jnp.concatenate(parts, axis=dim)


def coarse_solve(rhs_two, tiles):
    extended = rhs_two
    starts = []
    tiles_by_step = {}
    extended, start, tiles_by_step = extend_axis(extended, "gx", 0, COARSE_HALO, tiles)
    starts.append(start)
    extended, joint_starts = extend_joint(extended, ("gy", "gz"), (1, 2), COARSE_HALO)
    starts.extend(joint_starts)
    width = extended.shape[3] * extended.shape[4]
    chunks = 1
    while extended.size * 4 // chunks > CHUNK_BYTES and width % (2 * chunks * 128) == 0:
        chunks *= 2
    if chunks == 1:
        return coarse_levels(extended, starts, rhs_two.shape), tiles_by_step
    part = width // chunks

    groups = extended.shape[3] // chunks

    def one_chunk(k):
        piece = lax.dynamic_slice_in_dim(extended, k * groups, groups, axis=3)
        return coarse_levels(piece, starts, rhs_two.shape)

    outs = lax.map(one_chunk, jnp.arange(chunks))
    outs = jnp.moveaxis(outs, 0, 3)
    return outs.reshape(outs.shape[:3] + (extended.shape[3], extended.shape[4])), tiles_by_step


def coarse_levels(extended, starts, block_shape):
    level_two = LEVELS - 2
    center, coupling = level_coeffs(level_two)
    correct_two = omega * extended / center
    remain = extended - stencil(correct_two, wrap_faces(correct_two), level_two)
    current = restrict(remain)
    top_level = LEVELS - 1
    center_top, coupling_top = level_coeffs(top_level)
    correct = omega * current / center_top
    for sweep_id in range(COARSE - 1):
        correct = correct + omega * (current - stencil(correct, wrap_faces(correct), top_level)) / center_top
    updated = correct_two + prolong(correct)
    post = updated + omega * (extended - stencil(updated, wrap_faces(updated), level_two)) / center
    for dim, start in enumerate(starts):
        post = periodic_take(post, dim, start - 1, block_shape[dim] + 2)
    return post


def prolong_face(face, dim):
    for other in range(3):
        if other != dim:
            face = jnp.repeat(face, 2, other)
    return face


def coarse_faces(halo_block, dim):
    inner = halo_block
    for other in range(3):
        if other != dim:
            inner = lax.slice_in_dim(inner, 1, inner.shape[other] - 1, axis=other)
    size = inner.shape[dim]
    lo = lax.slice_in_dim(inner, 0, 1, axis=dim)
    hi = lax.slice_in_dim(inner, size - 1, size, axis=dim)
    return lo, hi


def post_smooth(level_id, corr, corr_faces, rhs, coarse_inner, coarse_face_list):
    center, coupling = level_coeffs(level_id)
    updated = corr + prolong(coarse_inner)
    faces = []
    for dim in range(3):
        lo = corr_faces[dim][0] + prolong_face(coarse_face_list[dim][0], dim)
        hi = corr_faces[dim][1] + prolong_face(coarse_face_list[dim][1], dim)
        faces.append((lo, hi))
    return updated + omega * (rhs - stencil(updated, faces, level_id)) / center


def dim_mask(box_part, offset, extent):
    cells = offset + jnp.arange(extent, dtype=jnp.int32)[:, None]
    return ((box_part[0][None, :] <= cells) & (cells < box_part[1][None, :])).astype(jnp.float32)


def gram_matrix(tiles_by_step, inv_tiles, tile_pairs, orb_count):
    count = lax.axis_size("gx")
    local = inv_tiles.shape[0]
    tile_edge = inv_tiles.shape[1]
    me = lax.axis_index("gx")
    total = jnp.zeros((orb_count, orb_count), jnp.float32)
    for step in range(count):
        piece = tiles_by_step.get(step)
        if piece is None:
            piece = inv_tiles if step == 0 else shifted(inv_tiles, "gx", step)
        owner = (me + step) % count
        for slot in range(local):
            tile_id = owner * local + slot
            row = tile_pairs[tile_id, 0] * tile_edge
            col = tile_pairs[tile_id, 1] * tile_edge
            total = lax.dynamic_update_slice(total, piece[slot], (row, col))
    return total


def vcycle(residuals, inv_tiles):
    rhs_zero = residuals.astype(jnp.float32)
    center, coupling = level_coeffs(0)
    corr_zero = omega * rhs_zero / center
    faces_zero = all_faces(corr_zero)
    rhs_one = restrict(rhs_zero - stencil(corr_zero, faces_zero, 0))
    center, coupling = level_coeffs(1)
    corr_one = omega * rhs_one / center
    faces_one = all_faces(corr_one)
    rhs_two = restrict(rhs_one - stencil(corr_one, faces_one, 1))
    post_two, tiles_by_step = coarse_solve(rhs_two, inv_tiles)
    inner_two = post_two[1:-1, 1:-1, 1:-1]
    post_one = post_smooth(
        1, corr_one, faces_one, rhs_one, inner_two, [coarse_faces(post_two, dim) for dim in range(3)]
    )
    return post_smooth(0, corr_zero, faces_zero, rhs_zero, post_one, all_faces(post_one)), tiles_by_step


def body(residuals, patch_box, tile_pairs, inv_tiles):
    size_a, size_b, size_c, orb_count = residuals.shape
    lanes = LANES if orb_count % LANES == 0 else orb_count
    grouped = residuals.reshape(size_a, size_b, size_c, orb_count // lanes, lanes)
    correct, tiles_by_step = vcycle(grouped, inv_tiles)
    correct = correct.reshape(size_a, size_b, size_c, orb_count)
    gram = gram_matrix(tiles_by_step, inv_tiles, tile_pairs, orb_count)
    mask_first = dim_mask(patch_box[0], lax.axis_index("gx") * size_a, size_a)
    mask_second = dim_mask(patch_box[1], lax.axis_index("gy") * size_b, size_b)
    mask_third = dim_mask(patch_box[2], lax.axis_index("gz") * size_c, size_c)
    precond = correct * (
        mask_first[:, None, None, :] * mask_second[None, :, None, :] * mask_third[None, None, :, :]
    )
    cell_count = size_a * size_b * size_c
    rows = precond.reshape(cell_count, orb_count)
    mixed = jnp.dot(rows, gram, precision=lax.Precision.HIGH, preferred_element_type=jnp.float32)
    return mixed.reshape(size_a, size_b, size_c, orb_count).astype(jnp.bfloat16)


def solution(mesh):
    return jax.shard_map(
        body,
        mesh=mesh,
        in_specs=(P("gx", "gy", "gz", None), P(), P(), P("gx", None, None)),
        out_specs=P("gx", "gy", "gz", None),
        check_vma=False,
    )
```

```python
import jax
import jax.numpy as jnp
from jax import lax
from jax.sharding import PartitionSpec as P

LEVELS = 4
COARSE = 4


omega = 0.8
shift_sigma = 0.01

GRID_AXES = (("gx", 0), ("gy", 1), ("gz", 2))
COARSE_HALO = 10
CHUNK_BYTES = 1 << 21
LANES = 128


def shifted(block, axis, offset):
    count = lax.axis_size(axis)
    step = offset % count
    if step == 0:
        return block
    return lax.ppermute(block, axis, [(j, (j - step) % count) for j in range(count)])


def axis_faces(block, axis, dim):
    count = lax.axis_size(axis)
    first = lax.slice_in_dim(block, 0, 1, axis=dim)
    last = lax.slice_in_dim(block, block.shape[dim] - 1, None, axis=dim)
    if count == 1:
        return last, first
    if count == 2:
        both = lax.ppermute(jnp.concatenate([first, last], axis=dim), axis, [(0, 1), (1, 0)])
        hi = lax.slice_in_dim(both, 0, 1, axis=dim)
        lo = lax.slice_in_dim(both, 1, 2, axis=dim)
        return lo, hi
    lo = shifted(last, axis, -1)
    hi = shifted(first, axis, 1)
    return lo, hi


def all_faces(block):
    return [axis_faces(block, axis, dim) for axis, dim in GRID_AXES]


def extend_axis(block, axis, dim, halo, extra=None):
    count = lax.axis_size(axis)
    size = block.shape[dim]
    reach = -(-halo // size)
    if 2 * reach + 1 >= count:
        offsets = list(range(count))
        start = 0
    else:
        offsets = list(range(-reach, reach + 1))
        start = reach * size
    cache = {}
    extras = {}
    pieces = []
    for offset in offsets:
        step = offset % count
        if step not in cache:
            if extra is None or step == 0:
                cache[step] = shifted(block, axis, step)
                extras[step] = extra
            else:
                both = jnp.concatenate([block.reshape(-1), extra.reshape(-1)])
                both = shifted(both, axis, step)
                cache[step] = both[: block.size].reshape(block.shape)
                extras[step] = both[block.size :].reshape(extra.shape)
        pieces.append(cache[step])
    return jnp.concatenate(pieces, axis=dim), start, extras


def axis_offsets(count, size, halo):
    reach = -(-halo // size)
    if 2 * reach + 1 >= count:
        return list(range(count)), 0
    return list(range(-reach, reach + 1)), reach * size


def extend_joint(block, axes, dims, halo):
    counts = [lax.axis_size(axis) for axis in axes]
    plans = [axis_offsets(count, block.shape[dim], halo) for count, dim in zip(counts, dims)]
    cache = {}

    def fetch(offset):
        steps = tuple(o % c for o, c in zip(offset, counts))
        if steps not in cache:
            if not any(steps):
                cache[steps] = block
            else:
                pairs = []
                for target in range(_prod(counts)):
                    coords = _unravel(target, counts)
                    source = _ravel([(c + s) % n for c, s, n in zip(coords, steps, counts)], counts)
                    pairs.append((source, target))
                cache[steps] = lax.ppermute(block, tuple(axes), pairs)
        return cache[steps]

    def assemble(level, prefix):
        offsets, start = plans[level]
        if level == len(axes) - 1:
            pieces = [fetch(prefix + (o,)) for o in offsets]
        else:
            pieces = [assemble(level + 1, prefix + (o,)) for o in offsets]
        return jnp.concatenate(pieces, axis=dims[level])

    return assemble(0, ()), [start for offsets, start in plans]


def _prod(values):
    total = 1
    for v in values:
        total *= v
    return total


def _unravel(index, counts):
    coords = []
    for n in reversed(counts):
        coords.append(index % n)
        index //= n
    return list(reversed(coords))


def _ravel(coords, counts):
    index = 0
    for c, n in zip(coords, counts):
        index = index * n + c
    return index


def level_coeffs(level_id):
    coupling = 0.5 / 4.0**level_id
    return (6.0 * coupling + shift_sigma, coupling)


def pad_with(block, faces):
    padded = block
    for dim, (lo, hi) in enumerate(faces):
        widths = [(0, 0)] * block.ndim
        for other in range(dim):
            widths[other] = (1, 1)
        lo = jnp.pad(lo, widths)
        hi = jnp.pad(hi, widths)
        padded = jnp.concatenate([lo, padded, hi], axis=dim)
    return padded


def stencil(block, faces, level_id):
    return padded_stencil(pad_with(block, faces), level_id)


def padded_stencil(padded, level_id):
    center, coupling = level_coeffs(level_id)
    middle = padded[1:-1, 1:-1, 1:-1]
    beside = padded[2:, 1:-1, 1:-1] + padded[:-2, 1:-1, 1:-1]
    beside = beside + padded[1:-1, 2:, 1:-1] + padded[1:-1, :-2, 1:-1]
    beside = beside + padded[1:-1, 1:-1, 2:] + padded[1:-1, 1:-1, :-2]
    return center * middle - coupling * beside


def wrap_faces(block):
    faces = []
    for dim in range(3):
        size = block.shape[dim]
        faces.append(
            (lax.slice_in_dim(block, size - 1, size, axis=dim), lax.slice_in_dim(block, 0, 1, axis=dim))
        )
    return faces


def restrict(field):
    size_a, size_b, size_c = field.shape[:3]
    rest = field.shape[3:]
    return field.reshape((size_a // 2, 2, size_b // 2, 2, size_c // 2, 2) + rest).mean(axis=(1, 3, 5))


def prolong(field):
    return jnp.repeat(jnp.repeat(jnp.repeat(field, 2, 0), 2, 1), 2, 2)


def periodic_take(field, dim, first, count):
    size = field.shape[dim]
    index = [(first + k) % size for k in range(count)]
    parts = [lax.slice_in_dim(field, i, i + 1, axis=dim) for i in index]
    return jnp.concatenate(parts, axis=dim)


def coarse_solve(rhs_two, tiles):
    extended = rhs_two
    starts = []
    tiles_by_step = {}
    extended, start, tiles_by_step = extend_axis(extended, "gx", 0, COARSE_HALO, tiles)
    starts.append(start)
    extended, joint_starts = extend_joint(extended, ("gy", "gz"), (1, 2), COARSE_HALO)
    starts.extend(joint_starts)
    width = extended.shape[3] * extended.shape[4]
    chunks = 1
    while extended.size * 4 // chunks > CHUNK_BYTES and width % (2 * chunks * 128) == 0:
        chunks *= 2
    if chunks == 1:
        return coarse_levels(extended, starts, rhs_two.shape), tiles_by_step
    part = width // chunks

    groups = extended.shape[3] // chunks

    def one_chunk(k):
        piece = lax.dynamic_slice_in_dim(extended, k * groups, groups, axis=3)
        return coarse_levels(piece, starts, rhs_two.shape)

    outs = lax.map(one_chunk, jnp.arange(chunks))
    outs = jnp.moveaxis(outs, 0, 3)
    return outs.reshape(outs.shape[:3] + (extended.shape[3], extended.shape[4])), tiles_by_step


def coarse_levels(extended, starts, block_shape):
    level_two = LEVELS - 2
    center, coupling = level_coeffs(level_two)
    correct_two = omega * extended / center
    remain = extended - stencil(correct_two, wrap_faces(correct_two), level_two)
    current = restrict(remain)
    top_level = LEVELS - 1
    center_top, coupling_top = level_coeffs(top_level)
    correct = omega * current / center_top
    for sweep_id in range(COARSE - 1):
        correct = correct + omega * (current - stencil(correct, wrap_faces(correct), top_level)) / center_top
    updated = correct_two + prolong(correct)
    post = updated + omega * (extended - stencil(updated, wrap_faces(updated), level_two)) / center
    for dim, start in enumerate(starts):
        post = periodic_take(post, dim, start - 1, block_shape[dim] + 2)
    return post


def prolong_face(face, dim):
    for other in range(3):
        if other != dim:
            face = jnp.repeat(face, 2, other)
    return face


def coarse_faces(halo_block, dim):
    inner = halo_block
    for other in range(3):
        if other != dim:
            inner = lax.slice_in_dim(inner, 1, inner.shape[other] - 1, axis=other)
    size = inner.shape[dim]
    lo = lax.slice_in_dim(inner, 0, 1, axis=dim)
    hi = lax.slice_in_dim(inner, size - 1, size, axis=dim)
    return lo, hi


def post_smooth(level_id, corr, corr_faces, rhs, coarse_inner, coarse_face_list):
    center, coupling = level_coeffs(level_id)
    updated = corr + prolong(coarse_inner)
    faces = []
    for dim in range(3):
        lo = corr_faces[dim][0] + prolong_face(coarse_face_list[dim][0], dim)
        hi = corr_faces[dim][1] + prolong_face(coarse_face_list[dim][1], dim)
        faces.append((lo, hi))
    return updated + omega * (rhs - stencil(updated, faces, level_id)) / center


def post_smooth_padded(level_id, corr_padded, rhs, coarse_inner, coarse_face_list):
    center, coupling = level_coeffs(level_id)
    faces = [(prolong_face(lo, dim), prolong_face(hi, dim)) for dim, (lo, hi) in enumerate(coarse_face_list)]
    updated_padded = corr_padded + pad_with(prolong(coarse_inner), faces)
    updated = updated_padded[1:-1, 1:-1, 1:-1]
    return updated + omega * (rhs - padded_stencil(updated_padded, level_id)) / center


def dim_mask(box_part, offset, extent):
    cells = offset + jnp.arange(extent, dtype=jnp.int32)[:, None]
    return ((box_part[0][None, :] <= cells) & (cells < box_part[1][None, :])).astype(jnp.float32)


def gram_matrix(tiles_by_step, inv_tiles, tile_pairs, orb_count):
    count = lax.axis_size("gx")
    local = inv_tiles.shape[0]
    tile_edge = inv_tiles.shape[1]
    me = lax.axis_index("gx")
    total = jnp.zeros((orb_count, orb_count), jnp.float32)
    for step in range(count):
        piece = tiles_by_step.get(step)
        if piece is None:
            piece = inv_tiles if step == 0 else shifted(inv_tiles, "gx", step)
        owner = (me + step) % count
        for slot in range(local):
            tile_id = owner * local + slot
            row = tile_pairs[tile_id, 0] * tile_edge
            col = tile_pairs[tile_id, 1] * tile_edge
            total = lax.dynamic_update_slice(total, piece[slot], (row, col))
    return total


def vcycle(residuals, inv_tiles):
    rhs_zero = residuals.astype(jnp.float32)
    center, coupling = level_coeffs(0)
    corr_zero = omega * rhs_zero / center
    faces_zero = all_faces(corr_zero)
    rhs_one = restrict(rhs_zero - stencil(corr_zero, faces_zero, 0))
    center, coupling = level_coeffs(1)
    corr_one = omega * rhs_one / center
    padded_one = pad_with(corr_one, all_faces(corr_one))
    rhs_two = restrict(rhs_one - padded_stencil(padded_one, 1))
    post_two, tiles_by_step = coarse_solve(rhs_two, inv_tiles)
    inner_two = post_two[1:-1, 1:-1, 1:-1]
    post_one = post_smooth_padded(
        1, padded_one, rhs_one, inner_two, [coarse_faces(post_two, dim) for dim in range(3)]
    )
    return post_smooth(0, corr_zero, faces_zero, rhs_zero, post_one, all_faces(post_one)), tiles_by_step


def body(residuals, patch_box, tile_pairs, inv_tiles):
    size_a, size_b, size_c, orb_count = residuals.shape
    lanes = LANES if orb_count % LANES == 0 else orb_count
    grouped = residuals.reshape(size_a, size_b, size_c, orb_count // lanes, lanes)
    correct, tiles_by_step = vcycle(grouped, inv_tiles)
    correct = correct.reshape(size_a, size_b, size_c, orb_count)
    gram = gram_matrix(tiles_by_step, inv_tiles, tile_pairs, orb_count)
    mask_first = dim_mask(patch_box[0], lax.axis_index("gx") * size_a, size_a)
    mask_second = dim_mask(patch_box[1], lax.axis_index("gy") * size_b, size_b)
    mask_third = dim_mask(patch_box[2], lax.axis_index("gz") * size_c, size_c)
    precond = correct * (
        mask_first[:, None, None, :] * mask_second[None, :, None, :] * mask_third[None, None, :, :]
    )
    cell_count = size_a * size_b * size_c
    rows = precond.reshape(cell_count, orb_count)
    mixed = jnp.dot(rows, gram, precision=lax.Precision.HIGH, preferred_element_type=jnp.float32)
    return mixed.reshape(size_a, size_b, size_c, orb_count).astype(jnp.bfloat16)


def solution(mesh):
    return jax.shard_map(
        body,
        mesh=mesh,
        in_specs=(P("gx", "gy", "gz", None), P(), P(), P("gx", None, None)),
        out_specs=P("gx", "gy", "gz", None),
        check_vma=False,
    )
```

```python
import jax
import jax.numpy as jnp
from jax import lax
from jax.sharding import PartitionSpec as P

LEVELS = 4
COARSE = 4


omega = 0.8
shift_sigma = 0.01

GRID_AXES = (("gx", 0), ("gy", 1), ("gz", 2))
COARSE_HALO = 10
CHUNK_BYTES = 1 << 21
LANES = 128


def shifted(block, axis, offset):
    count = lax.axis_size(axis)
    step = offset % count
    if step == 0:
        return block
    return lax.ppermute(block, axis, [(j, (j - step) % count) for j in range(count)])


def axis_faces(block, axis, dim, prepare=None):
    count = lax.axis_size(axis)
    first = lax.slice_in_dim(block, 0, 1, axis=dim)
    last = lax.slice_in_dim(block, block.shape[dim] - 1, None, axis=dim)
    if prepare is not None:
        first = prepare(first)
        last = prepare(last)
    if count == 1:
        return last, first
    if count == 2:
        both = lax.ppermute(jnp.concatenate([first, last], axis=dim), axis, [(0, 1), (1, 0)])
        hi = lax.slice_in_dim(both, 0, 1, axis=dim)
        lo = lax.slice_in_dim(both, 1, 2, axis=dim)
        return lo, hi
    lo = shifted(last, axis, -1)
    hi = shifted(first, axis, 1)
    return lo, hi


def all_faces(block, prepare=None):
    return [axis_faces(block, axis, dim, prepare) for axis, dim in GRID_AXES]


def extend_axis(block, axis, dim, halo, extra=None):
    count = lax.axis_size(axis)
    size = block.shape[dim]
    reach = -(-halo // size)
    if 2 * reach + 1 >= count:
        offsets = list(range(count))
        start = 0
    else:
        offsets = list(range(-reach, reach + 1))
        start = reach * size
    cache = {}
    extras = {}
    pieces = []
    for offset in offsets:
        step = offset % count
        if step not in cache:
            if extra is None or step == 0:
                cache[step] = shifted(block, axis, step)
                extras[step] = extra
            else:
                both = jnp.concatenate([block.reshape(-1), extra.reshape(-1)])
                both = shifted(both, axis, step)
                cache[step] = both[: block.size].reshape(block.shape)
                extras[step] = both[block.size :].reshape(extra.shape)
        pieces.append(cache[step])
    return jnp.concatenate(pieces, axis=dim), start, extras


def axis_offsets(count, size, halo):
    reach = -(-halo // size)
    if 2 * reach + 1 >= count:
        return list(range(count)), 0
    return list(range(-reach, reach + 1)), reach * size


def extend_joint(block, axes, dims, halo):
    counts = [lax.axis_size(axis) for axis in axes]
    plans = [axis_offsets(count, block.shape[dim], halo) for count, dim in zip(counts, dims)]
    cache = {}

    def fetch(offset):
        steps = tuple(o % c for o, c in zip(offset, counts))
        if steps not in cache:
            if not any(steps):
                cache[steps] = block
            else:
                pairs = []
                for target in range(_prod(counts)):
                    coords = _unravel(target, counts)
                    source = _ravel([(c + s) % n for c, s, n in zip(coords, steps, counts)], counts)
                    pairs.append((source, target))
                cache[steps] = lax.ppermute(block, tuple(axes), pairs)
        return cache[steps]

    def assemble(level, prefix):
        offsets, start = plans[level]
        if level == len(axes) - 1:
            pieces = [fetch(prefix + (o,)) for o in offsets]
        else:
            pieces = [assemble(level + 1, prefix + (o,)) for o in offsets]
        return jnp.concatenate(pieces, axis=dims[level])

    return assemble(0, ()), [start for offsets, start in plans]


def _prod(values):
    total = 1
    for v in values:
        total *= v
    return total


def _unravel(index, counts):
    coords = []
    for n in reversed(counts):
        coords.append(index % n)
        index //= n
    return list(reversed(coords))


def _ravel(coords, counts):
    index = 0
    for c, n in zip(coords, counts):
        index = index * n + c
    return index


def level_coeffs(level_id):
    coupling = 0.5 / 4.0**level_id
    return (6.0 * coupling + shift_sigma, coupling)


def pad_with(block, faces):
    padded = block
    for dim, (lo, hi) in enumerate(faces):
        widths = [(0, 0)] * block.ndim
        for other in range(dim):
            widths[other] = (1, 1)
        lo = jnp.pad(lo, widths)
        hi = jnp.pad(hi, widths)
        padded = jnp.concatenate([lo, padded, hi], axis=dim)
    return padded


def stencil(block, faces, level_id):
    return padded_stencil(pad_with(block, faces), level_id)


def padded_stencil(padded, level_id):
    center, coupling = level_coeffs(level_id)
    middle = padded[1:-1, 1:-1, 1:-1]
    beside = padded[2:, 1:-1, 1:-1] + padded[:-2, 1:-1, 1:-1]
    beside = beside + padded[1:-1, 2:, 1:-1] + padded[1:-1, :-2, 1:-1]
    beside = beside + padded[1:-1, 1:-1, 2:] + padded[1:-1, 1:-1, :-2]
    return center * middle - coupling * beside


def wrap_faces(block):
    faces = []
    for dim in range(3):
        size = block.shape[dim]
        faces.append(
            (lax.slice_in_dim(block, size - 1, size, axis=dim), lax.slice_in_dim(block, 0, 1, axis=dim))
        )
    return faces


def restrict(field):
    size_a, size_b, size_c = field.shape[:3]
    rest = field.shape[3:]
    return field.reshape((size_a // 2, 2, size_b // 2, 2, size_c // 2, 2) + rest).mean(axis=(1, 3, 5))


def prolong(field):
    return jnp.repeat(jnp.repeat(jnp.repeat(field, 2, 0), 2, 1), 2, 2)


def periodic_take(field, dim, first, count):
    size = field.shape[dim]
    index = [(first + k) % size for k in range(count)]
    parts = [lax.slice_in_dim(field, i, i + 1, axis=dim) for i in index]
    return jnp.concatenate(parts, axis=dim)


def coarse_solve(rhs_two, tiles):
    extended = rhs_two
    starts = []
    tiles_by_step = {}
    extended, start, tiles_by_step = extend_axis(extended, "gx", 0, COARSE_HALO, tiles)
    starts.append(start)
    extended, joint_starts = extend_joint(extended, ("gy", "gz"), (1, 2), COARSE_HALO)
    starts.extend(joint_starts)
    width = extended.shape[3] * extended.shape[4]
    chunks = 1
    while extended.size * 4 // chunks > CHUNK_BYTES and width % (2 * chunks * 128) == 0:
        chunks *= 2
    if chunks == 1:
        return coarse_levels(extended, starts, rhs_two.shape), tiles_by_step
    part = width // chunks

    groups = extended.shape[3] // chunks

    def one_chunk(k):
        piece = lax.dynamic_slice_in_dim(extended, k * groups, groups, axis=3)
        return coarse_levels(piece, starts, rhs_two.shape)

    outs = lax.map(one_chunk, jnp.arange(chunks))
    outs = jnp.moveaxis(outs, 0, 3)
    return outs.reshape(outs.shape[:3] + (extended.shape[3], extended.shape[4])), tiles_by_step


def coarse_levels(extended, starts, block_shape):
    level_two = LEVELS - 2
    center, coupling = level_coeffs(level_two)
    correct_two = omega * extended / center
    remain = extended - stencil(correct_two, wrap_faces(correct_two), level_two)
    current = restrict(remain)
    top_level = LEVELS - 1
    center_top, coupling_top = level_coeffs(top_level)
    correct = omega * current / center_top
    for sweep_id in range(COARSE - 1):
        correct = correct + omega * (current - stencil(correct, wrap_faces(correct), top_level)) / center_top
    updated = correct_two + prolong(correct)
    post = updated + omega * (extended - stencil(updated, wrap_faces(updated), level_two)) / center
    for dim, start in enumerate(starts):
        post = periodic_take(post, dim, start - 1, block_shape[dim] + 2)
    return post


def prolong_face(face, dim):
    for other in range(3):
        if other != dim:
            face = jnp.repeat(face, 2, other)
    return face


def coarse_faces(halo_block, dim):
    inner = halo_block
    for other in range(3):
        if other != dim:
            inner = lax.slice_in_dim(inner, 1, inner.shape[other] - 1, axis=other)
    size = inner.shape[dim]
    lo = lax.slice_in_dim(inner, 0, 1, axis=dim)
    hi = lax.slice_in_dim(inner, size - 1, size, axis=dim)
    return lo, hi


def post_smooth(level_id, corr, corr_faces, rhs, coarse_inner, coarse_face_list):
    center, coupling = level_coeffs(level_id)
    updated = corr + prolong(coarse_inner)
    faces = []
    for dim in range(3):
        lo = corr_faces[dim][0] + prolong_face(coarse_face_list[dim][0], dim)
        hi = corr_faces[dim][1] + prolong_face(coarse_face_list[dim][1], dim)
        faces.append((lo, hi))
    return updated + omega * (rhs - stencil(updated, faces, level_id)) / center


def post_smooth_padded(level_id, corr_padded, rhs, coarse_inner, coarse_face_list):
    center, coupling = level_coeffs(level_id)
    faces = [(prolong_face(lo, dim), prolong_face(hi, dim)) for dim, (lo, hi) in enumerate(coarse_face_list)]
    updated_padded = corr_padded + pad_with(prolong(coarse_inner), faces)
    updated = updated_padded[1:-1, 1:-1, 1:-1]
    return updated + omega * (rhs - padded_stencil(updated_padded, level_id)) / center


def dim_mask(box_part, offset, extent):
    cells = offset + jnp.arange(extent, dtype=jnp.int32)[:, None]
    return ((box_part[0][None, :] <= cells) & (cells < box_part[1][None, :])).astype(jnp.float32)


def gram_matrix(tiles_by_step, inv_tiles, tile_pairs, orb_count):
    count = lax.axis_size("gx")
    local = inv_tiles.shape[0]
    tile_edge = inv_tiles.shape[1]
    me = lax.axis_index("gx")
    total = jnp.zeros((orb_count, orb_count), jnp.float32)
    for step in range(count):
        piece = tiles_by_step.get(step)
        if piece is None:
            piece = inv_tiles if step == 0 else shifted(inv_tiles, "gx", step)
        owner = (me + step) % count
        for slot in range(local):
            tile_id = owner * local + slot
            row = tile_pairs[tile_id, 0] * tile_edge
            col = tile_pairs[tile_id, 1] * tile_edge
            total = lax.dynamic_update_slice(total, piece[slot], (row, col))
    return total


def vcycle(residuals, inv_tiles):
    center, coupling = level_coeffs(0)
    faces_zero = all_faces(residuals, lambda part: omega * part.astype(jnp.float32) / center)
    rhs_zero = residuals.astype(jnp.float32)
    corr_zero = omega * rhs_zero / center
    rhs_one = restrict(rhs_zero - stencil(corr_zero, faces_zero, 0))
    center, coupling = level_coeffs(1)
    corr_one = omega * rhs_one / center
    padded_one = pad_with(corr_one, all_faces(corr_one))
    rhs_two = restrict(rhs_one - padded_stencil(padded_one, 1))
    post_two, tiles_by_step = coarse_solve(rhs_two, inv_tiles)
    inner_two = post_two[1:-1, 1:-1, 1:-1]
    post_one = post_smooth_padded(
        1, padded_one, rhs_one, inner_two, [coarse_faces(post_two, dim) for dim in range(3)]
    )
    return post_smooth(0, corr_zero, faces_zero, rhs_zero, post_one, all_faces(post_one)), tiles_by_step


def body(residuals, patch_box, tile_pairs, inv_tiles):
    size_a, size_b, size_c, orb_count = residuals.shape
    lanes = LANES if orb_count % LANES == 0 else orb_count
    grouped = residuals.reshape(size_a, size_b, size_c, orb_count // lanes, lanes)
    correct, tiles_by_step = vcycle(grouped, inv_tiles)
    correct = correct.reshape(size_a, size_b, size_c, orb_count)
    gram = gram_matrix(tiles_by_step, inv_tiles, tile_pairs, orb_count)
    mask_first = dim_mask(patch_box[0], lax.axis_index("gx") * size_a, size_a)
    mask_second = dim_mask(patch_box[1], lax.axis_index("gy") * size_b, size_b)
    mask_third = dim_mask(patch_box[2], lax.axis_index("gz") * size_c, size_c)
    precond = correct * (
        mask_first[:, None, None, :] * mask_second[None, :, None, :] * mask_third[None, None, :, :]
    )
    cell_count = size_a * size_b * size_c
    rows = lax.optimization_barrier(precond.reshape(cell_count, orb_count))
    mixed = jnp.dot(rows, gram, precision=lax.Precision.HIGH, preferred_element_type=jnp.float32)
    return mixed.reshape(size_a, size_b, size_c, orb_count).astype(jnp.bfloat16)


def solution(mesh):
    return jax.shard_map(
        body,
        mesh=mesh,
        in_specs=(P("gx", "gy", "gz", None), P(), P(), P("gx", None, None)),
        out_specs=P("gx", "gy", "gz", None),
        check_vma=False,
    )
```

```python
import jax
import jax.numpy as jnp
import numpy as np
from jax import lax
from jax.sharding import PartitionSpec as P

LEVELS = 4
COARSE = 4


omega = 0.8
shift_sigma = 0.01

GRID_AXES = (("gx", 0), ("gy", 1), ("gz", 2))
COARSE_HALO = 10
LANES = 128


def shifted(block, axis, offset):
    count = lax.axis_size(axis)
    step = offset % count
    if step == 0:
        return block
    return lax.ppermute(block, axis, [(j, (j - step) % count) for j in range(count)])


def axis_faces(block, axis, dim, prepare=None):
    count = lax.axis_size(axis)
    first = lax.slice_in_dim(block, 0, 1, axis=dim)
    last = lax.slice_in_dim(block, block.shape[dim] - 1, None, axis=dim)
    if prepare is not None:
        first = prepare(first)
        last = prepare(last)
    if count == 1:
        return last, first
    if count == 2:
        both = lax.ppermute(jnp.concatenate([first, last], axis=dim), axis, [(0, 1), (1, 0)])
        hi = lax.slice_in_dim(both, 0, 1, axis=dim)
        lo = lax.slice_in_dim(both, 1, 2, axis=dim)
        return lo, hi
    lo = shifted(last, axis, -1)
    hi = shifted(first, axis, 1)
    return lo, hi


def all_faces(block, prepare=None):
    return [axis_faces(block, axis, dim, prepare) for axis, dim in GRID_AXES]


def extend_axis(block, axis, dim, halo, extra=None):
    count = lax.axis_size(axis)
    size = block.shape[dim]
    reach = -(-halo // size)
    if 2 * reach + 1 >= count:
        offsets = list(range(count))
        start = 0
    else:
        offsets = list(range(-reach, reach + 1))
        start = reach * size
    cache = {}
    extras = {}
    pieces = []
    for offset in offsets:
        step = offset % count
        if step not in cache:
            if extra is None or step == 0:
                cache[step] = shifted(block, axis, step)
                extras[step] = extra
            else:
                both = jnp.concatenate([block.reshape(-1), extra.reshape(-1)])
                both = shifted(both, axis, step)
                cache[step] = both[: block.size].reshape(block.shape)
                extras[step] = both[block.size :].reshape(extra.shape)
        pieces.append(cache[step])
    return jnp.concatenate(pieces, axis=dim), start, extras


def axis_offsets(count, size, halo):
    reach = -(-halo // size)
    if 2 * reach + 1 >= count:
        return list(range(count)), 0
    return list(range(-reach, reach + 1)), reach * size


def extend_joint(block, axes, dims, halo):
    counts = [lax.axis_size(axis) for axis in axes]
    plans = [axis_offsets(count, block.shape[dim], halo) for count, dim in zip(counts, dims)]
    cache = {}

    def fetch(offset):
        steps = tuple(o % c for o, c in zip(offset, counts))
        if steps not in cache:
            if not any(steps):
                cache[steps] = block
            else:
                pairs = []
                for target in range(_prod(counts)):
                    coords = _unravel(target, counts)
                    source = _ravel([(c + s) % n for c, s, n in zip(coords, steps, counts)], counts)
                    pairs.append((source, target))
                cache[steps] = lax.ppermute(block, tuple(axes), pairs)
        return cache[steps]

    def assemble(level, prefix):
        offsets, start = plans[level]
        if level == len(axes) - 1:
            pieces = [fetch(prefix + (o,)) for o in offsets]
        else:
            pieces = [assemble(level + 1, prefix + (o,)) for o in offsets]
        return jnp.concatenate(pieces, axis=dims[level])

    return assemble(0, ()), [start for offsets, start in plans]


def _prod(values):
    total = 1
    for v in values:
        total *= v
    return total


def _unravel(index, counts):
    coords = []
    for n in reversed(counts):
        coords.append(index % n)
        index //= n
    return list(reversed(coords))


def _ravel(coords, counts):
    index = 0
    for c, n in zip(coords, counts):
        index = index * n + c
    return index


def level_coeffs(level_id):
    coupling = 0.5 / 4.0**level_id
    return (6.0 * coupling + shift_sigma, coupling)


def pad_with(block, faces):
    padded = block
    for dim, (lo, hi) in enumerate(faces):
        widths = [(0, 0)] * block.ndim
        for other in range(dim):
            widths[other] = (1, 1)
        lo = jnp.pad(lo, widths)
        hi = jnp.pad(hi, widths)
        padded = jnp.concatenate([lo, padded, hi], axis=dim)
    return padded


def stencil(block, faces, level_id):
    return padded_stencil(pad_with(block, faces), level_id)


def padded_stencil(padded, level_id):
    center, coupling = level_coeffs(level_id)
    middle = padded[1:-1, 1:-1, 1:-1]
    beside = padded[2:, 1:-1, 1:-1] + padded[:-2, 1:-1, 1:-1]
    beside = beside + padded[1:-1, 2:, 1:-1] + padded[1:-1, :-2, 1:-1]
    beside = beside + padded[1:-1, 1:-1, 2:] + padded[1:-1, 1:-1, :-2]
    return center * middle - coupling * beside


def restrict(field):
    size_a, size_b, size_c = field.shape[:3]
    rest = field.shape[3:]
    return field.reshape((size_a // 2, 2, size_b // 2, 2, size_c // 2, 2) + rest).mean(axis=(1, 3, 5))


def prolong(field):
    return jnp.repeat(jnp.repeat(jnp.repeat(field, 2, 0), 2, 1), 2, 2)


def coarse_solve(rhs_two, tiles):
    extended = rhs_two
    starts = []
    extended, start, tiles_by_step = extend_axis(extended, "gx", 0, COARSE_HALO, tiles)
    starts.append(start)
    extended, joint_starts = extend_joint(extended, ("gy", "gz"), (1, 2), COARSE_HALO)
    starts.extend(joint_starts)
    grid = extended.shape[:3]
    orbs = extended.shape[3:]
    operator = jnp.asarray(coarse_matrix(grid, tuple(starts), rhs_two.shape[:3]))
    flat = extended.reshape((-1,) + (int(np.prod(orbs)),))
    post = jnp.dot(operator, flat, precision=lax.Precision.HIGHEST, preferred_element_type=jnp.float32)
    return post.reshape(tuple(size + 2 for size in rhs_two.shape[:3]) + orbs), tiles_by_step


def coarse_matrix(grid, starts, block):
    cells = int(np.prod(grid))
    field = np.eye(cells).reshape(tuple(grid) + (cells,))

    def apply(v, level_id):
        center, coupling = level_coeffs(level_id)
        beside = 0.0
        for dim in range(3):
            beside = beside + np.roll(v, -1, dim) + np.roll(v, 1, dim)
        return center * v - coupling * beside

    def shrink(v):
        a, b, c = v.shape[:3]
        return v.reshape(a // 2, 2, b // 2, 2, c // 2, 2, -1).mean(axis=(1, 3, 5))

    def grow(v):
        return np.repeat(np.repeat(np.repeat(v, 2, 0), 2, 1), 2, 2)

    level_two = LEVELS - 2
    center, coupling = level_coeffs(level_two)
    correct_two = omega * field / center
    current = shrink(field - apply(correct_two, level_two))
    top_level = LEVELS - 1
    center_top, coupling_top = level_coeffs(top_level)
    correct = omega * current / center_top
    for sweep_id in range(COARSE - 1):
        correct = correct + omega * (current - apply(correct, top_level)) / center_top
    updated = correct_two + grow(correct)
    post = updated + omega * (field - apply(updated, level_two)) / center
    for dim, start in enumerate(starts):
        index = [(start - 1 + k) % grid[dim] for k in range(block[dim] + 2)]
        post = np.take(post, index, axis=dim)
    return post.reshape(-1, cells).astype(np.float32)


def prolong_face(face, dim):
    for other in range(3):
        if other != dim:
            face = jnp.repeat(face, 2, other)
    return face


def coarse_faces(halo_block, dim):
    inner = halo_block
    for other in range(3):
        if other != dim:
            inner = lax.slice_in_dim(inner, 1, inner.shape[other] - 1, axis=other)
    size = inner.shape[dim]
    lo = lax.slice_in_dim(inner, 0, 1, axis=dim)
    hi = lax.slice_in_dim(inner, size - 1, size, axis=dim)
    return lo, hi


def post_smooth(level_id, corr, corr_faces, rhs, coarse_inner, coarse_face_list):
    center, coupling = level_coeffs(level_id)
    updated = corr + prolong(coarse_inner)
    faces = []
    for dim in range(3):
        lo = corr_faces[dim][0] + prolong_face(coarse_face_list[dim][0], dim)
        hi = corr_faces[dim][1] + prolong_face(coarse_face_list[dim][1], dim)
        faces.append((lo, hi))
    return updated + omega * (rhs - stencil(updated, faces, level_id)) / center


def post_smooth_padded(level_id, corr_padded, rhs, coarse_inner, coarse_face_list):
    center, coupling = level_coeffs(level_id)
    faces = [(prolong_face(lo, dim), prolong_face(hi, dim)) for dim, (lo, hi) in enumerate(coarse_face_list)]
    updated_padded = corr_padded + pad_with(prolong(coarse_inner), faces)
    updated = updated_padded[1:-1, 1:-1, 1:-1]
    return updated + omega * (rhs - padded_stencil(updated_padded, level_id)) / center


def dim_mask(box_part, offset, extent):
    cells = offset + jnp.arange(extent, dtype=jnp.int32)[:, None]
    return ((box_part[0][None, :] <= cells) & (cells < box_part[1][None, :])).astype(jnp.float32)


def gram_matrix(tiles_by_step, inv_tiles, tile_pairs, orb_count):
    count = lax.axis_size("gx")
    local = inv_tiles.shape[0]
    tile_edge = inv_tiles.shape[1]
    me = lax.axis_index("gx")
    total = jnp.zeros((orb_count, orb_count), jnp.float32)
    for step in range(count):
        piece = tiles_by_step.get(step)
        if piece is None:
            piece = inv_tiles if step == 0 else shifted(inv_tiles, "gx", step)
        owner = (me + step) % count
        for slot in range(local):
            tile_id = owner * local + slot
            row = tile_pairs[tile_id, 0] * tile_edge
            col = tile_pairs[tile_id, 1] * tile_edge
            total = lax.dynamic_update_slice(total, piece[slot], (row, col))
    return total


def vcycle(residuals, inv_tiles):
    center, coupling = level_coeffs(0)
    faces_zero = all_faces(residuals, lambda part: omega * part.astype(jnp.float32) / center)
    rhs_zero = residuals.astype(jnp.float32)
    corr_zero = omega * rhs_zero / center
    rhs_one = restrict(rhs_zero - stencil(corr_zero, faces_zero, 0))
    center, coupling = level_coeffs(1)
    corr_one = omega * rhs_one / center
    padded_one = pad_with(corr_one, all_faces(corr_one))
    rhs_two = restrict(rhs_one - padded_stencil(padded_one, 1))
    post_two, tiles_by_step = coarse_solve(rhs_two, inv_tiles)
    inner_two = post_two[1:-1, 1:-1, 1:-1]
    post_one = post_smooth_padded(
        1, padded_one, rhs_one, inner_two, [coarse_faces(post_two, dim) for dim in range(3)]
    )
    return post_smooth(0, corr_zero, faces_zero, rhs_zero, post_one, all_faces(post_one)), tiles_by_step


def body(residuals, patch_box, tile_pairs, inv_tiles):
    size_a, size_b, size_c, orb_count = residuals.shape
    lanes = LANES if orb_count % LANES == 0 else orb_count
    grouped = residuals.reshape(size_a, size_b, size_c, orb_count // lanes, lanes)
    correct, tiles_by_step = vcycle(grouped, inv_tiles)
    correct = correct.reshape(size_a, size_b, size_c, orb_count)
    gram = gram_matrix(tiles_by_step, inv_tiles, tile_pairs, orb_count)
    mask_first = dim_mask(patch_box[0], lax.axis_index("gx") * size_a, size_a)
    mask_second = dim_mask(patch_box[1], lax.axis_index("gy") * size_b, size_b)
    mask_third = dim_mask(patch_box[2], lax.axis_index("gz") * size_c, size_c)
    precond = correct * (
        mask_first[:, None, None, :] * mask_second[None, :, None, :] * mask_third[None, None, :, :]
    )
    cell_count = size_a * size_b * size_c
    rows = lax.optimization_barrier(precond.reshape(cell_count, orb_count))
    mixed = jnp.dot(rows, gram, precision=lax.Precision.HIGH, preferred_element_type=jnp.float32)
    return mixed.reshape(size_a, size_b, size_c, orb_count).astype(jnp.bfloat16)


def solution(mesh):
    return jax.shard_map(
        body,
        mesh=mesh,
        in_specs=(P("gx", "gy", "gz", None), P(), P(), P("gx", None, None)),
        out_specs=P("gx", "gy", "gz", None),
        check_vma=False,
    )
```

```python
import jax
import jax.numpy as jnp
import numpy as np
from jax import lax
from jax.sharding import PartitionSpec as P

LEVELS = 4
COARSE = 4


omega = 0.8
shift_sigma = 0.01

GRID_AXES = (("gx", 0), ("gy", 1), ("gz", 2))
COARSE_HALO = 10
LANES = 128


def shifted(block, axis, offset):
    count = lax.axis_size(axis)
    step = offset % count
    if step == 0:
        return block
    return lax.ppermute(block, axis, [(j, (j - step) % count) for j in range(count)])


def axis_faces(block, axis, dim, prepare=None):
    count = lax.axis_size(axis)
    first = lax.slice_in_dim(block, 0, 1, axis=dim)
    last = lax.slice_in_dim(block, block.shape[dim] - 1, None, axis=dim)
    if prepare is not None:
        first = prepare(first)
        last = prepare(last)
    if count == 1:
        return last, first
    if count == 2:
        both = lax.ppermute(jnp.concatenate([first, last], axis=dim), axis, [(0, 1), (1, 0)])
        hi = lax.slice_in_dim(both, 0, 1, axis=dim)
        lo = lax.slice_in_dim(both, 1, 2, axis=dim)
        return lo, hi
    lo = shifted(last, axis, -1)
    hi = shifted(first, axis, 1)
    return lo, hi


def all_faces(block, prepare=None):
    return [axis_faces(block, axis, dim, prepare) for axis, dim in GRID_AXES]


def extend_axis(block, axis, dim, halo, extra=None):
    count = lax.axis_size(axis)
    size = block.shape[dim]
    reach = -(-halo // size)
    if 2 * reach + 1 >= count:
        offsets = list(range(count))
        start = 0
    else:
        offsets = list(range(-reach, reach + 1))
        start = reach * size
    cache = {}
    extras = {}
    pieces = []
    for offset in offsets:
        step = offset % count
        if step not in cache:
            if extra is None or step == 0:
                cache[step] = shifted(block, axis, step)
                extras[step] = extra
            else:
                both = jnp.concatenate([block.reshape(-1), extra.reshape(-1)])
                both = shifted(both, axis, step)
                cache[step] = both[: block.size].reshape(block.shape)
                extras[step] = both[block.size :].reshape(extra.shape)
        pieces.append(cache[step])
    return jnp.concatenate(pieces, axis=dim), start, extras


def axis_offsets(count, size, halo):
    reach = -(-halo // size)
    if 2 * reach + 1 >= count:
        return list(range(count)), 0
    return list(range(-reach, reach + 1)), reach * size


def extend_joint(block, axes, dims, halo):
    counts = [lax.axis_size(axis) for axis in axes]
    plans = [axis_offsets(count, block.shape[dim], halo) for count, dim in zip(counts, dims)]
    cache = {}

    def fetch(offset):
        steps = tuple(o % c for o, c in zip(offset, counts))
        if steps not in cache:
            if not any(steps):
                cache[steps] = block
            else:
                pairs = []
                for target in range(_prod(counts)):
                    coords = _unravel(target, counts)
                    source = _ravel([(c + s) % n for c, s, n in zip(coords, steps, counts)], counts)
                    pairs.append((source, target))
                cache[steps] = lax.ppermute(block, tuple(axes), pairs)
        return cache[steps]

    def assemble(level, prefix):
        offsets, start = plans[level]
        if level == len(axes) - 1:
            pieces = [fetch(prefix + (o,)) for o in offsets]
        else:
            pieces = [assemble(level + 1, prefix + (o,)) for o in offsets]
        return jnp.concatenate(pieces, axis=dims[level])

    return assemble(0, ()), [start for offsets, start in plans]


def _prod(values):
    total = 1
    for v in values:
        total *= v
    return total


def _unravel(index, counts):
    coords = []
    for n in reversed(counts):
        coords.append(index % n)
        index //= n
    return list(reversed(coords))


def _ravel(coords, counts):
    index = 0
    for c, n in zip(coords, counts):
        index = index * n + c
    return index


def level_coeffs(level_id):
    coupling = 0.5 / 4.0**level_id
    return (6.0 * coupling + shift_sigma, coupling)


def pad_with(block, faces):
    padded = block
    for dim, (lo, hi) in enumerate(faces):
        widths = [(0, 0)] * block.ndim
        for other in range(dim):
            widths[other] = (1, 1)
        lo = jnp.pad(lo, widths)
        hi = jnp.pad(hi, widths)
        padded = jnp.concatenate([lo, padded, hi], axis=dim)
    return padded


def stencil(block, faces, level_id):
    return padded_stencil(pad_with(block, faces), level_id)


def padded_stencil(padded, level_id):
    center, coupling = level_coeffs(level_id)
    middle = padded[1:-1, 1:-1, 1:-1]
    beside = padded[2:, 1:-1, 1:-1] + padded[:-2, 1:-1, 1:-1]
    beside = beside + padded[1:-1, 2:, 1:-1] + padded[1:-1, :-2, 1:-1]
    beside = beside + padded[1:-1, 1:-1, 2:] + padded[1:-1, 1:-1, :-2]
    return center * middle - coupling * beside


def restrict(field):
    size_a, size_b, size_c = field.shape[:3]
    rest = field.shape[3:]
    return field.reshape((size_a // 2, 2, size_b // 2, 2, size_c // 2, 2) + rest).mean(axis=(1, 3, 5))


def prolong(field):
    return jnp.repeat(jnp.repeat(jnp.repeat(field, 2, 0), 2, 1), 2, 2)


def coarse_solve(rhs_two, tiles):
    block = rhs_two.shape[:3]
    orbs = rhs_two.shape[3:]
    width = int(np.prod(orbs))
    rows = rhs_two.reshape(-1, width)
    tile_rows = tiles.reshape(-1, width)
    count_x = lax.axis_size("gx")
    offsets_x, start_x = axis_offsets(count_x, block[0], COARSE_HALO)
    cache = {}
    tiles_by_step = {0: tiles}
    for offset in offsets_x:
        step = offset % count_x
        if step in cache:
            continue
        if step == 0:
            cache[step] = rows
            continue
        both = shifted(jnp.concatenate([rows, tile_rows], axis=0), "gx", step)
        cache[step] = both[: rows.shape[0]]
        tiles_by_step[step] = both[rows.shape[0] :].reshape(tiles.shape)
    line = jnp.concatenate([cache[offset % count_x] for offset in offsets_x], axis=0)
    axes = ("gy", "gz")
    counts = [lax.axis_size(axis) for axis in axes]
    plans = [axis_offsets(count, block[dim], COARSE_HALO) for count, dim in zip(counts, (1, 2))]
    moved = {}
    pieces = []
    for offset_y in plans[0][0]:
        for offset_z in plans[1][0]:
            steps = (offset_y % counts[0], offset_z % counts[1])
            if steps not in moved:
                if steps == (0, 0):
                    moved[steps] = line
                else:
                    pairs = []
                    for target in range(counts[0] * counts[1]):
                        ty, tz = divmod(target, counts[1])
                        source = ((ty + steps[0]) % counts[0]) * counts[1] + (tz + steps[1]) % counts[1]
                        pairs.append((source, target))
                    moved[steps] = lax.ppermute(line, axes, pairs)
            pieces.append(moved[steps])
    gathered = jnp.concatenate(pieces, axis=0)
    operator = coarse_matrix(
        block, (offsets_x, plans[0][0], plans[1][0]), (start_x, plans[0][1], plans[1][1])
    )
    post = jnp.dot(
        jnp.asarray(operator), gathered, precision=lax.Precision.HIGHEST, preferred_element_type=jnp.float32
    )
    return post.reshape(tuple(2 * size + 2 for size in block) + orbs), tiles_by_step


def coarse_matrix(block, offsets, starts):
    grid = tuple(len(offs) * size for offs, size in zip(offsets, block))
    cells = int(np.prod(grid))
    field = np.eye(cells).reshape(grid + (cells,))

    def apply(v, level_id):
        center, coupling = level_coeffs(level_id)
        beside = 0.0
        for dim in range(3):
            beside = beside + np.roll(v, -1, dim) + np.roll(v, 1, dim)
        return center * v - coupling * beside

    def shrink(v):
        a, b, c = v.shape[:3]
        return v.reshape(a // 2, 2, b // 2, 2, c // 2, 2, -1).mean(axis=(1, 3, 5))

    def grow(v):
        return np.repeat(np.repeat(np.repeat(v, 2, 0), 2, 1), 2, 2)

    level_two = LEVELS - 2
    center, coupling = level_coeffs(level_two)
    correct_two = omega * field / center
    current = shrink(field - apply(correct_two, level_two))
    top_level = LEVELS - 1
    center_top, coupling_top = level_coeffs(top_level)
    correct = omega * current / center_top
    for sweep_id in range(COARSE - 1):
        correct = correct + omega * (current - apply(correct, top_level)) / center_top
    updated = correct_two + grow(correct)
    post = updated + omega * (field - apply(updated, level_two)) / center
    padded = [2 * size + 2 for size in block]
    for dim in range(3):
        index = [(starts[dim] + (p - 1) // 2) % grid[dim] for p in range(padded[dim])]
        post = np.take(post, index, axis=dim)
    rim = np.zeros(padded, np.int32)
    for dim in range(3):
        edge = np.zeros(padded[dim], np.int32)
        edge[0] = edge[-1] = 1
        rim = rim + edge.reshape([-1 if d == dim else 1 for d in range(3)])
    post = post * (rim <= 1)[..., None]
    order = []
    for iy in range(len(offsets[1])):
        for iz in range(len(offsets[2])):
            for ix in range(len(offsets[0])):
                for lx in range(block[0]):
                    for ly in range(block[1]):
                        for lz in range(block[2]):
                            x = ix * block[0] + lx
                            y = iy * block[1] + ly
                            z = iz * block[2] + lz
                            order.append((x * grid[1] + y) * grid[2] + z)
    post = post.reshape(-1, cells)[:, np.array(order)]
    return post.astype(np.float32)


def prolong_face(face, dim):
    for other in range(3):
        if other != dim:
            face = jnp.repeat(face, 2, other)
    return face


def coarse_faces(halo_block, dim):
    inner = halo_block
    for other in range(3):
        if other != dim:
            inner = lax.slice_in_dim(inner, 1, inner.shape[other] - 1, axis=other)
    size = inner.shape[dim]
    lo = lax.slice_in_dim(inner, 0, 1, axis=dim)
    hi = lax.slice_in_dim(inner, size - 1, size, axis=dim)
    return lo, hi


def post_smooth(level_id, corr, corr_faces, rhs, coarse_inner, coarse_face_list):
    center, coupling = level_coeffs(level_id)
    updated = corr + prolong(coarse_inner)
    faces = []
    for dim in range(3):
        lo = corr_faces[dim][0] + prolong_face(coarse_face_list[dim][0], dim)
        hi = corr_faces[dim][1] + prolong_face(coarse_face_list[dim][1], dim)
        faces.append((lo, hi))
    return updated + omega * (rhs - stencil(updated, faces, level_id)) / center


def post_smooth_padded(level_id, corr_padded, rhs, coarse_inner, coarse_face_list):
    center, coupling = level_coeffs(level_id)
    faces = [(prolong_face(lo, dim), prolong_face(hi, dim)) for dim, (lo, hi) in enumerate(coarse_face_list)]
    updated_padded = corr_padded + pad_with(prolong(coarse_inner), faces)
    updated = updated_padded[1:-1, 1:-1, 1:-1]
    return updated + omega * (rhs - padded_stencil(updated_padded, level_id)) / center


def dim_mask(box_part, offset, extent):
    cells = offset + jnp.arange(extent, dtype=jnp.int32)[:, None]
    return ((box_part[0][None, :] <= cells) & (cells < box_part[1][None, :])).astype(jnp.float32)


def gram_matrix(tiles_by_step, inv_tiles, tile_pairs, orb_count):
    count = lax.axis_size("gx")
    local = inv_tiles.shape[0]
    tile_edge = inv_tiles.shape[1]
    me = lax.axis_index("gx")
    total = jnp.zeros((orb_count, orb_count), jnp.float32)
    for step in range(count):
        piece = tiles_by_step.get(step)
        if piece is None:
            piece = inv_tiles if step == 0 else shifted(inv_tiles, "gx", step)
        owner = (me + step) % count
        for slot in range(local):
            tile_id = owner * local + slot
            row = tile_pairs[tile_id, 0] * tile_edge
            col = tile_pairs[tile_id, 1] * tile_edge
            total = lax.dynamic_update_slice(total, piece[slot], (row, col))
    return total


def vcycle(residuals, inv_tiles):
    center, coupling = level_coeffs(0)
    faces_zero = all_faces(residuals, lambda part: omega * part.astype(jnp.float32) / center)
    rhs_zero = residuals.astype(jnp.float32)
    corr_zero = omega * rhs_zero / center
    rhs_one = restrict(rhs_zero - stencil(corr_zero, faces_zero, 0))
    center, coupling = level_coeffs(1)
    corr_one = omega * rhs_one / center
    padded_one = pad_with(corr_one, all_faces(corr_one))
    rhs_two = restrict(rhs_one - padded_stencil(padded_one, 1))
    coarse_padded, tiles_by_step = coarse_solve(rhs_two, inv_tiles)
    center, coupling = level_coeffs(1)
    updated_padded = padded_one + coarse_padded
    updated = updated_padded[1:-1, 1:-1, 1:-1]
    post_one = updated + omega * (rhs_one - padded_stencil(updated_padded, 1)) / center
    return post_smooth(0, corr_zero, faces_zero, rhs_zero, post_one, all_faces(post_one)), tiles_by_step


def body(residuals, patch_box, tile_pairs, inv_tiles):
    size_a, size_b, size_c, orb_count = residuals.shape
    lanes = LANES if orb_count % LANES == 0 else orb_count
    grouped = residuals.reshape(size_a, size_b, size_c, orb_count // lanes, lanes)
    correct, tiles_by_step = vcycle(grouped, inv_tiles)
    correct = correct.reshape(size_a, size_b, size_c, orb_count)
    gram = gram_matrix(tiles_by_step, inv_tiles, tile_pairs, orb_count)
    mask_first = dim_mask(patch_box[0], lax.axis_index("gx") * size_a, size_a)
    mask_second = dim_mask(patch_box[1], lax.axis_index("gy") * size_b, size_b)
    mask_third = dim_mask(patch_box[2], lax.axis_index("gz") * size_c, size_c)
    precond = correct * (
        mask_first[:, None, None, :] * mask_second[None, :, None, :] * mask_third[None, None, :, :]
    )
    cell_count = size_a * size_b * size_c
    rows = lax.optimization_barrier(precond.reshape(cell_count, orb_count))
    mixed = jnp.dot(rows, gram, precision=lax.Precision.HIGH, preferred_element_type=jnp.float32)
    return mixed.reshape(size_a, size_b, size_c, orb_count).astype(jnp.bfloat16)


def solution(mesh):
    return jax.shard_map(
        body,
        mesh=mesh,
        in_specs=(P("gx", "gy", "gz", None), P(), P(), P("gx", None, None)),
        out_specs=P("gx", "gy", "gz", None),
        check_vma=False,
    )
```

```python
import jax
import jax.numpy as jnp
import numpy as np
from jax import lax
from jax.sharding import PartitionSpec as P

LEVELS = 4
COARSE = 4


omega = 0.8
shift_sigma = 0.01

GRID_AXES = (("gx", 0), ("gy", 1), ("gz", 2))
COARSE_HALO = 10
LANES = 128


def shifted(block, axis, offset):
    count = lax.axis_size(axis)
    step = offset % count
    if step == 0:
        return block
    return lax.ppermute(block, axis, [(j, (j - step) % count) for j in range(count)])


def axis_faces(block, axis, dim, prepare=None):
    count = lax.axis_size(axis)
    first = lax.slice_in_dim(block, 0, 1, axis=dim)
    last = lax.slice_in_dim(block, block.shape[dim] - 1, None, axis=dim)
    if prepare is not None:
        first = prepare(first)
        last = prepare(last)
    if count == 1:
        return last, first
    if count == 2:
        both = lax.ppermute(jnp.concatenate([first, last], axis=dim), axis, [(0, 1), (1, 0)])
        hi = lax.slice_in_dim(both, 0, 1, axis=dim)
        lo = lax.slice_in_dim(both, 1, 2, axis=dim)
        return lo, hi
    lo = shifted(last, axis, -1)
    hi = shifted(first, axis, 1)
    return lo, hi


def all_faces(block, prepare=None):
    return [axis_faces(block, axis, dim, prepare) for axis, dim in GRID_AXES]


def extend_axis(block, axis, dim, halo, extra=None):
    count = lax.axis_size(axis)
    size = block.shape[dim]
    reach = -(-halo // size)
    if 2 * reach + 1 >= count:
        offsets = list(range(count))
        start = 0
    else:
        offsets = list(range(-reach, reach + 1))
        start = reach * size
    cache = {}
    extras = {}
    pieces = []
    for offset in offsets:
        step = offset % count
        if step not in cache:
            if extra is None or step == 0:
                cache[step] = shifted(block, axis, step)
                extras[step] = extra
            else:
                both = jnp.concatenate([block.reshape(-1), extra.reshape(-1)])
                both = shifted(both, axis, step)
                cache[step] = both[: block.size].reshape(block.shape)
                extras[step] = both[block.size :].reshape(extra.shape)
        pieces.append(cache[step])
    return jnp.concatenate(pieces, axis=dim), start, extras


def axis_offsets(count, size, halo):
    reach = -(-halo // size)
    if 2 * reach + 1 >= count:
        return list(range(count)), 0
    return list(range(-reach, reach + 1)), reach * size


def extend_joint(block, axes, dims, halo):
    counts = [lax.axis_size(axis) for axis in axes]
    plans = [axis_offsets(count, block.shape[dim], halo) for count, dim in zip(counts, dims)]
    cache = {}

    def fetch(offset):
        steps = tuple(o % c for o, c in zip(offset, counts))
        if steps not in cache:
            if not any(steps):
                cache[steps] = block
            else:
                pairs = []
                for target in range(_prod(counts)):
                    coords = _unravel(target, counts)
                    source = _ravel([(c + s) % n for c, s, n in zip(coords, steps, counts)], counts)
                    pairs.append((source, target))
                cache[steps] = lax.ppermute(block, tuple(axes), pairs)
        return cache[steps]

    def assemble(level, prefix):
        offsets, start = plans[level]
        if level == len(axes) - 1:
            pieces = [fetch(prefix + (o,)) for o in offsets]
        else:
            pieces = [assemble(level + 1, prefix + (o,)) for o in offsets]
        return jnp.concatenate(pieces, axis=dims[level])

    return assemble(0, ()), [start for offsets, start in plans]


def _prod(values):
    total = 1
    for v in values:
        total *= v
    return total


def _unravel(index, counts):
    coords = []
    for n in reversed(counts):
        coords.append(index % n)
        index //= n
    return list(reversed(coords))


def _ravel(coords, counts):
    index = 0
    for c, n in zip(coords, counts):
        index = index * n + c
    return index


def level_coeffs(level_id):
    coupling = 0.5 / 4.0**level_id
    return (6.0 * coupling + shift_sigma, coupling)


def pad_with(block, faces):
    padded = block
    for dim, (lo, hi) in enumerate(faces):
        widths = [(0, 0)] * block.ndim
        for other in range(dim):
            widths[other] = (1, 1)
        lo = jnp.pad(lo, widths)
        hi = jnp.pad(hi, widths)
        padded = jnp.concatenate([lo, padded, hi], axis=dim)
    return padded


def stencil(block, faces, level_id):
    return padded_stencil(pad_with(block, faces), level_id)


def padded_stencil(padded, level_id):
    center, coupling = level_coeffs(level_id)
    middle = padded[1:-1, 1:-1, 1:-1]
    beside = padded[2:, 1:-1, 1:-1] + padded[:-2, 1:-1, 1:-1]
    beside = beside + padded[1:-1, 2:, 1:-1] + padded[1:-1, :-2, 1:-1]
    beside = beside + padded[1:-1, 1:-1, 2:] + padded[1:-1, 1:-1, :-2]
    return center * middle - coupling * beside


def restrict(field):
    size_a, size_b, size_c = field.shape[:3]
    rest = field.shape[3:]
    return field.reshape((size_a // 2, 2, size_b // 2, 2, size_c // 2, 2) + rest).mean(axis=(1, 3, 5))


def prolong(field):
    return jnp.repeat(jnp.repeat(jnp.repeat(field, 2, 0), 2, 1), 2, 2)


def coarse_solve(rhs_two, tiles):
    extended = rhs_two
    starts = []
    extended, start, tiles_by_step = extend_axis(extended, "gx", 0, COARSE_HALO, tiles)
    starts.append(start)
    extended, joint_starts = extend_joint(extended, ("gy", "gz"), (1, 2), COARSE_HALO)
    starts.extend(joint_starts)
    grid = extended.shape[:3]
    orbs = extended.shape[3:]
    operator = coarse_matrix(grid, tuple(starts), rhs_two.shape[:3])
    operator = jnp.asarray(operator.reshape((-1,) + tuple(grid)))
    post = jnp.einsum(
        "qxyz,xyzgl->qgl", operator, extended, precision=lax.Precision.HIGHEST, preferred_element_type=jnp.float32
    )
    return post.reshape(tuple(2 * size + 2 for size in rhs_two.shape[:3]) + orbs), tiles_by_step


def coarse_matrix(grid, starts, block):
    cells = int(np.prod(grid))
    field = np.eye(cells).reshape(grid + (cells,))

    def apply(v, level_id):
        center, coupling = level_coeffs(level_id)
        beside = 0.0
        for dim in range(3):
            beside = beside + np.roll(v, -1, dim) + np.roll(v, 1, dim)
        return center * v - coupling * beside

    def shrink(v):
        a, b, c = v.shape[:3]
        return v.reshape(a // 2, 2, b // 2, 2, c // 2, 2, -1).mean(axis=(1, 3, 5))

    def grow(v):
        return np.repeat(np.repeat(np.repeat(v, 2, 0), 2, 1), 2, 2)

    level_two = LEVELS - 2
    center, coupling = level_coeffs(level_two)
    correct_two = omega * field / center
    current = shrink(field - apply(correct_two, level_two))
    top_level = LEVELS - 1
    center_top, coupling_top = level_coeffs(top_level)
    correct = omega * current / center_top
    for sweep_id in range(COARSE - 1):
        correct = correct + omega * (current - apply(correct, top_level)) / center_top
    updated = correct_two + grow(correct)
    post = updated + omega * (field - apply(updated, level_two)) / center
    padded = [2 * size + 2 for size in block]
    for dim in range(3):
        index = [(starts[dim] + (p - 1) // 2) % grid[dim] for p in range(padded[dim])]
        post = np.take(post, index, axis=dim)
    rim = np.zeros(padded, np.int32)
    for dim in range(3):
        edge = np.zeros(padded[dim], np.int32)
        edge[0] = edge[-1] = 1
        rim = rim + edge.reshape([-1 if d == dim else 1 for d in range(3)])
    post = post * (rim <= 1)[..., None]
    post = post.reshape(-1, cells)
    return post.astype(np.float32)


def prolong_face(face, dim):
    for other in range(3):
        if other != dim:
            face = jnp.repeat(face, 2, other)
    return face


def coarse_faces(halo_block, dim):
    inner = halo_block
    for other in range(3):
        if other != dim:
            inner = lax.slice_in_dim(inner, 1, inner.shape[other] - 1, axis=other)
    size = inner.shape[dim]
    lo = lax.slice_in_dim(inner, 0, 1, axis=dim)
    hi = lax.slice_in_dim(inner, size - 1, size, axis=dim)
    return lo, hi


def post_smooth(level_id, corr, corr_faces, rhs, coarse_inner, coarse_face_list):
    center, coupling = level_coeffs(level_id)
    updated = corr + prolong(coarse_inner)
    faces = []
    for dim in range(3):
        lo = corr_faces[dim][0] + prolong_face(coarse_face_list[dim][0], dim)
        hi = corr_faces[dim][1] + prolong_face(coarse_face_list[dim][1], dim)
        faces.append((lo, hi))
    return updated + omega * (rhs - stencil(updated, faces, level_id)) / center


def post_smooth_padded(level_id, corr_padded, rhs, coarse_inner, coarse_face_list):
    center, coupling = level_coeffs(level_id)
    faces = [(prolong_face(lo, dim), prolong_face(hi, dim)) for dim, (lo, hi) in enumerate(coarse_face_list)]
    updated_padded = corr_padded + pad_with(prolong(coarse_inner), faces)
    updated = updated_padded[1:-1, 1:-1, 1:-1]
    return updated + omega * (rhs - padded_stencil(updated_padded, level_id)) / center


def dim_mask(box_part, offset, extent):
    cells = offset + jnp.arange(extent, dtype=jnp.int32)[:, None]
    return ((box_part[0][None, :] <= cells) & (cells < box_part[1][None, :])).astype(jnp.float32)


def gram_matrix(tiles_by_step, inv_tiles, tile_pairs, orb_count):
    count = lax.axis_size("gx")
    local = inv_tiles.shape[0]
    tile_edge = inv_tiles.shape[1]
    me = lax.axis_index("gx")
    total = jnp.zeros((orb_count, orb_count), jnp.float32)
    for step in range(count):
        piece = tiles_by_step.get(step)
        if piece is None:
            piece = inv_tiles if step == 0 else shifted(inv_tiles, "gx", step)
        owner = (me + step) % count
        for slot in range(local):
            tile_id = owner * local + slot
            row = tile_pairs[tile_id, 0] * tile_edge
            col = tile_pairs[tile_id, 1] * tile_edge
            total = lax.dynamic_update_slice(total, piece[slot], (row, col))
    return total


def vcycle(residuals, inv_tiles):
    center, coupling = level_coeffs(0)
    faces_zero = all_faces(residuals, lambda part: omega * part.astype(jnp.float32) / center)
    rhs_zero = residuals.astype(jnp.float32)
    corr_zero = omega * rhs_zero / center
    rhs_one = restrict(rhs_zero - stencil(corr_zero, faces_zero, 0))
    center, coupling = level_coeffs(1)
    corr_one = omega * rhs_one / center
    padded_one = pad_with(corr_one, all_faces(corr_one))
    rhs_two = restrict(rhs_one - padded_stencil(padded_one, 1))
    coarse_padded, tiles_by_step = coarse_solve(rhs_two, inv_tiles)
    center, coupling = level_coeffs(1)
    updated_padded = padded_one + coarse_padded
    updated = updated_padded[1:-1, 1:-1, 1:-1]
    post_one = updated + omega * (rhs_one - padded_stencil(updated_padded, 1)) / center
    return post_smooth(0, corr_zero, faces_zero, rhs_zero, post_one, all_faces(post_one)), tiles_by_step


def body(residuals, patch_box, tile_pairs, inv_tiles):
    size_a, size_b, size_c, orb_count = residuals.shape
    lanes = LANES if orb_count % LANES == 0 else orb_count
    grouped = residuals.reshape(size_a, size_b, size_c, orb_count // lanes, lanes)
    correct, tiles_by_step = vcycle(grouped, inv_tiles)
    correct = correct.reshape(size_a, size_b, size_c, orb_count)
    gram = gram_matrix(tiles_by_step, inv_tiles, tile_pairs, orb_count)
    mask_first = dim_mask(patch_box[0], lax.axis_index("gx") * size_a, size_a)
    mask_second = dim_mask(patch_box[1], lax.axis_index("gy") * size_b, size_b)
    mask_third = dim_mask(patch_box[2], lax.axis_index("gz") * size_c, size_c)
    precond = correct * (
        mask_first[:, None, None, :] * mask_second[None, :, None, :] * mask_third[None, None, :, :]
    )
    cell_count = size_a * size_b * size_c
    rows = lax.optimization_barrier(precond.reshape(cell_count, orb_count))
    mixed = jnp.dot(rows, gram, precision=lax.Precision.HIGH, preferred_element_type=jnp.float32)
    return mixed.reshape(size_a, size_b, size_c, orb_count).astype(jnp.bfloat16)


def solution(mesh):
    return jax.shard_map(
        body,
        mesh=mesh,
        in_specs=(P("gx", "gy", "gz", None), P(), P(), P("gx", None, None)),
        out_specs=P("gx", "gy", "gz", None),
        check_vma=False,
    )
```

```python
import jax
import jax.numpy as jnp
import numpy as np
from jax import lax
from jax.sharding import PartitionSpec as P

LEVELS = 4
COARSE = 4


omega = 0.8
shift_sigma = 0.01

GRID_AXES = (("gx", 0), ("gy", 1), ("gz", 2))
COARSE_HALO = 10
LANES = 128


def shifted(block, axis, offset):
    count = lax.axis_size(axis)
    step = offset % count
    if step == 0:
        return block
    return lax.ppermute(block, axis, [(j, (j - step) % count) for j in range(count)])


def axis_faces(block, axis, dim, prepare=None):
    count = lax.axis_size(axis)
    first = lax.slice_in_dim(block, 0, 1, axis=dim)
    last = lax.slice_in_dim(block, block.shape[dim] - 1, None, axis=dim)
    if prepare is not None:
        first = prepare(first)
        last = prepare(last)
    if count == 1:
        return last, first
    if count == 2:
        both = lax.ppermute(jnp.concatenate([first, last], axis=dim), axis, [(0, 1), (1, 0)])
        hi = lax.slice_in_dim(both, 0, 1, axis=dim)
        lo = lax.slice_in_dim(both, 1, 2, axis=dim)
        return lo, hi
    lo = shifted(last, axis, -1)
    hi = shifted(first, axis, 1)
    return lo, hi


def all_faces(block, prepare=None):
    return [axis_faces(block, axis, dim, prepare) for axis, dim in GRID_AXES]


def extend_axis(block, axis, dim, halo, extra=None):
    count = lax.axis_size(axis)
    size = block.shape[dim]
    reach = -(-halo // size)
    if 2 * reach + 1 >= count:
        offsets = list(range(count))
        start = 0
    else:
        offsets = list(range(-reach, reach + 1))
        start = reach * size
    cache = {}
    extras = {}
    pieces = []
    for offset in offsets:
        step = offset % count
        if step not in cache:
            if extra is None or step == 0:
                cache[step] = shifted(block, axis, step)
                extras[step] = extra
            else:
                trailing = block.shape[1:]
                if extra.size % int(np.prod(trailing)) == 0:
                    both = jnp.concatenate([block, extra.reshape((-1,) + trailing)], axis=0)
                    both = shifted(both, axis, step)
                    cache[step] = both[: block.shape[0]]
                    extras[step] = both[block.shape[0] :].reshape(extra.shape)
                else:
                    both = jnp.concatenate([block.reshape(-1), extra.reshape(-1)])
                    both = shifted(both, axis, step)
                    cache[step] = both[: block.size].reshape(block.shape)
                    extras[step] = both[block.size :].reshape(extra.shape)
        pieces.append(cache[step])
    return jnp.concatenate(pieces, axis=dim), start, extras


def axis_offsets(count, size, halo):
    reach = -(-halo // size)
    if 2 * reach + 1 >= count:
        return list(range(count)), 0
    return list(range(-reach, reach + 1)), reach * size


def extend_joint(block, axes, dims, halo):
    counts = [lax.axis_size(axis) for axis in axes]
    plans = [axis_offsets(count, block.shape[dim], halo) for count, dim in zip(counts, dims)]
    cache = {}

    def fetch(offset):
        steps = tuple(o % c for o, c in zip(offset, counts))
        if steps not in cache:
            if not any(steps):
                cache[steps] = block
            else:
                pairs = []
                for target in range(_prod(counts)):
                    coords = _unravel(target, counts)
                    source = _ravel([(c + s) % n for c, s, n in zip(coords, steps, counts)], counts)
                    pairs.append((source, target))
                cache[steps] = lax.ppermute(block, tuple(axes), pairs)
        return cache[steps]

    def assemble(level, prefix):
        offsets, start = plans[level]
        if level == len(axes) - 1:
            pieces = [fetch(prefix + (o,)) for o in offsets]
        else:
            pieces = [assemble(level + 1, prefix + (o,)) for o in offsets]
        return jnp.concatenate(pieces, axis=dims[level])

    return assemble(0, ()), [start for offsets, start in plans]


def _prod(values):
    total = 1
    for v in values:
        total *= v
    return total


def _unravel(index, counts):
    coords = []
    for n in reversed(counts):
        coords.append(index % n)
        index //= n
    return list(reversed(coords))


def _ravel(coords, counts):
    index = 0
    for c, n in zip(coords, counts):
        index = index * n + c
    return index


def level_coeffs(level_id):
    coupling = 0.5 / 4.0**level_id
    return (6.0 * coupling + shift_sigma, coupling)


def pad_with(block, faces):
    padded = block
    for dim, (lo, hi) in enumerate(faces):
        widths = [(0, 0)] * block.ndim
        for other in range(dim):
            widths[other] = (1, 1)
        lo = jnp.pad(lo, widths)
        hi = jnp.pad(hi, widths)
        padded = jnp.concatenate([lo, padded, hi], axis=dim)
    return padded


def stencil(block, faces, level_id):
    return padded_stencil(pad_with(block, faces), level_id)


def padded_stencil(padded, level_id):
    center, coupling = level_coeffs(level_id)
    middle = padded[1:-1, 1:-1, 1:-1]
    beside = padded[2:, 1:-1, 1:-1] + padded[:-2, 1:-1, 1:-1]
    beside = beside + padded[1:-1, 2:, 1:-1] + padded[1:-1, :-2, 1:-1]
    beside = beside + padded[1:-1, 1:-1, 2:] + padded[1:-1, 1:-1, :-2]
    return center * middle - coupling * beside


def restrict(field):
    size_a, size_b, size_c = field.shape[:3]
    rest = field.shape[3:]
    return field.reshape((size_a // 2, 2, size_b // 2, 2, size_c // 2, 2) + rest).mean(axis=(1, 3, 5))


def prolong(field):
    return jnp.repeat(jnp.repeat(jnp.repeat(field, 2, 0), 2, 1), 2, 2)


def coarse_solve(rhs_two, tiles):
    extended = rhs_two
    starts = []
    extended, start, tiles_by_step = extend_axis(extended, "gx", 0, COARSE_HALO, tiles)
    starts.append(start)
    extended, joint_starts = extend_joint(extended, ("gy", "gz"), (1, 2), COARSE_HALO)
    starts.extend(joint_starts)
    grid = extended.shape[:3]
    orbs = extended.shape[3:]
    operator = coarse_matrix(grid, tuple(starts), rhs_two.shape[:3])
    operator = jnp.asarray(operator.reshape((-1,) + tuple(grid)))
    post = jnp.einsum(
        "qxyz,xyzgl->qgl", operator, extended, precision=lax.Precision.HIGHEST, preferred_element_type=jnp.float32
    )
    return post.reshape(tuple(2 * size + 2 for size in rhs_two.shape[:3]) + orbs), tiles_by_step


def coarse_matrix(grid, starts, block):
    cells = int(np.prod(grid))
    field = np.eye(cells).reshape(grid + (cells,))

    def apply(v, level_id):
        center, coupling = level_coeffs(level_id)
        beside = 0.0
        for dim in range(3):
            beside = beside + np.roll(v, -1, dim) + np.roll(v, 1, dim)
        return center * v - coupling * beside

    def shrink(v):
        a, b, c = v.shape[:3]
        return v.reshape(a // 2, 2, b // 2, 2, c // 2, 2, -1).mean(axis=(1, 3, 5))

    def grow(v):
        return np.repeat(np.repeat(np.repeat(v, 2, 0), 2, 1), 2, 2)

    level_two = LEVELS - 2
    center, coupling = level_coeffs(level_two)
    correct_two = omega * field / center
    current = shrink(field - apply(correct_two, level_two))
    top_level = LEVELS - 1
    center_top, coupling_top = level_coeffs(top_level)
    correct = omega * current / center_top
    for sweep_id in range(COARSE - 1):
        correct = correct + omega * (current - apply(correct, top_level)) / center_top
    updated = correct_two + grow(correct)
    post = updated + omega * (field - apply(updated, level_two)) / center
    padded = [2 * size + 2 for size in block]
    for dim in range(3):
        index = [(starts[dim] + (p - 1) // 2) % grid[dim] for p in range(padded[dim])]
        post = np.take(post, index, axis=dim)
    rim = np.zeros(padded, np.int32)
    for dim in range(3):
        edge = np.zeros(padded[dim], np.int32)
        edge[0] = edge[-1] = 1
        rim = rim + edge.reshape([-1 if d == dim else 1 for d in range(3)])
    post = post * (rim <= 1)[..., None]
    post = post.reshape(-1, cells)
    return post.astype(np.float32)


def prolong_face(face, dim):
    for other in range(3):
        if other != dim:
            face = jnp.repeat(face, 2, other)
    return face


def coarse_faces(halo_block, dim):
    inner = halo_block
    for other in range(3):
        if other != dim:
            inner = lax.slice_in_dim(inner, 1, inner.shape[other] - 1, axis=other)
    size = inner.shape[dim]
    lo = lax.slice_in_dim(inner, 0, 1, axis=dim)
    hi = lax.slice_in_dim(inner, size - 1, size, axis=dim)
    return lo, hi


def post_smooth(level_id, corr, corr_faces, rhs, coarse_inner, coarse_face_list):
    center, coupling = level_coeffs(level_id)
    updated = corr + prolong(coarse_inner)
    faces = []
    for dim in range(3):
        lo = corr_faces[dim][0] + prolong_face(coarse_face_list[dim][0], dim)
        hi = corr_faces[dim][1] + prolong_face(coarse_face_list[dim][1], dim)
        faces.append((lo, hi))
    return updated + omega * (rhs - stencil(updated, faces, level_id)) / center


def post_smooth_padded(level_id, corr_padded, rhs, coarse_inner, coarse_face_list):
    center, coupling = level_coeffs(level_id)
    faces = [(prolong_face(lo, dim), prolong_face(hi, dim)) for dim, (lo, hi) in enumerate(coarse_face_list)]
    updated_padded = corr_padded + pad_with(prolong(coarse_inner), faces)
    updated = updated_padded[1:-1, 1:-1, 1:-1]
    return updated + omega * (rhs - padded_stencil(updated_padded, level_id)) / center


def dim_mask(box_part, offset, extent):
    cells = offset + jnp.arange(extent, dtype=jnp.int32)[:, None]
    return ((box_part[0][None, :] <= cells) & (cells < box_part[1][None, :])).astype(jnp.float32)


def gram_matrix(tiles_by_step, inv_tiles, tile_pairs, orb_count):
    count = lax.axis_size("gx")
    local = inv_tiles.shape[0]
    tile_edge = inv_tiles.shape[1]
    me = lax.axis_index("gx")
    total = jnp.zeros((orb_count, orb_count), jnp.float32)
    for step in range(count):
        piece = tiles_by_step.get(step)
        if piece is None:
            piece = inv_tiles if step == 0 else shifted(inv_tiles, "gx", step)
        owner = (me + step) % count
        for slot in range(local):
            tile_id = owner * local + slot
            row = tile_pairs[tile_id, 0] * tile_edge
            col = tile_pairs[tile_id, 1] * tile_edge
            total = lax.dynamic_update_slice(total, piece[slot], (row, col))
    return total


def vcycle(residuals, inv_tiles):
    center, coupling = level_coeffs(0)
    faces_zero = all_faces(residuals, lambda part: omega * part.astype(jnp.float32) / center)
    rhs_zero = residuals.astype(jnp.float32)
    corr_zero = omega * rhs_zero / center
    rhs_one = restrict(rhs_zero - stencil(corr_zero, faces_zero, 0))
    center, coupling = level_coeffs(1)
    corr_one = omega * rhs_one / center
    padded_one = pad_with(corr_one, all_faces(corr_one))
    rhs_two = restrict(rhs_one - padded_stencil(padded_one, 1))
    coarse_padded, tiles_by_step = coarse_solve(rhs_two, inv_tiles)
    center, coupling = level_coeffs(1)
    updated_padded = padded_one + coarse_padded
    updated = updated_padded[1:-1, 1:-1, 1:-1]
    post_one = updated + omega * (rhs_one - padded_stencil(updated_padded, 1)) / center
    return post_smooth(0, corr_zero, faces_zero, rhs_zero, post_one, all_faces(post_one)), tiles_by_step


def body(residuals, patch_box, tile_pairs, inv_tiles):
    size_a, size_b, size_c, orb_count = residuals.shape
    lanes = LANES if orb_count % LANES == 0 else orb_count
    grouped = residuals.reshape(size_a, size_b, size_c, orb_count // lanes, lanes)
    correct, tiles_by_step = vcycle(grouped, inv_tiles)
    correct = correct.reshape(size_a, size_b, size_c, orb_count)
    gram = gram_matrix(tiles_by_step, inv_tiles, tile_pairs, orb_count)
    mask_first = dim_mask(patch_box[0], lax.axis_index("gx") * size_a, size_a)
    mask_second = dim_mask(patch_box[1], lax.axis_index("gy") * size_b, size_b)
    mask_third = dim_mask(patch_box[2], lax.axis_index("gz") * size_c, size_c)
    precond = correct * (
        mask_first[:, None, None, :] * mask_second[None, :, None, :] * mask_third[None, None, :, :]
    )
    cell_count = size_a * size_b * size_c
    rows = lax.optimization_barrier(precond.reshape(cell_count, orb_count))
    mixed = jnp.dot(rows, gram, precision=lax.Precision.HIGH, preferred_element_type=jnp.float32)
    return mixed.reshape(size_a, size_b, size_c, orb_count).astype(jnp.bfloat16)


def solution(mesh):
    return jax.shard_map(
        body,
        mesh=mesh,
        in_specs=(P("gx", "gy", "gz", None), P(), P(), P("gx", None, None)),
        out_specs=P("gx", "gy", "gz", None),
        check_vma=False,
    )
```

```python
import jax
import jax.numpy as jnp
import numpy as np
from jax import lax
from jax.sharding import PartitionSpec as P

LEVELS = 4
COARSE = 4


omega = 0.8
shift_sigma = 0.01

GRID_AXES = (("gx", 0), ("gy", 1), ("gz", 2))
COARSE_HALO = 10
LANES = 128


def shifted(block, axis, offset):
    count = lax.axis_size(axis)
    step = offset % count
    if step == 0:
        return block
    return lax.ppermute(block, axis, [(j, (j - step) % count) for j in range(count)])


def axis_faces(block, axis, dim, prepare=None):
    count = lax.axis_size(axis)
    first = lax.slice_in_dim(block, 0, 1, axis=dim)
    last = lax.slice_in_dim(block, block.shape[dim] - 1, None, axis=dim)
    if prepare is not None:
        first = prepare(first)
        last = prepare(last)
    if count == 1:
        return last, first
    if count == 2:
        both = lax.ppermute(jnp.concatenate([first, last], axis=dim), axis, [(0, 1), (1, 0)])
        hi = lax.slice_in_dim(both, 0, 1, axis=dim)
        lo = lax.slice_in_dim(both, 1, 2, axis=dim)
        return lo, hi
    lo = shifted(last, axis, -1)
    hi = shifted(first, axis, 1)
    return lo, hi


def all_faces(block, prepare=None):
    return [axis_faces(block, axis, dim, prepare) for axis, dim in GRID_AXES]


def extend_axis(block, axis, dim, halo, extra=None):
    count = lax.axis_size(axis)
    size = block.shape[dim]
    reach = -(-halo // size)
    if 2 * reach + 1 >= count:
        offsets = list(range(count))
        start = 0
    else:
        offsets = list(range(-reach, reach + 1))
        start = reach * size
    cache = {}
    extras = {}
    pieces = []
    for offset in offsets:
        step = offset % count
        if step not in cache:
            if extra is None or step == 0:
                cache[step] = shifted(block, axis, step)
                extras[step] = extra
            else:
                trailing = block.shape[1:]
                if extra.size % int(np.prod(trailing)) == 0:
                    both = jnp.concatenate([block, extra.reshape((-1,) + trailing)], axis=0)
                    both = shifted(both, axis, step)
                    cache[step] = both[: block.shape[0]]
                    extras[step] = both[block.shape[0] :].reshape(extra.shape)
                else:
                    both = jnp.concatenate([block.reshape(-1), extra.reshape(-1)])
                    both = shifted(both, axis, step)
                    cache[step] = both[: block.size].reshape(block.shape)
                    extras[step] = both[block.size :].reshape(extra.shape)
        pieces.append(cache[step])
    return jnp.concatenate(pieces, axis=dim), start, extras


def axis_offsets(count, size, halo):
    reach = -(-halo // size)
    if 2 * reach + 1 >= count:
        return list(range(count)), 0
    return list(range(-reach, reach + 1)), reach * size


def extend_joint(block, axes, dims, halo):
    counts = [lax.axis_size(axis) for axis in axes]
    plans = [axis_offsets(count, block.shape[dim], halo) for count, dim in zip(counts, dims)]
    cache = {}

    def fetch(offset):
        steps = tuple(o % c for o, c in zip(offset, counts))
        if steps not in cache:
            if not any(steps):
                cache[steps] = block
            else:
                pairs = []
                for target in range(_prod(counts)):
                    coords = _unravel(target, counts)
                    source = _ravel([(c + s) % n for c, s, n in zip(coords, steps, counts)], counts)
                    pairs.append((source, target))
                cache[steps] = lax.ppermute(block, tuple(axes), pairs)
        return cache[steps]

    def assemble(level, prefix):
        offsets, start = plans[level]
        if level == len(axes) - 1:
            pieces = [fetch(prefix + (o,)) for o in offsets]
        else:
            pieces = [assemble(level + 1, prefix + (o,)) for o in offsets]
        return jnp.concatenate(pieces, axis=dims[level])

    return assemble(0, ()), [start for offsets, start in plans]


def _prod(values):
    total = 1
    for v in values:
        total *= v
    return total


def _unravel(index, counts):
    coords = []
    for n in reversed(counts):
        coords.append(index % n)
        index //= n
    return list(reversed(coords))


def _ravel(coords, counts):
    index = 0
    for c, n in zip(coords, counts):
        index = index * n + c
    return index


def level_coeffs(level_id):
    coupling = 0.5 / 4.0**level_id
    return (6.0 * coupling + shift_sigma, coupling)


def pad_with(block, faces):
    padded = block
    for dim, (lo, hi) in enumerate(faces):
        widths = [(0, 0)] * block.ndim
        for other in range(dim):
            widths[other] = (1, 1)
        lo = jnp.pad(lo, widths)
        hi = jnp.pad(hi, widths)
        padded = jnp.concatenate([lo, padded, hi], axis=dim)
    return padded


def stencil(block, faces, level_id):
    return padded_stencil(pad_with(block, faces), level_id)


def padded_stencil(padded, level_id):
    center, coupling = level_coeffs(level_id)
    middle = padded[1:-1, 1:-1, 1:-1]
    beside = padded[2:, 1:-1, 1:-1] + padded[:-2, 1:-1, 1:-1]
    beside = beside + padded[1:-1, 2:, 1:-1] + padded[1:-1, :-2, 1:-1]
    beside = beside + padded[1:-1, 1:-1, 2:] + padded[1:-1, 1:-1, :-2]
    return center * middle - coupling * beside


def restrict(field):
    size_a, size_b, size_c = field.shape[:3]
    rest = field.shape[3:]
    return field.reshape((size_a // 2, 2, size_b // 2, 2, size_c // 2, 2) + rest).mean(axis=(1, 3, 5))


def prolong(field):
    return jnp.repeat(jnp.repeat(jnp.repeat(field, 2, 0), 2, 1), 2, 2)


def coarse_solve(rhs_two, tiles):
    extended = rhs_two
    starts = []
    extended, start, tiles_by_step = extend_axis(extended, "gx", 0, COARSE_HALO, tiles)
    starts.append(start)
    extended, joint_starts = extend_joint(extended, ("gy", "gz"), (1, 2), COARSE_HALO)
    starts.extend(joint_starts)
    grid = extended.shape[:3]
    orbs = extended.shape[3:]
    operator = coarse_matrix(grid, tuple(starts), rhs_two.shape[:3])
    operator = jnp.asarray(operator.reshape((-1,) + tuple(grid)))
    post = jnp.einsum(
        "qxyz,xyzgl->qgl", operator, extended, precision=lax.Precision.HIGHEST, preferred_element_type=jnp.float32
    )
    return post.reshape(tuple(2 * size + 2 for size in rhs_two.shape[:3]) + orbs), tiles_by_step


def coarse_matrix(grid, starts, block):
    cells = int(np.prod(grid))
    field = np.eye(cells).reshape(grid + (cells,))

    def apply(v, level_id):
        center, coupling = level_coeffs(level_id)
        beside = 0.0
        for dim in range(3):
            beside = beside + np.roll(v, -1, dim) + np.roll(v, 1, dim)
        return center * v - coupling * beside

    def shrink(v):
        a, b, c = v.shape[:3]
        return v.reshape(a // 2, 2, b // 2, 2, c // 2, 2, -1).mean(axis=(1, 3, 5))

    def grow(v):
        return np.repeat(np.repeat(np.repeat(v, 2, 0), 2, 1), 2, 2)

    level_two = LEVELS - 2
    center, coupling = level_coeffs(level_two)
    correct_two = omega * field / center
    current = shrink(field - apply(correct_two, level_two))
    top_level = LEVELS - 1
    center_top, coupling_top = level_coeffs(top_level)
    correct = omega * current / center_top
    for sweep_id in range(COARSE - 1):
        correct = correct + omega * (current - apply(correct, top_level)) / center_top
    updated = correct_two + grow(correct)
    post = updated + omega * (field - apply(updated, level_two)) / center
    padded = [2 * size + 2 for size in block]
    for dim in range(3):
        index = [(starts[dim] + (p - 1) // 2) % grid[dim] for p in range(padded[dim])]
        post = np.take(post, index, axis=dim)
    rim = np.zeros(padded, np.int32)
    for dim in range(3):
        edge = np.zeros(padded[dim], np.int32)
        edge[0] = edge[-1] = 1
        rim = rim + edge.reshape([-1 if d == dim else 1 for d in range(3)])
    post = post * (rim <= 1)[..., None]
    post = post.reshape(-1, cells)
    return post.astype(np.float32)


def prolong_face(face, dim):
    for other in range(3):
        if other != dim:
            face = jnp.repeat(face, 2, other)
    return face


def coarse_faces(halo_block, dim):
    inner = halo_block
    for other in range(3):
        if other != dim:
            inner = lax.slice_in_dim(inner, 1, inner.shape[other] - 1, axis=other)
    size = inner.shape[dim]
    lo = lax.slice_in_dim(inner, 0, 1, axis=dim)
    hi = lax.slice_in_dim(inner, size - 1, size, axis=dim)
    return lo, hi


def post_smooth(level_id, corr, corr_faces, rhs, coarse_inner, coarse_face_list):
    center, coupling = level_coeffs(level_id)
    updated = corr + prolong(coarse_inner)
    faces = []
    for dim in range(3):
        lo = corr_faces[dim][0] + prolong_face(coarse_face_list[dim][0], dim)
        hi = corr_faces[dim][1] + prolong_face(coarse_face_list[dim][1], dim)
        faces.append((lo, hi))
    return updated + omega * (rhs - stencil(updated, faces, level_id)) / center


def post_smooth_padded(level_id, corr_padded, rhs, coarse_inner, coarse_face_list):
    center, coupling = level_coeffs(level_id)
    faces = [(prolong_face(lo, dim), prolong_face(hi, dim)) for dim, (lo, hi) in enumerate(coarse_face_list)]
    updated_padded = corr_padded + pad_with(prolong(coarse_inner), faces)
    updated = updated_padded[1:-1, 1:-1, 1:-1]
    return updated + omega * (rhs - padded_stencil(updated_padded, level_id)) / center


def dim_mask(box_part, offset, extent):
    cells = offset + jnp.arange(extent, dtype=jnp.int32)[:, None]
    return ((box_part[0][None, :] <= cells) & (cells < box_part[1][None, :])).astype(jnp.float32)


def gram_matrix(tiles_by_step, inv_tiles, tile_pairs, orb_count, later):
    count = lax.axis_size("gx")
    local = inv_tiles.shape[0]
    tile_edge = inv_tiles.shape[1]
    me = lax.axis_index("gx")
    total = jnp.zeros((orb_count, orb_count), jnp.float32) + later
    for step in range(count):
        piece = tiles_by_step.get(step)
        if piece is None:
            piece = inv_tiles if step == 0 else shifted(inv_tiles, "gx", step)
        piece = piece + later
        owner = (me + step) % count
        for slot in range(local):
            tile_id = owner * local + slot
            row = tile_pairs[tile_id, 0] * tile_edge
            col = tile_pairs[tile_id, 1] * tile_edge
            total = lax.dynamic_update_slice(total, piece[slot], (row, col))
    return total


def vcycle(residuals, inv_tiles):
    center, coupling = level_coeffs(0)
    faces_zero = all_faces(residuals, lambda part: omega * part.astype(jnp.float32) / center)
    rhs_zero = residuals.astype(jnp.float32)
    corr_zero = omega * rhs_zero / center
    rhs_one = restrict(rhs_zero - stencil(corr_zero, faces_zero, 0))
    center, coupling = level_coeffs(1)
    corr_one = omega * rhs_one / center
    padded_one = pad_with(corr_one, all_faces(corr_one))
    rhs_two = restrict(rhs_one - padded_stencil(padded_one, 1))
    coarse_padded, tiles_by_step = coarse_solve(rhs_two, inv_tiles)
    center, coupling = level_coeffs(1)
    updated_padded = padded_one + coarse_padded
    updated = updated_padded[1:-1, 1:-1, 1:-1]
    post_one = updated + omega * (rhs_one - padded_stencil(updated_padded, 1)) / center
    later = 0.0 * post_one[(0,) * post_one.ndim]
    return post_smooth(0, corr_zero, faces_zero, rhs_zero, post_one, all_faces(post_one)), tiles_by_step, later


def body(residuals, patch_box, tile_pairs, inv_tiles):
    size_a, size_b, size_c, orb_count = residuals.shape
    lanes = LANES if orb_count % LANES == 0 else orb_count
    grouped = residuals.reshape(size_a, size_b, size_c, orb_count // lanes, lanes)
    correct, tiles_by_step, later = vcycle(grouped, inv_tiles)
    correct = correct.reshape(size_a, size_b, size_c, orb_count)
    gram = gram_matrix(tiles_by_step, inv_tiles, tile_pairs, orb_count, later)
    mask_first = dim_mask(patch_box[0], lax.axis_index("gx") * size_a, size_a)
    mask_second = dim_mask(patch_box[1], lax.axis_index("gy") * size_b, size_b)
    mask_third = dim_mask(patch_box[2], lax.axis_index("gz") * size_c, size_c)
    precond = correct * (
        mask_first[:, None, None, :] * mask_second[None, :, None, :] * mask_third[None, None, :, :]
    )
    cell_count = size_a * size_b * size_c
    rows = lax.optimization_barrier(precond.reshape(cell_count, orb_count))
    mixed = jnp.dot(rows, gram, precision=lax.Precision.HIGH, preferred_element_type=jnp.float32)
    return mixed.reshape(size_a, size_b, size_c, orb_count).astype(jnp.bfloat16)


def solution(mesh):
    return jax.shard_map(
        body,
        mesh=mesh,
        in_specs=(P("gx", "gy", "gz", None), P(), P(), P("gx", None, None)),
        out_specs=P("gx", "gy", "gz", None),
        check_vma=False,
    )
```

```python
import jax
import jax.numpy as jnp
import numpy as np
from jax import lax
from jax.sharding import PartitionSpec as P

LEVELS = 4
COARSE = 4


omega = 0.8
shift_sigma = 0.01

GRID_AXES = (("gx", 0), ("gy", 1), ("gz", 2))
COARSE_HALO = 10
LANES = 128


def shifted(block, axis, offset):
    count = lax.axis_size(axis)
    step = offset % count
    if step == 0:
        return block
    return lax.ppermute(block, axis, [(j, (j - step) % count) for j in range(count)])


def axis_faces(block, axis, dim, prepare=None):
    count = lax.axis_size(axis)
    first = lax.slice_in_dim(block, 0, 1, axis=dim)
    last = lax.slice_in_dim(block, block.shape[dim] - 1, None, axis=dim)
    if prepare is not None:
        first = prepare(first)
        last = prepare(last)
    if count == 1:
        return last, first
    if count == 2:
        both = lax.ppermute(jnp.concatenate([first, last], axis=dim), axis, [(0, 1), (1, 0)])
        hi = lax.slice_in_dim(both, 0, 1, axis=dim)
        lo = lax.slice_in_dim(both, 1, 2, axis=dim)
        return lo, hi
    lo = shifted(last, axis, -1)
    hi = shifted(first, axis, 1)
    return lo, hi


def all_faces(block, prepare=None):
    return [axis_faces(block, axis, dim, prepare) for axis, dim in GRID_AXES]


def extend_axis(block, axis, dim, halo, extra=None):
    count = lax.axis_size(axis)
    size = block.shape[dim]
    reach = -(-halo // size)
    if 2 * reach + 1 >= count:
        offsets = list(range(count))
        start = 0
    else:
        offsets = list(range(-reach, reach + 1))
        start = reach * size
    cache = {}
    extras = {}
    pieces = []
    for offset in offsets:
        step = offset % count
        if step not in cache:
            if extra is None or step == 0:
                cache[step] = shifted(block, axis, step)
                extras[step] = extra
            else:
                trailing = block.shape[1:]
                if extra.size % int(np.prod(trailing)) == 0:
                    both = jnp.concatenate([block, extra.reshape((-1,) + trailing)], axis=0)
                    both = shifted(both, axis, step)
                    cache[step] = both[: block.shape[0]]
                    extras[step] = both[block.shape[0] :].reshape(extra.shape)
                else:
                    both = jnp.concatenate([block.reshape(-1), extra.reshape(-1)])
                    both = shifted(both, axis, step)
                    cache[step] = both[: block.size].reshape(block.shape)
                    extras[step] = both[block.size :].reshape(extra.shape)
        pieces.append(cache[step])
    return jnp.concatenate(pieces, axis=dim), start, extras


def axis_offsets(count, size, halo):
    reach = -(-halo // size)
    if 2 * reach + 1 >= count:
        return list(range(count)), 0
    return list(range(-reach, reach + 1)), reach * size


def extend_joint(block, axes, dims, halo):
    counts = [lax.axis_size(axis) for axis in axes]
    plans = [axis_offsets(count, block.shape[dim], halo) for count, dim in zip(counts, dims)]
    cache = {}

    def fetch(offset):
        steps = tuple(o % c for o, c in zip(offset, counts))
        if steps not in cache:
            if not any(steps):
                cache[steps] = block
            else:
                pairs = []
                for target in range(_prod(counts)):
                    coords = _unravel(target, counts)
                    source = _ravel([(c + s) % n for c, s, n in zip(coords, steps, counts)], counts)
                    pairs.append((source, target))
                cache[steps] = lax.ppermute(block, tuple(axes), pairs)
        return cache[steps]

    def assemble(level, prefix):
        offsets, start = plans[level]
        if level == len(axes) - 1:
            pieces = [fetch(prefix + (o,)) for o in offsets]
        else:
            pieces = [assemble(level + 1, prefix + (o,)) for o in offsets]
        return jnp.concatenate(pieces, axis=dims[level])

    return assemble(0, ()), [start for offsets, start in plans]


def _prod(values):
    total = 1
    for v in values:
        total *= v
    return total


def _unravel(index, counts):
    coords = []
    for n in reversed(counts):
        coords.append(index % n)
        index //= n
    return list(reversed(coords))


def _ravel(coords, counts):
    index = 0
    for c, n in zip(coords, counts):
        index = index * n + c
    return index


def level_coeffs(level_id):
    coupling = 0.5 / 4.0**level_id
    return (6.0 * coupling + shift_sigma, coupling)


def pad_with(block, faces):
    padded = block
    for dim, (lo, hi) in enumerate(faces):
        widths = [(0, 0)] * block.ndim
        for other in range(dim):
            widths[other] = (1, 1)
        lo = jnp.pad(lo, widths)
        hi = jnp.pad(hi, widths)
        padded = jnp.concatenate([lo, padded, hi], axis=dim)
    return padded


def stencil(block, faces, level_id):
    return padded_stencil(pad_with(block, faces), level_id)


def padded_stencil(padded, level_id):
    center, coupling = level_coeffs(level_id)
    middle = padded[1:-1, 1:-1, 1:-1]
    beside = padded[2:, 1:-1, 1:-1] + padded[:-2, 1:-1, 1:-1]
    beside = beside + padded[1:-1, 2:, 1:-1] + padded[1:-1, :-2, 1:-1]
    beside = beside + padded[1:-1, 1:-1, 2:] + padded[1:-1, 1:-1, :-2]
    return center * middle - coupling * beside


def restrict(field):
    size_a, size_b, size_c = field.shape[:3]
    rest = field.shape[3:]
    return field.reshape((size_a // 2, 2, size_b // 2, 2, size_c // 2, 2) + rest).mean(axis=(1, 3, 5))


def prolong(field):
    return jnp.repeat(jnp.repeat(jnp.repeat(field, 2, 0), 2, 1), 2, 2)


def coarse_solve(rhs_two, tiles):
    extended = rhs_two
    starts = []
    extended, start, tiles_by_step = extend_axis(extended, "gx", 0, COARSE_HALO, tiles)
    starts.append(start)
    extended, joint_starts = extend_joint(extended, ("gy", "gz"), (1, 2), COARSE_HALO)
    starts.extend(joint_starts)
    grid = extended.shape[:3]
    orbs = extended.shape[3:]
    operator = coarse_matrix(grid, tuple(starts), rhs_two.shape[:3])
    operator = jnp.asarray(operator.reshape((-1,) + tuple(grid)))
    post = jnp.einsum(
        "qxyz,xyzgl->qgl", operator, extended, precision=lax.Precision.HIGHEST, preferred_element_type=jnp.float32
    )
    return post.reshape(tuple(2 * size + 2 for size in rhs_two.shape[:3]) + orbs), tiles_by_step


def coarse_matrix(grid, starts, block):
    cells = int(np.prod(grid))
    field = np.eye(cells).reshape(grid + (cells,))

    def apply(v, level_id):
        center, coupling = level_coeffs(level_id)
        beside = 0.0
        for dim in range(3):
            beside = beside + np.roll(v, -1, dim) + np.roll(v, 1, dim)
        return center * v - coupling * beside

    def shrink(v):
        a, b, c = v.shape[:3]
        return v.reshape(a // 2, 2, b // 2, 2, c // 2, 2, -1).mean(axis=(1, 3, 5))

    def grow(v):
        return np.repeat(np.repeat(np.repeat(v, 2, 0), 2, 1), 2, 2)

    level_two = LEVELS - 2
    center, coupling = level_coeffs(level_two)
    correct_two = omega * field / center
    current = shrink(field - apply(correct_two, level_two))
    top_level = LEVELS - 1
    center_top, coupling_top = level_coeffs(top_level)
    correct = omega * current / center_top
    for sweep_id in range(COARSE - 1):
        correct = correct + omega * (current - apply(correct, top_level)) / center_top
    updated = correct_two + grow(correct)
    post = updated + omega * (field - apply(updated, level_two)) / center
    padded = [2 * size + 2 for size in block]
    for dim in range(3):
        index = [(starts[dim] + (p - 1) // 2) % grid[dim] for p in range(padded[dim])]
        post = np.take(post, index, axis=dim)
    rim = np.zeros(padded, np.int32)
    for dim in range(3):
        edge = np.zeros(padded[dim], np.int32)
        edge[0] = edge[-1] = 1
        rim = rim + edge.reshape([-1 if d == dim else 1 for d in range(3)])
    post = post * (rim <= 1)[..., None]
    post = post.reshape(-1, cells)
    return post.astype(np.float32)


def prolong_face(face, dim):
    for other in range(3):
        if other != dim:
            face = jnp.repeat(face, 2, other)
    return face


def coarse_faces(halo_block, dim):
    inner = halo_block
    for other in range(3):
        if other != dim:
            inner = lax.slice_in_dim(inner, 1, inner.shape[other] - 1, axis=other)
    size = inner.shape[dim]
    lo = lax.slice_in_dim(inner, 0, 1, axis=dim)
    hi = lax.slice_in_dim(inner, size - 1, size, axis=dim)
    return lo, hi


def post_smooth(level_id, corr, corr_faces, rhs, coarse_inner, coarse_face_list):
    center, coupling = level_coeffs(level_id)
    updated = corr + prolong(coarse_inner)
    faces = []
    for dim in range(3):
        lo = corr_faces[dim][0] + prolong_face(coarse_face_list[dim][0], dim)
        hi = corr_faces[dim][1] + prolong_face(coarse_face_list[dim][1], dim)
        faces.append((lo, hi))
    return updated + omega * (rhs - stencil(updated, faces, level_id)) / center


def post_smooth_padded(level_id, corr_padded, rhs, coarse_inner, coarse_face_list):
    center, coupling = level_coeffs(level_id)
    faces = [(prolong_face(lo, dim), prolong_face(hi, dim)) for dim, (lo, hi) in enumerate(coarse_face_list)]
    updated_padded = corr_padded + pad_with(prolong(coarse_inner), faces)
    updated = updated_padded[1:-1, 1:-1, 1:-1]
    return updated + omega * (rhs - padded_stencil(updated_padded, level_id)) / center


def dim_mask(box_part, offset, extent):
    cells = offset + jnp.arange(extent, dtype=jnp.int32)[:, None]
    return ((box_part[0][None, :] <= cells) & (cells < box_part[1][None, :])).astype(jnp.float32)


def gram_matrix(tiles_by_step, inv_tiles, tile_pairs, orb_count):
    count = lax.axis_size("gx")
    local = inv_tiles.shape[0]
    tile_edge = inv_tiles.shape[1]
    blocks = orb_count // tile_edge
    me = lax.axis_index("gx")
    pieces = []
    ids = []
    for step in range(count):
        piece = tiles_by_step.get(step)
        if piece is None:
            piece = inv_tiles if step == 0 else shifted(inv_tiles, "gx", step)
        pieces.append(piece)
        ids.append(((me + step) % count) * local + jnp.arange(local, dtype=jnp.int32))
    tiles = jnp.concatenate(pieces, axis=0)
    pairs = jnp.take(tile_pairs, jnp.concatenate(ids), axis=0)
    block_ids = jnp.arange(blocks, dtype=jnp.int32)
    rows = (pairs[:, 0][:, None] == block_ids[None, :]).astype(jnp.float32)
    cols = (pairs[:, 1][:, None] == block_ids[None, :]).astype(jnp.float32)
    spread = rows[:, :, None, None, None] * cols[:, None, None, :, None] * tiles[:, None, :, None, :]
    return spread.sum(axis=0).reshape(orb_count, orb_count)


def vcycle(residuals, inv_tiles):
    center, coupling = level_coeffs(0)
    faces_zero = all_faces(residuals, lambda part: omega * part.astype(jnp.float32) / center)
    rhs_zero = residuals.astype(jnp.float32)
    corr_zero = omega * rhs_zero / center
    rhs_one = restrict(rhs_zero - stencil(corr_zero, faces_zero, 0))
    center, coupling = level_coeffs(1)
    corr_one = omega * rhs_one / center
    padded_one = pad_with(corr_one, all_faces(corr_one))
    rhs_two = restrict(rhs_one - padded_stencil(padded_one, 1))
    coarse_padded, tiles_by_step = coarse_solve(rhs_two, inv_tiles)
    center, coupling = level_coeffs(1)
    updated_padded = padded_one + coarse_padded
    updated = updated_padded[1:-1, 1:-1, 1:-1]
    post_one = updated + omega * (rhs_one - padded_stencil(updated_padded, 1)) / center
    return post_smooth(0, corr_zero, faces_zero, rhs_zero, post_one, all_faces(post_one)), tiles_by_step


def body(residuals, patch_box, tile_pairs, inv_tiles):
    size_a, size_b, size_c, orb_count = residuals.shape
    lanes = LANES if orb_count % LANES == 0 else orb_count
    grouped = residuals.reshape(size_a, size_b, size_c, orb_count // lanes, lanes)
    correct, tiles_by_step = vcycle(grouped, inv_tiles)
    correct = correct.reshape(size_a, size_b, size_c, orb_count)
    gram = gram_matrix(tiles_by_step, inv_tiles, tile_pairs, orb_count)
    mask_first = dim_mask(patch_box[0], lax.axis_index("gx") * size_a, size_a)
    mask_second = dim_mask(patch_box[1], lax.axis_index("gy") * size_b, size_b)
    mask_third = dim_mask(patch_box[2], lax.axis_index("gz") * size_c, size_c)
    precond = correct * (
        mask_first[:, None, None, :] * mask_second[None, :, None, :] * mask_third[None, None, :, :]
    )
    cell_count = size_a * size_b * size_c
    rows = lax.optimization_barrier(precond.reshape(cell_count, orb_count))
    mixed = jnp.dot(rows, gram, precision=lax.Precision.HIGH, preferred_element_type=jnp.float32)
    return mixed.reshape(size_a, size_b, size_c, orb_count).astype(jnp.bfloat16)


def solution(mesh):
    return jax.shard_map(
        body,
        mesh=mesh,
        in_specs=(P("gx", "gy", "gz", None), P(), P(), P("gx", None, None)),
        out_specs=P("gx", "gy", "gz", None),
        check_vma=False,
    )
```

```python
import jax
import jax.numpy as jnp
import numpy as np
from jax import lax
from jax.sharding import PartitionSpec as P

LEVELS = 4
COARSE = 4


omega = 0.8
shift_sigma = 0.01

GRID_AXES = (("gx", 0), ("gy", 1), ("gz", 2))
COARSE_HALO = 10
LANES = 128


def shifted(block, axis, offset):
    count = lax.axis_size(axis)
    step = offset % count
    if step == 0:
        return block
    return lax.ppermute(block, axis, [(j, (j - step) % count) for j in range(count)])


def axis_faces(block, axis, dim, prepare=None):
    count = lax.axis_size(axis)
    first = lax.slice_in_dim(block, 0, 1, axis=dim)
    last = lax.slice_in_dim(block, block.shape[dim] - 1, None, axis=dim)
    if prepare is not None:
        first = prepare(first)
        last = prepare(last)
    if count == 1:
        return last, first
    if count == 2:
        both = lax.ppermute(jnp.concatenate([first, last], axis=dim), axis, [(0, 1), (1, 0)])
        hi = lax.slice_in_dim(both, 0, 1, axis=dim)
        lo = lax.slice_in_dim(both, 1, 2, axis=dim)
        return lo, hi
    lo = shifted(last, axis, -1)
    hi = shifted(first, axis, 1)
    return lo, hi


def all_faces(block, prepare=None):
    return [axis_faces(block, axis, dim, prepare) for axis, dim in GRID_AXES]


def extend_axis(block, axis, dim, halo, extra=None):
    count = lax.axis_size(axis)
    size = block.shape[dim]
    reach = -(-halo // size)
    if 2 * reach + 1 >= count:
        offsets = list(range(count))
        start = 0
    else:
        offsets = list(range(-reach, reach + 1))
        start = reach * size
    cache = {}
    extras = {}
    pieces = []
    for offset in offsets:
        step = offset % count
        if step not in cache:
            if extra is None or step == 0:
                cache[step] = shifted(block, axis, step)
                extras[step] = extra
            else:
                trailing = block.shape[1:]
                if extra.size % int(np.prod(trailing)) == 0:
                    both = jnp.concatenate([block, extra.reshape((-1,) + trailing)], axis=0)
                    both = shifted(both, axis, step)
                    cache[step] = both[: block.shape[0]]
                    extras[step] = both[block.shape[0] :].reshape(extra.shape)
                else:
                    both = jnp.concatenate([block.reshape(-1), extra.reshape(-1)])
                    both = shifted(both, axis, step)
                    cache[step] = both[: block.size].reshape(block.shape)
                    extras[step] = both[block.size :].reshape(extra.shape)
        pieces.append(cache[step])
    return jnp.concatenate(pieces, axis=dim), start, extras


def axis_offsets(count, size, halo):
    reach = -(-halo // size)
    if 2 * reach + 1 >= count:
        return list(range(count)), 0
    return list(range(-reach, reach + 1)), reach * size


def extend_joint(block, axes, dims, halo):
    counts = [lax.axis_size(axis) for axis in axes]
    plans = [axis_offsets(count, block.shape[dim], halo) for count, dim in zip(counts, dims)]
    cache = {}

    def fetch(offset):
        steps = tuple(o % c for o, c in zip(offset, counts))
        if steps not in cache:
            if not any(steps):
                cache[steps] = block
            else:
                pairs = []
                for target in range(_prod(counts)):
                    coords = _unravel(target, counts)
                    source = _ravel([(c + s) % n for c, s, n in zip(coords, steps, counts)], counts)
                    pairs.append((source, target))
                cache[steps] = lax.ppermute(block, tuple(axes), pairs)
        return cache[steps]

    def assemble(level, prefix):
        offsets, start = plans[level]
        if level == len(axes) - 1:
            pieces = [fetch(prefix + (o,)) for o in offsets]
        else:
            pieces = [assemble(level + 1, prefix + (o,)) for o in offsets]
        return jnp.concatenate(pieces, axis=dims[level])

    return assemble(0, ()), [start for offsets, start in plans]


def _prod(values):
    total = 1
    for v in values:
        total *= v
    return total


def _unravel(index, counts):
    coords = []
    for n in reversed(counts):
        coords.append(index % n)
        index //= n
    return list(reversed(coords))


def _ravel(coords, counts):
    index = 0
    for c, n in zip(coords, counts):
        index = index * n + c
    return index


def level_coeffs(level_id):
    coupling = 0.5 / 4.0**level_id
    return (6.0 * coupling + shift_sigma, coupling)


def pad_with(block, faces):
    padded = block
    for dim, (lo, hi) in enumerate(faces):
        widths = [(0, 0)] * block.ndim
        for other in range(dim):
            widths[other] = (1, 1)
        lo = jnp.pad(lo, widths)
        hi = jnp.pad(hi, widths)
        padded = jnp.concatenate([lo, padded, hi], axis=dim)
    return padded


def stencil(block, faces, level_id):
    return padded_stencil(pad_with(block, faces), level_id)


def padded_stencil(padded, level_id):
    center, coupling = level_coeffs(level_id)
    middle = padded[1:-1, 1:-1, 1:-1]
    beside = padded[2:, 1:-1, 1:-1] + padded[:-2, 1:-1, 1:-1]
    beside = beside + padded[1:-1, 2:, 1:-1] + padded[1:-1, :-2, 1:-1]
    beside = beside + padded[1:-1, 1:-1, 2:] + padded[1:-1, 1:-1, :-2]
    return center * middle - coupling * beside


def restrict(field):
    size_a, size_b, size_c = field.shape[:3]
    rest = field.shape[3:]
    return field.reshape((size_a // 2, 2, size_b // 2, 2, size_c // 2, 2) + rest).mean(axis=(1, 3, 5))


def prolong(field):
    return jnp.repeat(jnp.repeat(jnp.repeat(field, 2, 0), 2, 1), 2, 2)


def coarse_solve(rhs_two, tiles):
    block = rhs_two.shape[:3]
    orbs = rhs_two.shape[3:]
    width = int(np.prod(orbs))
    rows = rhs_two.reshape(-1, width)
    tile_rows = tiles.reshape(-1, width)
    count_x = lax.axis_size("gx")
    offsets_x, start_x = axis_offsets(count_x, block[0], COARSE_HALO)
    cache = {}
    tiles_by_step = {0: tile_rows}
    for offset in offsets_x:
        step = offset % count_x
        if step in cache:
            continue
        if step == 0:
            cache[step] = rows
            continue
        both = shifted(jnp.concatenate([rows, tile_rows], axis=0), "gx", step)
        cache[step] = both[: rows.shape[0]]
        tiles_by_step[step] = both[rows.shape[0] :]
    line = jnp.concatenate([cache[offset % count_x] for offset in offsets_x], axis=0)
    axes = ("gy", "gz")
    counts = [lax.axis_size(axis) for axis in axes]
    plans = [axis_offsets(count, block[dim], COARSE_HALO) for count, dim in zip(counts, (1, 2))]
    moved = {}
    pieces = []
    for offset_y in plans[0][0]:
        for offset_z in plans[1][0]:
            steps = (offset_y % counts[0], offset_z % counts[1])
            if steps not in moved:
                if steps == (0, 0):
                    moved[steps] = line
                else:
                    pairs = []
                    for target in range(counts[0] * counts[1]):
                        ty, tz = divmod(target, counts[1])
                        source = ((ty + steps[0]) % counts[0]) * counts[1] + (tz + steps[1]) % counts[1]
                        pairs.append((source, target))
                    moved[steps] = lax.ppermute(line, axes, pairs)
            pieces.append(moved[steps])
    gathered = jnp.concatenate(pieces, axis=0)
    operator = coarse_matrix(
        block, (offsets_x, plans[0][0], plans[1][0]), (start_x, plans[0][1], plans[1][1])
    )
    post = jnp.dot(
        jnp.asarray(operator), gathered, precision=lax.Precision.HIGHEST, preferred_element_type=jnp.float32
    )
    return post.reshape(tuple(2 * size + 2 for size in block) + orbs), tiles_by_step


def coarse_matrix(block, offsets, starts):
    grid = tuple(len(offs) * size for offs, size in zip(offsets, block))
    cells = int(np.prod(grid))
    field = np.eye(cells).reshape(grid + (cells,))

    def apply(v, level_id):
        center, coupling = level_coeffs(level_id)
        beside = 0.0
        for dim in range(3):
            beside = beside + np.roll(v, -1, dim) + np.roll(v, 1, dim)
        return center * v - coupling * beside

    def shrink(v):
        a, b, c = v.shape[:3]
        return v.reshape(a // 2, 2, b // 2, 2, c // 2, 2, -1).mean(axis=(1, 3, 5))

    def grow(v):
        return np.repeat(np.repeat(np.repeat(v, 2, 0), 2, 1), 2, 2)

    level_two = LEVELS - 2
    center, coupling = level_coeffs(level_two)
    correct_two = omega * field / center
    current = shrink(field - apply(correct_two, level_two))
    top_level = LEVELS - 1
    center_top, coupling_top = level_coeffs(top_level)
    correct = omega * current / center_top
    for sweep_id in range(COARSE - 1):
        correct = correct + omega * (current - apply(correct, top_level)) / center_top
    updated = correct_two + grow(correct)
    post = updated + omega * (field - apply(updated, level_two)) / center
    padded = [2 * size + 2 for size in block]
    for dim in range(3):
        index = [(starts[dim] + (p - 1) // 2) % grid[dim] for p in range(padded[dim])]
        post = np.take(post, index, axis=dim)
    rim = np.zeros(padded, np.int32)
    for dim in range(3):
        edge = np.zeros(padded[dim], np.int32)
        edge[0] = edge[-1] = 1
        rim = rim + edge.reshape([-1 if d == dim else 1 for d in range(3)])
    post = post * (rim <= 1)[..., None]
    order = []
    for iy in range(len(offsets[1])):
        for iz in range(len(offsets[2])):
            for ix in range(len(offsets[0])):
                for lx in range(block[0]):
                    for ly in range(block[1]):
                        for lz in range(block[2]):
                            x = ix * block[0] + lx
                            y = iy * block[1] + ly
                            z = iz * block[2] + lz
                            order.append((x * grid[1] + y) * grid[2] + z)
    post = post.reshape(-1, cells)[:, np.array(order)]
    return post.astype(np.float32)


def prolong_face(face, dim):
    for other in range(3):
        if other != dim:
            face = jnp.repeat(face, 2, other)
    return face


def coarse_faces(halo_block, dim):
    inner = halo_block
    for other in range(3):
        if other != dim:
            inner = lax.slice_in_dim(inner, 1, inner.shape[other] - 1, axis=other)
    size = inner.shape[dim]
    lo = lax.slice_in_dim(inner, 0, 1, axis=dim)
    hi = lax.slice_in_dim(inner, size - 1, size, axis=dim)
    return lo, hi


def post_smooth(level_id, corr, corr_faces, rhs, coarse_inner, coarse_face_list):
    center, coupling = level_coeffs(level_id)
    updated = corr + prolong(coarse_inner)
    faces = []
    for dim in range(3):
        lo = corr_faces[dim][0] + prolong_face(coarse_face_list[dim][0], dim)
        hi = corr_faces[dim][1] + prolong_face(coarse_face_list[dim][1], dim)
        faces.append((lo, hi))
    return updated + omega * (rhs - stencil(updated, faces, level_id)) / center


def post_smooth_padded(level_id, corr_padded, rhs, coarse_inner, coarse_face_list):
    center, coupling = level_coeffs(level_id)
    faces = [(prolong_face(lo, dim), prolong_face(hi, dim)) for dim, (lo, hi) in enumerate(coarse_face_list)]
    updated_padded = corr_padded + pad_with(prolong(coarse_inner), faces)
    updated = updated_padded[1:-1, 1:-1, 1:-1]
    return updated + omega * (rhs - padded_stencil(updated_padded, level_id)) / center


def dim_mask(box_part, offset, extent):
    cells = offset + jnp.arange(extent, dtype=jnp.int32)[:, None]
    return ((box_part[0][None, :] <= cells) & (cells < box_part[1][None, :])).astype(jnp.float32)


def gram_matrix(tiles_by_step, inv_tiles, tile_pairs, orb_count):
    count = lax.axis_size("gx")
    local = inv_tiles.shape[0]
    tile_edge = inv_tiles.shape[1]
    blocks = orb_count // tile_edge
    me = lax.axis_index("gx")
    pieces = []
    ids = []
    for step in range(count):
        piece = tiles_by_step.get(step)
        if piece is None:
            piece = shifted(inv_tiles, "gx", step)
        split = orb_count // tile_edge
        pieces.append(piece.reshape(local, tile_edge // split, split, tile_edge))
        ids.append(((me + step) % count) * local + jnp.arange(local, dtype=jnp.int32))
    tiles = jnp.concatenate(pieces, axis=0)
    pairs = jnp.take(tile_pairs, jnp.concatenate(ids), axis=0)
    block_ids = jnp.arange(blocks, dtype=jnp.int32)
    rows = (pairs[:, 0][:, None] == block_ids[None, :]).astype(jnp.float32)
    cols = (pairs[:, 1][:, None] == block_ids[None, :]).astype(jnp.float32)
    spread = (
        rows[:, :, None, None, None, None]
        * cols[:, None, None, None, :, None]
        * tiles[:, None, :, :, None, :]
    )
    return spread.sum(axis=0).reshape(orb_count, orb_count)


def vcycle(residuals, inv_tiles):
    center, coupling = level_coeffs(0)
    faces_zero = all_faces(residuals, lambda part: omega * part.astype(jnp.float32) / center)
    rhs_zero = residuals.astype(jnp.float32)
    corr_zero = omega * rhs_zero / center
    rhs_one = restrict(rhs_zero - stencil(corr_zero, faces_zero, 0))
    center, coupling = level_coeffs(1)
    corr_one = omega * rhs_one / center
    padded_one = pad_with(corr_one, all_faces(corr_one))
    rhs_two = restrict(rhs_one - padded_stencil(padded_one, 1))
    coarse_padded, tiles_by_step = coarse_solve(rhs_two, inv_tiles)
    center, coupling = level_coeffs(1)
    updated_padded = padded_one + coarse_padded
    updated = updated_padded[1:-1, 1:-1, 1:-1]
    post_one = updated + omega * (rhs_one - padded_stencil(updated_padded, 1)) / center
    return post_smooth(0, corr_zero, faces_zero, rhs_zero, post_one, all_faces(post_one)), tiles_by_step


def body(residuals, patch_box, tile_pairs, inv_tiles):
    size_a, size_b, size_c, orb_count = residuals.shape
    lanes = LANES if orb_count % LANES == 0 else orb_count
    grouped = residuals.reshape(size_a, size_b, size_c, orb_count // lanes, lanes)
    correct, tiles_by_step = vcycle(grouped, inv_tiles)
    correct = correct.reshape(size_a, size_b, size_c, orb_count)
    gram = gram_matrix(tiles_by_step, inv_tiles, tile_pairs, orb_count)
    mask_first = dim_mask(patch_box[0], lax.axis_index("gx") * size_a, size_a)
    mask_second = dim_mask(patch_box[1], lax.axis_index("gy") * size_b, size_b)
    mask_third = dim_mask(patch_box[2], lax.axis_index("gz") * size_c, size_c)
    precond = correct * (
        mask_first[:, None, None, :] * mask_second[None, :, None, :] * mask_third[None, None, :, :]
    )
    cell_count = size_a * size_b * size_c
    rows = lax.optimization_barrier(precond.reshape(cell_count, orb_count))
    mixed = jnp.dot(rows, gram, precision=lax.Precision.HIGH, preferred_element_type=jnp.float32)
    return mixed.reshape(size_a, size_b, size_c, orb_count).astype(jnp.bfloat16)


def solution(mesh):
    return jax.shard_map(
        body,
        mesh=mesh,
        in_specs=(P("gx", "gy", "gz", None), P(), P(), P("gx", None, None)),
        out_specs=P("gx", "gy", "gz", None),
        check_vma=False,
    )
```

```python
import jax
import jax.numpy as jnp
import numpy as np
from jax import lax
from jax.sharding import PartitionSpec as P

LEVELS = 4
COARSE = 4


omega = 0.8
shift_sigma = 0.01

GRID_AXES = (("gx", 0), ("gy", 1), ("gz", 2))
COARSE_HALO = 10
LANES = 128


def shifted(block, axis, offset):
    count = lax.axis_size(axis)
    step = offset % count
    if step == 0:
        return block
    return lax.ppermute(block, axis, [(j, (j - step) % count) for j in range(count)])


def axis_faces(block, axis, dim, prepare=None):
    count = lax.axis_size(axis)
    first = lax.slice_in_dim(block, 0, 1, axis=dim)
    last = lax.slice_in_dim(block, block.shape[dim] - 1, None, axis=dim)
    if prepare is not None:
        first = prepare(first)
        last = prepare(last)
    if count == 1:
        return last, first
    if count == 2:
        both = lax.ppermute(jnp.concatenate([first, last], axis=dim), axis, [(0, 1), (1, 0)])
        hi = lax.slice_in_dim(both, 0, 1, axis=dim)
        lo = lax.slice_in_dim(both, 1, 2, axis=dim)
        return lo, hi
    lo = shifted(last, axis, -1)
    hi = shifted(first, axis, 1)
    return lo, hi


def all_faces(block, prepare=None):
    return [axis_faces(block, axis, dim, prepare) for axis, dim in GRID_AXES]


def extend_axis(block, axis, dim, halo, extra=None):
    count = lax.axis_size(axis)
    size = block.shape[dim]
    reach = -(-halo // size)
    if 2 * reach + 1 >= count:
        offsets = list(range(count))
        start = 0
    else:
        offsets = list(range(-reach, reach + 1))
        start = reach * size
    cache = {}
    extras = {}
    pieces = []
    for offset in offsets:
        step = offset % count
        if step not in cache:
            if extra is None or step == 0:
                cache[step] = shifted(block, axis, step)
                extras[step] = extra
            else:
                trailing = block.shape[1:]
                if extra.size % int(np.prod(trailing)) == 0:
                    both = jnp.concatenate([block, extra.reshape((-1,) + trailing)], axis=0)
                    both = shifted(both, axis, step)
                    cache[step] = both[: block.shape[0]]
                    extras[step] = both[block.shape[0] :].reshape(extra.shape)
                else:
                    both = jnp.concatenate([block.reshape(-1), extra.reshape(-1)])
                    both = shifted(both, axis, step)
                    cache[step] = both[: block.size].reshape(block.shape)
                    extras[step] = both[block.size :].reshape(extra.shape)
        pieces.append(cache[step])
    return jnp.concatenate(pieces, axis=dim), start, extras


def axis_offsets(count, size, halo):
    reach = -(-halo // size)
    if 2 * reach + 1 >= count:
        return list(range(count)), 0
    return list(range(-reach, reach + 1)), reach * size


def extend_joint(block, axes, dims, halo):
    counts = [lax.axis_size(axis) for axis in axes]
    plans = [axis_offsets(count, block.shape[dim], halo) for count, dim in zip(counts, dims)]
    cache = {}

    def fetch(offset):
        steps = tuple(o % c for o, c in zip(offset, counts))
        if steps not in cache:
            if not any(steps):
                cache[steps] = block
            else:
                pairs = []
                for target in range(_prod(counts)):
                    coords = _unravel(target, counts)
                    source = _ravel([(c + s) % n for c, s, n in zip(coords, steps, counts)], counts)
                    pairs.append((source, target))
                cache[steps] = lax.ppermute(block, tuple(axes), pairs)
        return cache[steps]

    def assemble(level, prefix):
        offsets, start = plans[level]
        if level == len(axes) - 1:
            pieces = [fetch(prefix + (o,)) for o in offsets]
        else:
            pieces = [assemble(level + 1, prefix + (o,)) for o in offsets]
        return jnp.concatenate(pieces, axis=dims[level])

    return assemble(0, ()), [start for offsets, start in plans]


def _prod(values):
    total = 1
    for v in values:
        total *= v
    return total


def _unravel(index, counts):
    coords = []
    for n in reversed(counts):
        coords.append(index % n)
        index //= n
    return list(reversed(coords))


def _ravel(coords, counts):
    index = 0
    for c, n in zip(coords, counts):
        index = index * n + c
    return index


def level_coeffs(level_id):
    coupling = 0.5 / 4.0**level_id
    return (6.0 * coupling + shift_sigma, coupling)


def pad_with(block, faces):
    padded = block
    for dim, (lo, hi) in enumerate(faces):
        widths = [(0, 0)] * block.ndim
        for other in range(dim):
            widths[other] = (1, 1)
        lo = jnp.pad(lo, widths)
        hi = jnp.pad(hi, widths)
        padded = jnp.concatenate([lo, padded, hi], axis=dim)
    return padded


def stencil(block, faces, level_id):
    return padded_stencil(pad_with(block, faces), level_id)


def padded_stencil(padded, level_id):
    center, coupling = level_coeffs(level_id)
    middle = padded[1:-1, 1:-1, 1:-1]
    beside = padded[2:, 1:-1, 1:-1] + padded[:-2, 1:-1, 1:-1]
    beside = beside + padded[1:-1, 2:, 1:-1] + padded[1:-1, :-2, 1:-1]
    beside = beside + padded[1:-1, 1:-1, 2:] + padded[1:-1, 1:-1, :-2]
    return center * middle - coupling * beside


def restrict(field):
    size_a, size_b, size_c = field.shape[:3]
    rest = field.shape[3:]
    return field.reshape((size_a // 2, 2, size_b // 2, 2, size_c // 2, 2) + rest).mean(axis=(1, 3, 5))


def prolong(field):
    return jnp.repeat(jnp.repeat(jnp.repeat(field, 2, 0), 2, 1), 2, 2)


def coarse_solve(rhs_two, tiles):
    block = rhs_two.shape[:3]
    orbs = rhs_two.shape[3:]
    rows = rhs_two.reshape((-1,) + orbs)
    tile_rows = tiles.reshape((-1,) + orbs)
    count_x = lax.axis_size("gx")
    offsets_x, start_x = axis_offsets(count_x, block[0], COARSE_HALO)
    cache = {}
    tiles_by_step = {0: tile_rows}
    for offset in offsets_x:
        step = offset % count_x
        if step in cache:
            continue
        if step == 0:
            cache[step] = rows
            continue
        both = shifted(jnp.concatenate([rows, tile_rows], axis=0), "gx", step)
        cache[step] = both[: rows.shape[0]]
        tiles_by_step[step] = both[rows.shape[0] :]
    line = jnp.concatenate([cache[offset % count_x] for offset in offsets_x], axis=0)
    axes = ("gy", "gz")
    counts = [lax.axis_size(axis) for axis in axes]
    plans = [axis_offsets(count, block[dim], COARSE_HALO) for count, dim in zip(counts, (1, 2))]
    moved = {}
    pieces = []
    for offset_y in plans[0][0]:
        for offset_z in plans[1][0]:
            steps = (offset_y % counts[0], offset_z % counts[1])
            if steps not in moved:
                if steps == (0, 0):
                    moved[steps] = line
                else:
                    pairs = []
                    for target in range(counts[0] * counts[1]):
                        ty, tz = divmod(target, counts[1])
                        source = ((ty + steps[0]) % counts[0]) * counts[1] + (tz + steps[1]) % counts[1]
                        pairs.append((source, target))
                    moved[steps] = lax.ppermute(line, axes, pairs)
            pieces.append(moved[steps])
    gathered = lax.optimization_barrier(jnp.concatenate(pieces, axis=0))
    operator = coarse_matrix(
        block, (offsets_x, plans[0][0], plans[1][0]), (start_x, plans[0][1], plans[1][1])
    )
    post = jnp.einsum(
        "qe,e...->q...", jnp.asarray(operator), gathered, precision=lax.Precision.HIGHEST,
        preferred_element_type=jnp.float32,
    )
    return post.reshape(tuple(2 * size + 2 for size in block) + orbs), tiles_by_step


def coarse_matrix(block, offsets, starts):
    grid = tuple(len(offs) * size for offs, size in zip(offsets, block))
    cells = int(np.prod(grid))
    field = np.eye(cells).reshape(grid + (cells,))

    def apply(v, level_id):
        center, coupling = level_coeffs(level_id)
        beside = 0.0
        for dim in range(3):
            beside = beside + np.roll(v, -1, dim) + np.roll(v, 1, dim)
        return center * v - coupling * beside

    def shrink(v):
        a, b, c = v.shape[:3]
        return v.reshape(a // 2, 2, b // 2, 2, c // 2, 2, -1).mean(axis=(1, 3, 5))

    def grow(v):
        return np.repeat(np.repeat(np.repeat(v, 2, 0), 2, 1), 2, 2)

    level_two = LEVELS - 2
    center, coupling = level_coeffs(level_two)
    correct_two = omega * field / center
    current = shrink(field - apply(correct_two, level_two))
    top_level = LEVELS - 1
    center_top, coupling_top = level_coeffs(top_level)
    correct = omega * current / center_top
    for sweep_id in range(COARSE - 1):
        correct = correct + omega * (current - apply(correct, top_level)) / center_top
    updated = correct_two + grow(correct)
    post = updated + omega * (field - apply(updated, level_two)) / center
    padded = [2 * size + 2 for size in block]
    for dim in range(3):
        index = [(starts[dim] + (p - 1) // 2) % grid[dim] for p in range(padded[dim])]
        post = np.take(post, index, axis=dim)
    rim = np.zeros(padded, np.int32)
    for dim in range(3):
        edge = np.zeros(padded[dim], np.int32)
        edge[0] = edge[-1] = 1
        rim = rim + edge.reshape([-1 if d == dim else 1 for d in range(3)])
    post = post * (rim <= 1)[..., None]
    order = []
    for iy in range(len(offsets[1])):
        for iz in range(len(offsets[2])):
            for ix in range(len(offsets[0])):
                for lx in range(block[0]):
                    for ly in range(block[1]):
                        for lz in range(block[2]):
                            x = ix * block[0] + lx
                            y = iy * block[1] + ly
                            z = iz * block[2] + lz
                            order.append((x * grid[1] + y) * grid[2] + z)
    post = post.reshape(-1, cells)[:, np.array(order)]
    return post.astype(np.float32)


def prolong_face(face, dim):
    for other in range(3):
        if other != dim:
            face = jnp.repeat(face, 2, other)
    return face


def coarse_faces(halo_block, dim):
    inner = halo_block
    for other in range(3):
        if other != dim:
            inner = lax.slice_in_dim(inner, 1, inner.shape[other] - 1, axis=other)
    size = inner.shape[dim]
    lo = lax.slice_in_dim(inner, 0, 1, axis=dim)
    hi = lax.slice_in_dim(inner, size - 1, size, axis=dim)
    return lo, hi


def post_smooth(level_id, corr, corr_faces, rhs, coarse_inner, coarse_face_list):
    center, coupling = level_coeffs(level_id)
    updated = corr + prolong(coarse_inner)
    faces = []
    for dim in range(3):
        lo = corr_faces[dim][0] + prolong_face(coarse_face_list[dim][0], dim)
        hi = corr_faces[dim][1] + prolong_face(coarse_face_list[dim][1], dim)
        faces.append((lo, hi))
    return updated + omega * (rhs - stencil(updated, faces, level_id)) / center


def post_smooth_padded(level_id, corr_padded, rhs, coarse_inner, coarse_face_list):
    center, coupling = level_coeffs(level_id)
    faces = [(prolong_face(lo, dim), prolong_face(hi, dim)) for dim, (lo, hi) in enumerate(coarse_face_list)]
    updated_padded = corr_padded + pad_with(prolong(coarse_inner), faces)
    updated = updated_padded[1:-1, 1:-1, 1:-1]
    return updated + omega * (rhs - padded_stencil(updated_padded, level_id)) / center


def dim_mask(box_part, offset, extent):
    cells = offset + jnp.arange(extent, dtype=jnp.int32)[:, None]
    return ((box_part[0][None, :] <= cells) & (cells < box_part[1][None, :])).astype(jnp.float32)


def gram_matrix(tiles_by_step, inv_tiles, tile_pairs, orb_count):
    count = lax.axis_size("gx")
    local = inv_tiles.shape[0]
    tile_edge = inv_tiles.shape[1]
    blocks = orb_count // tile_edge
    me = lax.axis_index("gx")
    pieces = []
    ids = []
    for step in range(count):
        piece = tiles_by_step.get(step)
        if piece is None:
            piece = shifted(inv_tiles, "gx", step)
        split = orb_count // tile_edge
        pieces.append(piece.reshape(local, tile_edge // split, split, tile_edge))
        ids.append(((me + step) % count) * local + jnp.arange(local, dtype=jnp.int32))
    tiles = jnp.concatenate(pieces, axis=0)
    pairs = jnp.take(tile_pairs, jnp.concatenate(ids), axis=0)
    block_ids = jnp.arange(blocks, dtype=jnp.int32)
    rows = (pairs[:, 0][:, None] == block_ids[None, :]).astype(jnp.float32)
    cols = (pairs[:, 1][:, None] == block_ids[None, :]).astype(jnp.float32)
    spread = (
        rows[:, :, None, None, None, None]
        * cols[:, None, None, None, :, None]
        * tiles[:, None, :, :, None, :]
    )
    return spread.sum(axis=0).reshape(orb_count, orb_count)


def vcycle(residuals, inv_tiles):
    center, coupling = level_coeffs(0)
    faces_zero = all_faces(residuals, lambda part: omega * part.astype(jnp.float32) / center)
    rhs_zero = residuals.astype(jnp.float32)
    corr_zero = omega * rhs_zero / center
    rhs_one = restrict(rhs_zero - stencil(corr_zero, faces_zero, 0))
    center, coupling = level_coeffs(1)
    corr_one = omega * rhs_one / center
    padded_one = pad_with(corr_one, all_faces(corr_one))
    rhs_two = restrict(rhs_one - padded_stencil(padded_one, 1))
    coarse_padded, tiles_by_step = coarse_solve(rhs_two, inv_tiles)
    center, coupling = level_coeffs(1)
    updated_padded = padded_one + coarse_padded
    updated = updated_padded[1:-1, 1:-1, 1:-1]
    post_one = updated + omega * (rhs_one - padded_stencil(updated_padded, 1)) / center
    return post_smooth(0, corr_zero, faces_zero, rhs_zero, post_one, all_faces(post_one)), tiles_by_step


def body(residuals, patch_box, tile_pairs, inv_tiles):
    size_a, size_b, size_c, orb_count = residuals.shape
    lanes = LANES if orb_count % LANES == 0 else orb_count
    grouped = residuals.reshape(size_a, size_b, size_c, orb_count // lanes, lanes)
    correct, tiles_by_step = vcycle(grouped, inv_tiles)
    correct = correct.reshape(size_a, size_b, size_c, orb_count)
    gram = gram_matrix(tiles_by_step, inv_tiles, tile_pairs, orb_count)
    mask_first = dim_mask(patch_box[0], lax.axis_index("gx") * size_a, size_a)
    mask_second = dim_mask(patch_box[1], lax.axis_index("gy") * size_b, size_b)
    mask_third = dim_mask(patch_box[2], lax.axis_index("gz") * size_c, size_c)
    precond = correct * (
        mask_first[:, None, None, :] * mask_second[None, :, None, :] * mask_third[None, None, :, :]
    )
    cell_count = size_a * size_b * size_c
    rows = lax.optimization_barrier(precond.reshape(cell_count, orb_count))
    mixed = jnp.dot(rows, gram, precision=lax.Precision.HIGH, preferred_element_type=jnp.float32)
    return mixed.reshape(size_a, size_b, size_c, orb_count).astype(jnp.bfloat16)


def solution(mesh):
    return jax.shard_map(
        body,
        mesh=mesh,
        in_specs=(P("gx", "gy", "gz", None), P(), P(), P("gx", None, None)),
        out_specs=P("gx", "gy", "gz", None),
        check_vma=False,
    )
```

```python
import jax
import jax.numpy as jnp
import numpy as np
from jax import lax
from jax.sharding import PartitionSpec as P

LEVELS = 4
COARSE = 4


omega = 0.8
shift_sigma = 0.01

GRID_AXES = (("gx", 0), ("gy", 1), ("gz", 2))
COARSE_HALO = 10
LANES = 128


def shifted(block, axis, offset):
    count = lax.axis_size(axis)
    step = offset % count
    if step == 0:
        return block
    return lax.ppermute(block, axis, [(j, (j - step) % count) for j in range(count)])


def axis_faces(block, axis, dim, prepare=None):
    count = lax.axis_size(axis)
    first = lax.slice_in_dim(block, 0, 1, axis=dim)
    last = lax.slice_in_dim(block, block.shape[dim] - 1, None, axis=dim)
    if prepare is not None:
        first = prepare(first)
        last = prepare(last)
    if count == 1:
        return last, first
    if count == 2:
        both = lax.ppermute(jnp.concatenate([first, last], axis=dim), axis, [(0, 1), (1, 0)])
        hi = lax.slice_in_dim(both, 0, 1, axis=dim)
        lo = lax.slice_in_dim(both, 1, 2, axis=dim)
        return lo, hi
    lo = shifted(last, axis, -1)
    hi = shifted(first, axis, 1)
    return lo, hi


def all_faces(block, prepare=None):
    return [axis_faces(block, axis, dim, prepare) for axis, dim in GRID_AXES]


def extend_axis(block, axis, dim, halo, extra=None):
    count = lax.axis_size(axis)
    size = block.shape[dim]
    reach = -(-halo // size)
    if 2 * reach + 1 >= count:
        offsets = list(range(count))
        start = 0
    else:
        offsets = list(range(-reach, reach + 1))
        start = reach * size
    cache = {}
    extras = {}
    pieces = []
    for offset in offsets:
        step = offset % count
        if step not in cache:
            if extra is None or step == 0:
                cache[step] = shifted(block, axis, step)
                extras[step] = extra
            else:
                trailing = block.shape[1:]
                if extra.size % int(np.prod(trailing)) == 0:
                    both = jnp.concatenate([block, extra.reshape((-1,) + trailing)], axis=0)
                    both = shifted(both, axis, step)
                    cache[step] = both[: block.shape[0]]
                    extras[step] = both[block.shape[0] :].reshape(extra.shape)
                else:
                    both = jnp.concatenate([block.reshape(-1), extra.reshape(-1)])
                    both = shifted(both, axis, step)
                    cache[step] = both[: block.size].reshape(block.shape)
                    extras[step] = both[block.size :].reshape(extra.shape)
        pieces.append(cache[step])
    return jnp.concatenate(pieces, axis=dim), start, extras


def axis_offsets(count, size, halo):
    reach = -(-halo // size)
    if 2 * reach + 1 >= count:
        return list(range(count)), 0
    return list(range(-reach, reach + 1)), reach * size


def extend_joint(block, axes, dims, halo):
    counts = [lax.axis_size(axis) for axis in axes]
    plans = [axis_offsets(count, block.shape[dim], halo) for count, dim in zip(counts, dims)]
    cache = {}

    def fetch(offset):
        steps = tuple(o % c for o, c in zip(offset, counts))
        if steps not in cache:
            if not any(steps):
                cache[steps] = block
            else:
                pairs = []
                for target in range(_prod(counts)):
                    coords = _unravel(target, counts)
                    source = _ravel([(c + s) % n for c, s, n in zip(coords, steps, counts)], counts)
                    pairs.append((source, target))
                cache[steps] = lax.ppermute(block, tuple(axes), pairs)
        return cache[steps]

    def assemble(level, prefix):
        offsets, start = plans[level]
        if level == len(axes) - 1:
            pieces = [fetch(prefix + (o,)) for o in offsets]
        else:
            pieces = [assemble(level + 1, prefix + (o,)) for o in offsets]
        return jnp.concatenate(pieces, axis=dims[level])

    return assemble(0, ()), [start for offsets, start in plans]


def _prod(values):
    total = 1
    for v in values:
        total *= v
    return total


def _unravel(index, counts):
    coords = []
    for n in reversed(counts):
        coords.append(index % n)
        index //= n
    return list(reversed(coords))


def _ravel(coords, counts):
    index = 0
    for c, n in zip(coords, counts):
        index = index * n + c
    return index


def level_coeffs(level_id):
    coupling = 0.5 / 4.0**level_id
    return (6.0 * coupling + shift_sigma, coupling)


def pad_with(block, faces):
    padded = block
    for dim, (lo, hi) in enumerate(faces):
        widths = [(0, 0)] * block.ndim
        for other in range(dim):
            widths[other] = (1, 1)
        lo = jnp.pad(lo, widths)
        hi = jnp.pad(hi, widths)
        padded = jnp.concatenate([lo, padded, hi], axis=dim)
    return padded


def stencil(block, faces, level_id):
    return padded_stencil(pad_with(block, faces), level_id)


def padded_stencil(padded, level_id):
    center, coupling = level_coeffs(level_id)
    middle = padded[1:-1, 1:-1, 1:-1]
    beside = padded[2:, 1:-1, 1:-1] + padded[:-2, 1:-1, 1:-1]
    beside = beside + padded[1:-1, 2:, 1:-1] + padded[1:-1, :-2, 1:-1]
    beside = beside + padded[1:-1, 1:-1, 2:] + padded[1:-1, 1:-1, :-2]
    return center * middle - coupling * beside


def restrict(field):
    size_a, size_b, size_c = field.shape[:3]
    rest = field.shape[3:]
    return field.reshape((size_a // 2, 2, size_b // 2, 2, size_c // 2, 2) + rest).mean(axis=(1, 3, 5))


def prolong(field):
    return jnp.repeat(jnp.repeat(jnp.repeat(field, 2, 0), 2, 1), 2, 2)


def coarse_solve(rhs_two, tiles):
    orbs = rhs_two.shape[3:]
    extended = rhs_two.reshape(rhs_two.shape[:3] + (-1,))
    starts = []
    extended, start, tiles_by_step = extend_axis(extended, "gx", 0, COARSE_HALO, tiles)
    starts.append(start)
    extended, joint_starts = extend_joint(extended, ("gy", "gz"), (1, 2), COARSE_HALO)
    starts.extend(joint_starts)
    grid = extended.shape[:3]
    operator = coarse_matrix(grid, tuple(starts), rhs_two.shape[:3])
    operator = jnp.asarray(operator.reshape((-1,) + tuple(grid)))
    post = jnp.einsum(
        "qxyz,xyzw->qw", operator, extended, precision=lax.Precision.HIGHEST, preferred_element_type=jnp.float32
    )
    return post.reshape(tuple(2 * size + 2 for size in rhs_two.shape[:3]) + orbs), tiles_by_step


def coarse_matrix(grid, starts, block):
    cells = int(np.prod(grid))
    field = np.eye(cells).reshape(grid + (cells,))

    def apply(v, level_id):
        center, coupling = level_coeffs(level_id)
        beside = 0.0
        for dim in range(3):
            beside = beside + np.roll(v, -1, dim) + np.roll(v, 1, dim)
        return center * v - coupling * beside

    def shrink(v):
        a, b, c = v.shape[:3]
        return v.reshape(a // 2, 2, b // 2, 2, c // 2, 2, -1).mean(axis=(1, 3, 5))

    def grow(v):
        return np.repeat(np.repeat(np.repeat(v, 2, 0), 2, 1), 2, 2)

    level_two = LEVELS - 2
    center, coupling = level_coeffs(level_two)
    correct_two = omega * field / center
    current = shrink(field - apply(correct_two, level_two))
    top_level = LEVELS - 1
    center_top, coupling_top = level_coeffs(top_level)
    correct = omega * current / center_top
    for sweep_id in range(COARSE - 1):
        correct = correct + omega * (current - apply(correct, top_level)) / center_top
    updated = correct_two + grow(correct)
    post = updated + omega * (field - apply(updated, level_two)) / center
    padded = [2 * size + 2 for size in block]
    for dim in range(3):
        index = [(starts[dim] + (p - 1) // 2) % grid[dim] for p in range(padded[dim])]
        post = np.take(post, index, axis=dim)
    rim = np.zeros(padded, np.int32)
    for dim in range(3):
        edge = np.zeros(padded[dim], np.int32)
        edge[0] = edge[-1] = 1
        rim = rim + edge.reshape([-1 if d == dim else 1 for d in range(3)])
    post = post * (rim <= 1)[..., None]
    post = post.reshape(-1, cells)
    return post.astype(np.float32)


def prolong_face(face, dim):
    for other in range(3):
        if other != dim:
            face = jnp.repeat(face, 2, other)
    return face


def coarse_faces(halo_block, dim):
    inner = halo_block
    for other in range(3):
        if other != dim:
            inner = lax.slice_in_dim(inner, 1, inner.shape[other] - 1, axis=other)
    size = inner.shape[dim]
    lo = lax.slice_in_dim(inner, 0, 1, axis=dim)
    hi = lax.slice_in_dim(inner, size - 1, size, axis=dim)
    return lo, hi


def post_smooth(level_id, corr, corr_faces, rhs, coarse_inner, coarse_face_list):
    center, coupling = level_coeffs(level_id)
    updated = corr + prolong(coarse_inner)
    faces = []
    for dim in range(3):
        lo = corr_faces[dim][0] + prolong_face(coarse_face_list[dim][0], dim)
        hi = corr_faces[dim][1] + prolong_face(coarse_face_list[dim][1], dim)
        faces.append((lo, hi))
    return updated + omega * (rhs - stencil(updated, faces, level_id)) / center


def post_smooth_padded(level_id, corr_padded, rhs, coarse_inner, coarse_face_list):
    center, coupling = level_coeffs(level_id)
    faces = [(prolong_face(lo, dim), prolong_face(hi, dim)) for dim, (lo, hi) in enumerate(coarse_face_list)]
    updated_padded = corr_padded + pad_with(prolong(coarse_inner), faces)
    updated = updated_padded[1:-1, 1:-1, 1:-1]
    return updated + omega * (rhs - padded_stencil(updated_padded, level_id)) / center


def dim_mask(box_part, offset, extent):
    cells = offset + jnp.arange(extent, dtype=jnp.int32)[:, None]
    return ((box_part[0][None, :] <= cells) & (cells < box_part[1][None, :])).astype(jnp.float32)


def gram_matrix(tiles_by_step, inv_tiles, tile_pairs, orb_count):
    count = lax.axis_size("gx")
    local = inv_tiles.shape[0]
    tile_edge = inv_tiles.shape[1]
    blocks = orb_count // tile_edge
    me = lax.axis_index("gx")
    pieces = []
    ids = []
    for step in range(count):
        piece = tiles_by_step.get(step)
        if piece is None:
            piece = inv_tiles if step == 0 else shifted(inv_tiles, "gx", step)
        pieces.append(piece)
        ids.append(((me + step) % count) * local + jnp.arange(local, dtype=jnp.int32))
    tiles = jnp.concatenate(pieces, axis=0)
    pairs = jnp.take(tile_pairs, jnp.concatenate(ids), axis=0)
    block_ids = jnp.arange(blocks, dtype=jnp.int32)
    rows = (pairs[:, 0][:, None] == block_ids[None, :]).astype(jnp.float32)
    cols = (pairs[:, 1][:, None] == block_ids[None, :]).astype(jnp.float32)
    spread = rows[:, :, None, None, None] * cols[:, None, None, :, None] * tiles[:, None, :, None, :]
    return spread.sum(axis=0).reshape(orb_count, orb_count)


def vcycle(residuals, inv_tiles):
    center, coupling = level_coeffs(0)
    faces_zero = all_faces(residuals, lambda part: omega * part.astype(jnp.float32) / center)
    rhs_zero = residuals.astype(jnp.float32)
    corr_zero = omega * rhs_zero / center
    rhs_one = restrict(rhs_zero - stencil(corr_zero, faces_zero, 0))
    center, coupling = level_coeffs(1)
    corr_one = omega * rhs_one / center
    padded_one = pad_with(corr_one, all_faces(corr_one))
    rhs_two = restrict(rhs_one - padded_stencil(padded_one, 1))
    coarse_padded, tiles_by_step = coarse_solve(rhs_two, inv_tiles)
    center, coupling = level_coeffs(1)
    updated_padded = padded_one + coarse_padded
    updated = updated_padded[1:-1, 1:-1, 1:-1]
    post_one = updated + omega * (rhs_one - padded_stencil(updated_padded, 1)) / center
    return post_smooth(0, corr_zero, faces_zero, rhs_zero, post_one, all_faces(post_one)), tiles_by_step


def body(residuals, patch_box, tile_pairs, inv_tiles):
    size_a, size_b, size_c, orb_count = residuals.shape
    lanes = LANES if orb_count % LANES == 0 else orb_count
    grouped = residuals.reshape(size_a, size_b, size_c, orb_count // lanes, lanes)
    correct, tiles_by_step = vcycle(grouped, inv_tiles)
    correct = correct.reshape(size_a, size_b, size_c, orb_count)
    gram = gram_matrix(tiles_by_step, inv_tiles, tile_pairs, orb_count)
    mask_first = dim_mask(patch_box[0], lax.axis_index("gx") * size_a, size_a)
    mask_second = dim_mask(patch_box[1], lax.axis_index("gy") * size_b, size_b)
    mask_third = dim_mask(patch_box[2], lax.axis_index("gz") * size_c, size_c)
    precond = correct * (
        mask_first[:, None, None, :] * mask_second[None, :, None, :] * mask_third[None, None, :, :]
    )
    cell_count = size_a * size_b * size_c
    rows = lax.optimization_barrier(precond.reshape(cell_count, orb_count))
    mixed = jnp.dot(rows, gram, precision=lax.Precision.HIGH, preferred_element_type=jnp.float32)
    return mixed.reshape(size_a, size_b, size_c, orb_count).astype(jnp.bfloat16)


def solution(mesh):
    return jax.shard_map(
        body,
        mesh=mesh,
        in_specs=(P("gx", "gy", "gz", None), P(), P(), P("gx", None, None)),
        out_specs=P("gx", "gy", "gz", None),
        check_vma=False,
    )
```

```python
import jax
import jax.numpy as jnp
import numpy as np
from jax import lax
from jax.sharding import PartitionSpec as P

LEVELS = 4
COARSE = 4


omega = 0.8
shift_sigma = 0.01

GRID_AXES = (("gx", 0), ("gy", 1), ("gz", 2))
COARSE_HALO = 10
LANES = 128


def shifted(block, axis, offset):
    count = lax.axis_size(axis)
    step = offset % count
    if step == 0:
        return block
    return lax.ppermute(block, axis, [(j, (j - step) % count) for j in range(count)])


def axis_faces(block, axis, dim, prepare=None):
    count = lax.axis_size(axis)
    first = lax.slice_in_dim(block, 0, 1, axis=dim)
    last = lax.slice_in_dim(block, block.shape[dim] - 1, None, axis=dim)
    if prepare is not None:
        first = prepare(first)
        last = prepare(last)
    if count == 1:
        return last, first
    if count == 2:
        both = lax.ppermute(jnp.concatenate([first, last], axis=dim), axis, [(0, 1), (1, 0)])
        hi = lax.slice_in_dim(both, 0, 1, axis=dim)
        lo = lax.slice_in_dim(both, 1, 2, axis=dim)
        return lo, hi
    lo = shifted(last, axis, -1)
    hi = shifted(first, axis, 1)
    return lo, hi


def all_faces(block, prepare=None):
    return [axis_faces(block, axis, dim, prepare) for axis, dim in GRID_AXES]


def extend_axis(block, axis, dim, halo, extra=None):
    count = lax.axis_size(axis)
    size = block.shape[dim]
    reach = -(-halo // size)
    if 2 * reach + 1 >= count:
        offsets = list(range(count))
        start = 0
    else:
        offsets = list(range(-reach, reach + 1))
        start = reach * size
    cache = {}
    extras = {}
    pieces = []
    for offset in offsets:
        step = offset % count
        if step not in cache:
            if extra is None or step == 0:
                cache[step] = shifted(block, axis, step)
                extras[step] = extra
            else:
                trailing = block.shape[1:]
                if extra.size % int(np.prod(trailing)) == 0:
                    both = jnp.concatenate([block, extra.reshape((-1,) + trailing)], axis=0)
                    both = shifted(both, axis, step)
                    cache[step] = both[: block.shape[0]]
                    extras[step] = both[block.shape[0] :].reshape(extra.shape)
                else:
                    both = jnp.concatenate([block.reshape(-1), extra.reshape(-1)])
                    both = shifted(both, axis, step)
                    cache[step] = both[: block.size].reshape(block.shape)
                    extras[step] = both[block.size :].reshape(extra.shape)
        pieces.append(cache[step])
    return jnp.concatenate(pieces, axis=dim), start, extras


def axis_offsets(count, size, halo):
    reach = -(-halo // size)
    if 2 * reach + 1 >= count:
        return list(range(count)), 0
    return list(range(-reach, reach + 1)), reach * size


def extend_joint(block, axes, dims, halo):
    counts = [lax.axis_size(axis) for axis in axes]
    plans = [axis_offsets(count, block.shape[dim], halo) for count, dim in zip(counts, dims)]
    cache = {}

    def fetch(offset):
        steps = tuple(o % c for o, c in zip(offset, counts))
        if steps not in cache:
            if not any(steps):
                cache[steps] = block
            else:
                pairs = []
                for target in range(_prod(counts)):
                    coords = _unravel(target, counts)
                    source = _ravel([(c + s) % n for c, s, n in zip(coords, steps, counts)], counts)
                    pairs.append((source, target))
                cache[steps] = lax.ppermute(block, tuple(axes), pairs)
        return cache[steps]

    def assemble(level, prefix):
        offsets, start = plans[level]
        if level == len(axes) - 1:
            pieces = [fetch(prefix + (o,)) for o in offsets]
        else:
            pieces = [assemble(level + 1, prefix + (o,)) for o in offsets]
        return jnp.concatenate(pieces, axis=dims[level])

    return assemble(0, ()), [start for offsets, start in plans]


def _prod(values):
    total = 1
    for v in values:
        total *= v
    return total


def _unravel(index, counts):
    coords = []
    for n in reversed(counts):
        coords.append(index % n)
        index //= n
    return list(reversed(coords))


def _ravel(coords, counts):
    index = 0
    for c, n in zip(coords, counts):
        index = index * n + c
    return index


def level_coeffs(level_id):
    coupling = 0.5 / 4.0**level_id
    return (6.0 * coupling + shift_sigma, coupling)


def pad_with(block, faces):
    padded = block
    for dim, (lo, hi) in enumerate(faces):
        widths = [(0, 0)] * block.ndim
        for other in range(dim):
            widths[other] = (1, 1)
        lo = jnp.pad(lo, widths)
        hi = jnp.pad(hi, widths)
        padded = jnp.concatenate([lo, padded, hi], axis=dim)
    return padded


def stencil(block, faces, level_id):
    return padded_stencil(pad_with(block, faces), level_id)


def padded_stencil(padded, level_id):
    center, coupling = level_coeffs(level_id)
    middle = padded[1:-1, 1:-1, 1:-1]
    beside = padded[2:, 1:-1, 1:-1] + padded[:-2, 1:-1, 1:-1]
    beside = beside + padded[1:-1, 2:, 1:-1] + padded[1:-1, :-2, 1:-1]
    beside = beside + padded[1:-1, 1:-1, 2:] + padded[1:-1, 1:-1, :-2]
    return center * middle - coupling * beside


def restrict(field):
    size_a, size_b, size_c = field.shape[:3]
    rest = field.shape[3:]
    return field.reshape((size_a // 2, 2, size_b // 2, 2, size_c // 2, 2) + rest).mean(axis=(1, 3, 5))


def prolong(field):
    return jnp.repeat(jnp.repeat(jnp.repeat(field, 2, 0), 2, 1), 2, 2)


def coarse_solve(rhs_two, tiles):
    extended = rhs_two
    starts = []
    extended, start, tiles_by_step = extend_axis(extended, "gx", 0, COARSE_HALO, tiles)
    starts.append(start)
    extended, joint_starts = extend_joint(extended, ("gy", "gz"), (1, 2), COARSE_HALO)
    starts.extend(joint_starts)
    grid = extended.shape[:3]
    orbs = extended.shape[3:]
    operator = coarse_matrix(grid, tuple(starts), rhs_two.shape[:3])
    operator = jnp.asarray(operator.reshape((-1,) + tuple(grid)))
    post = jnp.einsum(
        "qxyz,xyzgl->qgl", operator, extended, precision=lax.Precision.HIGH, preferred_element_type=jnp.float32
    )
    return post.reshape(tuple(2 * size + 2 for size in rhs_two.shape[:3]) + orbs), tiles_by_step


def coarse_matrix(grid, starts, block):
    cells = int(np.prod(grid))
    field = np.eye(cells).reshape(grid + (cells,))

    def apply(v, level_id):
        center, coupling = level_coeffs(level_id)
        beside = 0.0
        for dim in range(3):
            beside = beside + np.roll(v, -1, dim) + np.roll(v, 1, dim)
        return center * v - coupling * beside

    def shrink(v):
        a, b, c = v.shape[:3]
        return v.reshape(a // 2, 2, b // 2, 2, c // 2, 2, -1).mean(axis=(1, 3, 5))

    def grow(v):
        return np.repeat(np.repeat(np.repeat(v, 2, 0), 2, 1), 2, 2)

    level_two = LEVELS - 2
    center, coupling = level_coeffs(level_two)
    correct_two = omega * field / center
    current = shrink(field - apply(correct_two, level_two))
    top_level = LEVELS - 1
    center_top, coupling_top = level_coeffs(top_level)
    correct = omega * current / center_top
    for sweep_id in range(COARSE - 1):
        correct = correct + omega * (current - apply(correct, top_level)) / center_top
    updated = correct_two + grow(correct)
    post = updated + omega * (field - apply(updated, level_two)) / center
    padded = [2 * size + 2 for size in block]
    for dim in range(3):
        index = [(starts[dim] + (p - 1) // 2) % grid[dim] for p in range(padded[dim])]
        post = np.take(post, index, axis=dim)
    rim = np.zeros(padded, np.int32)
    for dim in range(3):
        edge = np.zeros(padded[dim], np.int32)
        edge[0] = edge[-1] = 1
        rim = rim + edge.reshape([-1 if d == dim else 1 for d in range(3)])
    post = post * (rim <= 1)[..., None]
    post = post.reshape(-1, cells)
    return post.astype(np.float32)


def prolong_face(face, dim):
    for other in range(3):
        if other != dim:
            face = jnp.repeat(face, 2, other)
    return face


def coarse_faces(halo_block, dim):
    inner = halo_block
    for other in range(3):
        if other != dim:
            inner = lax.slice_in_dim(inner, 1, inner.shape[other] - 1, axis=other)
    size = inner.shape[dim]
    lo = lax.slice_in_dim(inner, 0, 1, axis=dim)
    hi = lax.slice_in_dim(inner, size - 1, size, axis=dim)
    return lo, hi


def post_smooth(level_id, corr, corr_faces, rhs, coarse_inner, coarse_face_list):
    center, coupling = level_coeffs(level_id)
    updated = corr + prolong(coarse_inner)
    faces = []
    for dim in range(3):
        lo = corr_faces[dim][0] + prolong_face(coarse_face_list[dim][0], dim)
        hi = corr_faces[dim][1] + prolong_face(coarse_face_list[dim][1], dim)
        faces.append((lo, hi))
    return updated + omega * (rhs - stencil(updated, faces, level_id)) / center


def post_smooth_padded(level_id, corr_padded, rhs, coarse_inner, coarse_face_list):
    center, coupling = level_coeffs(level_id)
    faces = [(prolong_face(lo, dim), prolong_face(hi, dim)) for dim, (lo, hi) in enumerate(coarse_face_list)]
    updated_padded = corr_padded + pad_with(prolong(coarse_inner), faces)
    updated = updated_padded[1:-1, 1:-1, 1:-1]
    return updated + omega * (rhs - padded_stencil(updated_padded, level_id)) / center


def dim_mask(box_part, offset, extent):
    cells = offset + jnp.arange(extent, dtype=jnp.int32)[:, None]
    return ((box_part[0][None, :] <= cells) & (cells < box_part[1][None, :])).astype(jnp.float32)


def gram_matrix(tiles_by_step, inv_tiles, tile_pairs, orb_count):
    count = lax.axis_size("gx")
    local = inv_tiles.shape[0]
    tile_edge = inv_tiles.shape[1]
    blocks = orb_count // tile_edge
    me = lax.axis_index("gx")
    pieces = []
    ids = []
    for step in range(count):
        piece = tiles_by_step.get(step)
        if piece is None:
            piece = inv_tiles if step == 0 else shifted(inv_tiles, "gx", step)
        pieces.append(piece)
        ids.append(((me + step) % count) * local + jnp.arange(local, dtype=jnp.int32))
    tiles = jnp.concatenate(pieces, axis=0)
    pairs = jnp.take(tile_pairs, jnp.concatenate(ids), axis=0)
    block_ids = jnp.arange(blocks, dtype=jnp.int32)
    rows = (pairs[:, 0][:, None] == block_ids[None, :]).astype(jnp.float32)
    cols = (pairs[:, 1][:, None] == block_ids[None, :]).astype(jnp.float32)
    spread = rows[:, :, None, None, None] * cols[:, None, None, :, None] * tiles[:, None, :, None, :]
    return spread.sum(axis=0).reshape(orb_count, orb_count)


def vcycle(residuals, inv_tiles):
    center, coupling = level_coeffs(0)
    faces_zero = all_faces(residuals, lambda part: omega * part.astype(jnp.float32) / center)
    rhs_zero = residuals.astype(jnp.float32)
    corr_zero = omega * rhs_zero / center
    rhs_one = restrict(rhs_zero - stencil(corr_zero, faces_zero, 0))
    center, coupling = level_coeffs(1)
    corr_one = omega * rhs_one / center
    padded_one = pad_with(corr_one, all_faces(corr_one))
    rhs_two = restrict(rhs_one - padded_stencil(padded_one, 1))
    coarse_padded, tiles_by_step = coarse_solve(rhs_two, inv_tiles)
    center, coupling = level_coeffs(1)
    updated_padded = padded_one + coarse_padded
    updated = updated_padded[1:-1, 1:-1, 1:-1]
    post_one = updated + omega * (rhs_one - padded_stencil(updated_padded, 1)) / center
    return post_smooth(0, corr_zero, faces_zero, rhs_zero, post_one, all_faces(post_one)), tiles_by_step


def body(residuals, patch_box, tile_pairs, inv_tiles):
    size_a, size_b, size_c, orb_count = residuals.shape
    lanes = LANES if orb_count % LANES == 0 else orb_count
    grouped = residuals.reshape(size_a, size_b, size_c, orb_count // lanes, lanes)
    correct, tiles_by_step = vcycle(grouped, inv_tiles)
    correct = correct.reshape(size_a, size_b, size_c, orb_count)
    gram = gram_matrix(tiles_by_step, inv_tiles, tile_pairs, orb_count)
    mask_first = dim_mask(patch_box[0], lax.axis_index("gx") * size_a, size_a)
    mask_second = dim_mask(patch_box[1], lax.axis_index("gy") * size_b, size_b)
    mask_third = dim_mask(patch_box[2], lax.axis_index("gz") * size_c, size_c)
    precond = correct * (
        mask_first[:, None, None, :] * mask_second[None, :, None, :] * mask_third[None, None, :, :]
    )
    cell_count = size_a * size_b * size_c
    rows = lax.optimization_barrier(precond.reshape(cell_count, orb_count))
    mixed = jnp.dot(rows, gram, precision=lax.Precision.HIGH, preferred_element_type=jnp.float32)
    return mixed.reshape(size_a, size_b, size_c, orb_count).astype(jnp.bfloat16)


def solution(mesh):
    return jax.shard_map(
        body,
        mesh=mesh,
        in_specs=(P("gx", "gy", "gz", None), P(), P(), P("gx", None, None)),
        out_specs=P("gx", "gy", "gz", None),
        check_vma=False,
    )
```

```python
import jax
import jax.numpy as jnp
import numpy as np
from jax import lax
from jax.sharding import PartitionSpec as P

LEVELS = 4
COARSE = 4


omega = 0.8
shift_sigma = 0.01

GRID_AXES = (("gx", 0), ("gy", 1), ("gz", 2))
COARSE_HALO = 10
LANES = 128


def shifted(block, axis, offset):
    count = lax.axis_size(axis)
    step = offset % count
    if step == 0:
        return block
    return lax.ppermute(block, axis, [(j, (j - step) % count) for j in range(count)])


def axis_faces(block, axis, dim, prepare=None):
    count = lax.axis_size(axis)
    first = lax.slice_in_dim(block, 0, 1, axis=dim)
    last = lax.slice_in_dim(block, block.shape[dim] - 1, None, axis=dim)
    if prepare is not None:
        first = prepare(first)
        last = prepare(last)
    if count == 1:
        return last, first
    if count == 2:
        both = lax.ppermute(jnp.concatenate([first, last], axis=dim), axis, [(0, 1), (1, 0)])
        hi = lax.slice_in_dim(both, 0, 1, axis=dim)
        lo = lax.slice_in_dim(both, 1, 2, axis=dim)
        return lo, hi
    lo = shifted(last, axis, -1)
    hi = shifted(first, axis, 1)
    return lo, hi


def all_faces(block, prepare=None):
    return [axis_faces(block, axis, dim, prepare) for axis, dim in GRID_AXES]


def extend_axis(block, axis, dim, halo, extra=None):
    count = lax.axis_size(axis)
    size = block.shape[dim]
    reach = -(-halo // size)
    if 2 * reach + 1 >= count:
        offsets = list(range(count))
        start = 0
    else:
        offsets = list(range(-reach, reach + 1))
        start = reach * size
    cache = {}
    extras = {}
    pieces = []
    for offset in offsets:
        step = offset % count
        if step not in cache:
            if extra is None or step == 0:
                cache[step] = shifted(block, axis, step)
                extras[step] = extra
            else:
                trailing = block.shape[1:]
                if extra.size % int(np.prod(trailing)) == 0:
                    both = jnp.concatenate([block, extra.reshape((-1,) + trailing)], axis=0)
                    both = shifted(both, axis, step)
                    cache[step] = both[: block.shape[0]]
                    extras[step] = both[block.shape[0] :].reshape(extra.shape)
                else:
                    both = jnp.concatenate([block.reshape(-1), extra.reshape(-1)])
                    both = shifted(both, axis, step)
                    cache[step] = both[: block.size].reshape(block.shape)
                    extras[step] = both[block.size :].reshape(extra.shape)
        pieces.append(cache[step])
    return jnp.concatenate(pieces, axis=dim), start, extras


def axis_offsets(count, size, halo):
    reach = -(-halo // size)
    if 2 * reach + 1 >= count:
        return list(range(count)), 0
    return list(range(-reach, reach + 1)), reach * size


def extend_joint(block, axes, dims, halo):
    counts = [lax.axis_size(axis) for axis in axes]
    plans = [axis_offsets(count, block.shape[dim], halo) for count, dim in zip(counts, dims)]
    cache = {}

    def fetch(offset):
        steps = tuple(o % c for o, c in zip(offset, counts))
        if steps not in cache:
            if not any(steps):
                cache[steps] = block
            else:
                pairs = []
                for target in range(_prod(counts)):
                    coords = _unravel(target, counts)
                    source = _ravel([(c + s) % n for c, s, n in zip(coords, steps, counts)], counts)
                    pairs.append((source, target))
                cache[steps] = lax.ppermute(block, tuple(axes), pairs)
        return cache[steps]

    def assemble(level, prefix):
        offsets, start = plans[level]
        if level == len(axes) - 1:
            pieces = [fetch(prefix + (o,)) for o in offsets]
        else:
            pieces = [assemble(level + 1, prefix + (o,)) for o in offsets]
        return jnp.concatenate(pieces, axis=dims[level])

    return assemble(0, ()), [start for offsets, start in plans]


def _prod(values):
    total = 1
    for v in values:
        total *= v
    return total


def _unravel(index, counts):
    coords = []
    for n in reversed(counts):
        coords.append(index % n)
        index //= n
    return list(reversed(coords))


def _ravel(coords, counts):
    index = 0
    for c, n in zip(coords, counts):
        index = index * n + c
    return index


def level_coeffs(level_id):
    coupling = 0.5 / 4.0**level_id
    return (6.0 * coupling + shift_sigma, coupling)


def pad_with(block, faces):
    padded = block
    for dim, (lo, hi) in enumerate(faces):
        widths = [(0, 0)] * block.ndim
        for other in range(dim):
            widths[other] = (1, 1)
        lo = jnp.pad(lo, widths)
        hi = jnp.pad(hi, widths)
        padded = jnp.concatenate([lo, padded, hi], axis=dim)
    return padded


def stencil(block, faces, level_id):
    return padded_stencil(pad_with(block, faces), level_id)


def padded_stencil(padded, level_id):
    center, coupling = level_coeffs(level_id)
    middle = padded[1:-1, 1:-1, 1:-1]
    beside = padded[2:, 1:-1, 1:-1] + padded[:-2, 1:-1, 1:-1]
    beside = beside + padded[1:-1, 2:, 1:-1] + padded[1:-1, :-2, 1:-1]
    beside = beside + padded[1:-1, 1:-1, 2:] + padded[1:-1, 1:-1, :-2]
    return center * middle - coupling * beside


def restrict(field):
    for dim in range(3):
        size = field.shape[dim]
        even = lax.slice_in_dim(field, 0, size, stride=2, axis=dim)
        odd = lax.slice_in_dim(field, 1, size, stride=2, axis=dim)
        field = even + odd
    return field * 0.125


def prolong(field):
    return jnp.repeat(jnp.repeat(jnp.repeat(field, 2, 0), 2, 1), 2, 2)


def coarse_solve(rhs_two, tiles):
    extended = rhs_two
    starts = []
    extended, start, tiles_by_step = extend_axis(extended, "gx", 0, COARSE_HALO, tiles)
    starts.append(start)
    extended, joint_starts = extend_joint(extended, ("gy", "gz"), (1, 2), COARSE_HALO)
    starts.extend(joint_starts)
    grid = extended.shape[:3]
    orbs = extended.shape[3:]
    operator = coarse_matrix(grid, tuple(starts), rhs_two.shape[:3])
    operator = jnp.asarray(operator.reshape((-1,) + tuple(grid)))
    post = jnp.einsum(
        "qxyz,xyzgl->qgl", operator, extended, precision=lax.Precision.HIGHEST, preferred_element_type=jnp.float32
    )
    return post.reshape(tuple(2 * size + 2 for size in rhs_two.shape[:3]) + orbs), tiles_by_step


def coarse_matrix(grid, starts, block):
    cells = int(np.prod(grid))
    field = np.eye(cells).reshape(grid + (cells,))

    def apply(v, level_id):
        center, coupling = level_coeffs(level_id)
        beside = 0.0
        for dim in range(3):
            beside = beside + np.roll(v, -1, dim) + np.roll(v, 1, dim)
        return center * v - coupling * beside

    def shrink(v):
        a, b, c = v.shape[:3]
        return v.reshape(a // 2, 2, b // 2, 2, c // 2, 2, -1).mean(axis=(1, 3, 5))

    def grow(v):
        return np.repeat(np.repeat(np.repeat(v, 2, 0), 2, 1), 2, 2)

    level_two = LEVELS - 2
    center, coupling = level_coeffs(level_two)
    correct_two = omega * field / center
    current = shrink(field - apply(correct_two, level_two))
    top_level = LEVELS - 1
    center_top, coupling_top = level_coeffs(top_level)
    correct = omega * current / center_top
    for sweep_id in range(COARSE - 1):
        correct = correct + omega * (current - apply(correct, top_level)) / center_top
    updated = correct_two + grow(correct)
    post = updated + omega * (field - apply(updated, level_two)) / center
    padded = [2 * size + 2 for size in block]
    for dim in range(3):
        index = [(starts[dim] + (p - 1) // 2) % grid[dim] for p in range(padded[dim])]
        post = np.take(post, index, axis=dim)
    rim = np.zeros(padded, np.int32)
    for dim in range(3):
        edge = np.zeros(padded[dim], np.int32)
        edge[0] = edge[-1] = 1
        rim = rim + edge.reshape([-1 if d == dim else 1 for d in range(3)])
    post = post * (rim <= 1)[..., None]
    post = post.reshape(-1, cells)
    return post.astype(np.float32)


def prolong_face(face, dim):
    for other in range(3):
        if other != dim:
            face = jnp.repeat(face, 2, other)
    return face


def coarse_faces(halo_block, dim):
    inner = halo_block
    for other in range(3):
        if other != dim:
            inner = lax.slice_in_dim(inner, 1, inner.shape[other] - 1, axis=other)
    size = inner.shape[dim]
    lo = lax.slice_in_dim(inner, 0, 1, axis=dim)
    hi = lax.slice_in_dim(inner, size - 1, size, axis=dim)
    return lo, hi


def post_smooth(level_id, corr, corr_faces, rhs, coarse_inner, coarse_face_list):
    center, coupling = level_coeffs(level_id)
    updated = corr + prolong(coarse_inner)
    faces = []
    for dim in range(3):
        lo = corr_faces[dim][0] + prolong_face(coarse_face_list[dim][0], dim)
        hi = corr_faces[dim][1] + prolong_face(coarse_face_list[dim][1], dim)
        faces.append((lo, hi))
    return updated + omega * (rhs - stencil(updated, faces, level_id)) / center


def post_smooth_padded(level_id, corr_padded, rhs, coarse_inner, coarse_face_list):
    center, coupling = level_coeffs(level_id)
    faces = [(prolong_face(lo, dim), prolong_face(hi, dim)) for dim, (lo, hi) in enumerate(coarse_face_list)]
    updated_padded = corr_padded + pad_with(prolong(coarse_inner), faces)
    updated = updated_padded[1:-1, 1:-1, 1:-1]
    return updated + omega * (rhs - padded_stencil(updated_padded, level_id)) / center


def dim_mask(box_part, offset, extent):
    cells = offset + jnp.arange(extent, dtype=jnp.int32)[:, None]
    return ((box_part[0][None, :] <= cells) & (cells < box_part[1][None, :])).astype(jnp.float32)


def gram_matrix(tiles_by_step, inv_tiles, tile_pairs, orb_count):
    count = lax.axis_size("gx")
    local = inv_tiles.shape[0]
    tile_edge = inv_tiles.shape[1]
    blocks = orb_count // tile_edge
    me = lax.axis_index("gx")
    pieces = []
    ids = []
    for step in range(count):
        piece = tiles_by_step.get(step)
        if piece is None:
            piece = inv_tiles if step == 0 else shifted(inv_tiles, "gx", step)
        pieces.append(piece)
        ids.append(((me + step) % count) * local + jnp.arange(local, dtype=jnp.int32))
    tiles = jnp.concatenate(pieces, axis=0)
    pairs = jnp.take(tile_pairs, jnp.concatenate(ids), axis=0)
    block_ids = jnp.arange(blocks, dtype=jnp.int32)
    rows = (pairs[:, 0][:, None] == block_ids[None, :]).astype(jnp.float32)
    cols = (pairs[:, 1][:, None] == block_ids[None, :]).astype(jnp.float32)
    spread = rows[:, :, None, None, None] * cols[:, None, None, :, None] * tiles[:, None, :, None, :]
    return spread.sum(axis=0).reshape(orb_count, orb_count)


def vcycle(residuals, inv_tiles):
    center, coupling = level_coeffs(0)
    faces_zero = all_faces(residuals, lambda part: omega * part.astype(jnp.float32) / center)
    rhs_zero = residuals.astype(jnp.float32)
    corr_zero = omega * rhs_zero / center
    rhs_one = restrict(rhs_zero - stencil(corr_zero, faces_zero, 0))
    center, coupling = level_coeffs(1)
    corr_one = omega * rhs_one / center
    padded_one = pad_with(corr_one, all_faces(corr_one))
    rhs_two = restrict(rhs_one - padded_stencil(padded_one, 1))
    coarse_padded, tiles_by_step = coarse_solve(rhs_two, inv_tiles)
    center, coupling = level_coeffs(1)
    updated_padded = padded_one + coarse_padded
    updated = updated_padded[1:-1, 1:-1, 1:-1]
    post_one = updated + omega * (rhs_one - padded_stencil(updated_padded, 1)) / center
    return post_smooth(0, corr_zero, faces_zero, rhs_zero, post_one, all_faces(post_one)), tiles_by_step


def body(residuals, patch_box, tile_pairs, inv_tiles):
    size_a, size_b, size_c, orb_count = residuals.shape
    lanes = LANES if orb_count % LANES == 0 else orb_count
    grouped = residuals.reshape(size_a, size_b, size_c, orb_count // lanes, lanes)
    correct, tiles_by_step = vcycle(grouped, inv_tiles)
    correct = correct.reshape(size_a, size_b, size_c, orb_count)
    gram = gram_matrix(tiles_by_step, inv_tiles, tile_pairs, orb_count)
    mask_first = dim_mask(patch_box[0], lax.axis_index("gx") * size_a, size_a)
    mask_second = dim_mask(patch_box[1], lax.axis_index("gy") * size_b, size_b)
    mask_third = dim_mask(patch_box[2], lax.axis_index("gz") * size_c, size_c)
    precond = correct * (
        mask_first[:, None, None, :] * mask_second[None, :, None, :] * mask_third[None, None, :, :]
    )
    cell_count = size_a * size_b * size_c
    rows = lax.optimization_barrier(precond.reshape(cell_count, orb_count))
    mixed = jnp.dot(rows, gram, precision=lax.Precision.HIGH, preferred_element_type=jnp.float32)
    return mixed.reshape(size_a, size_b, size_c, orb_count).astype(jnp.bfloat16)


def solution(mesh):
    return jax.shard_map(
        body,
        mesh=mesh,
        in_specs=(P("gx", "gy", "gz", None), P(), P(), P("gx", None, None)),
        out_specs=P("gx", "gy", "gz", None),
        check_vma=False,
    )
```

```python
import jax
import jax.numpy as jnp
import numpy as np
from jax import lax
from jax.sharding import PartitionSpec as P

LEVELS = 4
COARSE = 4


omega = 0.8
shift_sigma = 0.01

GRID_AXES = (("gx", 0), ("gy", 1), ("gz", 2))
COARSE_HALO = 10
LANES = 128


def shifted(block, axis, offset):
    count = lax.axis_size(axis)
    step = offset % count
    if step == 0:
        return block
    return lax.ppermute(block, axis, [(j, (j - step) % count) for j in range(count)])


def axis_faces(block, axis, dim, prepare=None):
    count = lax.axis_size(axis)
    first = lax.slice_in_dim(block, 0, 1, axis=dim)
    last = lax.slice_in_dim(block, block.shape[dim] - 1, None, axis=dim)
    if prepare is not None:
        first = prepare(first)
        last = prepare(last)
    if count == 1:
        return last, first
    if count == 2:
        both = lax.ppermute(jnp.concatenate([first, last], axis=dim), axis, [(0, 1), (1, 0)])
        hi = lax.slice_in_dim(both, 0, 1, axis=dim)
        lo = lax.slice_in_dim(both, 1, 2, axis=dim)
        return lo, hi
    lo = shifted(last, axis, -1)
    hi = shifted(first, axis, 1)
    return lo, hi


def all_faces(block, prepare=None):
    return [axis_faces(block, axis, dim, prepare) for axis, dim in GRID_AXES]


def extend_axis(block, axis, dim, halo, extra=None):
    count = lax.axis_size(axis)
    size = block.shape[dim]
    reach = -(-halo // size)
    if 2 * reach + 1 >= count:
        offsets = list(range(count))
        start = 0
    else:
        offsets = list(range(-reach, reach + 1))
        start = reach * size
    cache = {}
    extras = {}
    pieces = []
    for offset in offsets:
        step = offset % count
        if step not in cache:
            if extra is None or step == 0:
                cache[step] = shifted(block, axis, step)
                extras[step] = extra
            else:
                trailing = block.shape[1:]
                if extra.size % int(np.prod(trailing)) == 0:
                    both = jnp.concatenate([block, extra.reshape((-1,) + trailing)], axis=0)
                    both = shifted(both, axis, step)
                    cache[step] = both[: block.shape[0]]
                    extras[step] = both[block.shape[0] :].reshape(extra.shape)
                else:
                    both = jnp.concatenate([block.reshape(-1), extra.reshape(-1)])
                    both = shifted(both, axis, step)
                    cache[step] = both[: block.size].reshape(block.shape)
                    extras[step] = both[block.size :].reshape(extra.shape)
        pieces.append(cache[step])
    return jnp.concatenate(pieces, axis=dim), start, extras


def axis_offsets(count, size, halo):
    reach = -(-halo // size)
    if 2 * reach + 1 >= count:
        return list(range(count)), 0
    return list(range(-reach, reach + 1)), reach * size


def extend_joint(block, axes, dims, halo):
    counts = [lax.axis_size(axis) for axis in axes]
    plans = [axis_offsets(count, block.shape[dim], halo) for count, dim in zip(counts, dims)]
    cache = {}

    def fetch(offset):
        steps = tuple(o % c for o, c in zip(offset, counts))
        if steps not in cache:
            if not any(steps):
                cache[steps] = block
            else:
                pairs = []
                for target in range(_prod(counts)):
                    coords = _unravel(target, counts)
                    source = _ravel([(c + s) % n for c, s, n in zip(coords, steps, counts)], counts)
                    pairs.append((source, target))
                cache[steps] = lax.ppermute(block, tuple(axes), pairs)
        return cache[steps]

    def assemble(level, prefix):
        offsets, start = plans[level]
        if level == len(axes) - 1:
            pieces = [fetch(prefix + (o,)) for o in offsets]
        else:
            pieces = [assemble(level + 1, prefix + (o,)) for o in offsets]
        return jnp.concatenate(pieces, axis=dims[level])

    return assemble(0, ()), [start for offsets, start in plans]


def _prod(values):
    total = 1
    for v in values:
        total *= v
    return total


def _unravel(index, counts):
    coords = []
    for n in reversed(counts):
        coords.append(index % n)
        index //= n
    return list(reversed(coords))


def _ravel(coords, counts):
    index = 0
    for c, n in zip(coords, counts):
        index = index * n + c
    return index


def level_coeffs(level_id):
    coupling = 0.5 / 4.0**level_id
    return (6.0 * coupling + shift_sigma, coupling)


def pad_with(block, faces):
    padded = block
    for dim, (lo, hi) in enumerate(faces):
        widths = [(0, 0)] * block.ndim
        for other in range(dim):
            widths[other] = (1, 1)
        lo = jnp.pad(lo, widths)
        hi = jnp.pad(hi, widths)
        padded = jnp.concatenate([lo, padded, hi], axis=dim)
    return padded


def stencil(block, faces, level_id):
    return padded_stencil(pad_with(block, faces), level_id)


def padded_stencil(padded, level_id):
    center, coupling = level_coeffs(level_id)
    middle = padded[1:-1, 1:-1, 1:-1]
    beside = padded[2:, 1:-1, 1:-1] + padded[:-2, 1:-1, 1:-1]
    beside = beside + padded[1:-1, 2:, 1:-1] + padded[1:-1, :-2, 1:-1]
    beside = beside + padded[1:-1, 1:-1, 2:] + padded[1:-1, 1:-1, :-2]
    return center * middle - coupling * beside


def restrict(field):
    for dim in range(3):
        size = field.shape[dim]
        even = lax.slice_in_dim(field, 0, size, stride=2, axis=dim)
        odd = lax.slice_in_dim(field, 1, size, stride=2, axis=dim)
        field = even + odd
    return field * 0.125


def prolong(field):
    return jnp.repeat(jnp.repeat(jnp.repeat(field, 2, 0), 2, 1), 2, 2)


def coarse_solve(rhs_two, tiles):
    extended, joint_starts = extend_joint(rhs_two, ("gy", "gz"), (1, 2), COARSE_HALO)
    extended, start, tiles_by_step = extend_axis(extended, "gx", 0, COARSE_HALO, tiles)
    starts = [start] + list(joint_starts)
    grid = extended.shape[:3]
    orbs = extended.shape[3:]
    operator = coarse_matrix(grid, tuple(starts), rhs_two.shape[:3])
    operator = jnp.asarray(operator.reshape((-1,) + tuple(grid)))
    post = jnp.einsum(
        "qxyz,xyzgl->qgl", operator, extended, precision=lax.Precision.HIGHEST, preferred_element_type=jnp.float32
    )
    return post.reshape(tuple(2 * size + 2 for size in rhs_two.shape[:3]) + orbs), tiles_by_step


def coarse_matrix(grid, starts, block):
    cells = int(np.prod(grid))
    field = np.eye(cells).reshape(grid + (cells,))

    def apply(v, level_id):
        center, coupling = level_coeffs(level_id)
        beside = 0.0
        for dim in range(3):
            beside = beside + np.roll(v, -1, dim) + np.roll(v, 1, dim)
        return center * v - coupling * beside

    def shrink(v):
        a, b, c = v.shape[:3]
        return v.reshape(a // 2, 2, b // 2, 2, c // 2, 2, -1).mean(axis=(1, 3, 5))

    def grow(v):
        return np.repeat(np.repeat(np.repeat(v, 2, 0), 2, 1), 2, 2)

    level_two = LEVELS - 2
    center, coupling = level_coeffs(level_two)
    correct_two = omega * field / center
    current = shrink(field - apply(correct_two, level_two))
    top_level = LEVELS - 1
    center_top, coupling_top = level_coeffs(top_level)
    correct = omega * current / center_top
    for sweep_id in range(COARSE - 1):
        correct = correct + omega * (current - apply(correct, top_level)) / center_top
    updated = correct_two + grow(correct)
    post = updated + omega * (field - apply(updated, level_two)) / center
    padded = [2 * size + 2 for size in block]
    for dim in range(3):
        index = [(starts[dim] + (p - 1) // 2) % grid[dim] for p in range(padded[dim])]
        post = np.take(post, index, axis=dim)
    rim = np.zeros(padded, np.int32)
    for dim in range(3):
        edge = np.zeros(padded[dim], np.int32)
        edge[0] = edge[-1] = 1
        rim = rim + edge.reshape([-1 if d == dim else 1 for d in range(3)])
    post = post * (rim <= 1)[..., None]
    post = post.reshape(-1, cells)
    return post.astype(np.float32)


def prolong_face(face, dim):
    for other in range(3):
        if other != dim:
            face = jnp.repeat(face, 2, other)
    return face


def coarse_faces(halo_block, dim):
    inner = halo_block
    for other in range(3):
        if other != dim:
            inner = lax.slice_in_dim(inner, 1, inner.shape[other] - 1, axis=other)
    size = inner.shape[dim]
    lo = lax.slice_in_dim(inner, 0, 1, axis=dim)
    hi = lax.slice_in_dim(inner, size - 1, size, axis=dim)
    return lo, hi


def post_smooth(level_id, corr, corr_faces, rhs, coarse_inner, coarse_face_list):
    center, coupling = level_coeffs(level_id)
    updated = corr + prolong(coarse_inner)
    faces = []
    for dim in range(3):
        lo = corr_faces[dim][0] + prolong_face(coarse_face_list[dim][0], dim)
        hi = corr_faces[dim][1] + prolong_face(coarse_face_list[dim][1], dim)
        faces.append((lo, hi))
    return updated + omega * (rhs - stencil(updated, faces, level_id)) / center


def post_smooth_padded(level_id, corr_padded, rhs, coarse_inner, coarse_face_list):
    center, coupling = level_coeffs(level_id)
    faces = [(prolong_face(lo, dim), prolong_face(hi, dim)) for dim, (lo, hi) in enumerate(coarse_face_list)]
    updated_padded = corr_padded + pad_with(prolong(coarse_inner), faces)
    updated = updated_padded[1:-1, 1:-1, 1:-1]
    return updated + omega * (rhs - padded_stencil(updated_padded, level_id)) / center


def dim_mask(box_part, offset, extent):
    cells = offset + jnp.arange(extent, dtype=jnp.int32)[:, None]
    return ((box_part[0][None, :] <= cells) & (cells < box_part[1][None, :])).astype(jnp.float32)


def gram_matrix(tiles_by_step, inv_tiles, tile_pairs, orb_count):
    count = lax.axis_size("gx")
    local = inv_tiles.shape[0]
    tile_edge = inv_tiles.shape[1]
    blocks = orb_count // tile_edge
    me = lax.axis_index("gx")
    pieces = []
    ids = []
    for step in range(count):
        piece = tiles_by_step.get(step)
        if piece is None:
            piece = inv_tiles if step == 0 else shifted(inv_tiles, "gx", step)
        pieces.append(piece)
        ids.append(((me + step) % count) * local + jnp.arange(local, dtype=jnp.int32))
    tiles = jnp.concatenate(pieces, axis=0)
    pairs = jnp.take(tile_pairs, jnp.concatenate(ids), axis=0)
    block_ids = jnp.arange(blocks, dtype=jnp.int32)
    rows = (pairs[:, 0][:, None] == block_ids[None, :]).astype(jnp.float32)
    cols = (pairs[:, 1][:, None] == block_ids[None, :]).astype(jnp.float32)
    spread = rows[:, :, None, None, None] * cols[:, None, None, :, None] * tiles[:, None, :, None, :]
    return spread.sum(axis=0).reshape(orb_count, orb_count)


def vcycle(residuals, inv_tiles):
    center, coupling = level_coeffs(0)
    faces_zero = all_faces(residuals, lambda part: omega * part.astype(jnp.float32) / center)
    rhs_zero = residuals.astype(jnp.float32)
    corr_zero = omega * rhs_zero / center
    rhs_one = restrict(rhs_zero - stencil(corr_zero, faces_zero, 0))
    center, coupling = level_coeffs(1)
    corr_one = omega * rhs_one / center
    padded_one = pad_with(corr_one, all_faces(corr_one))
    rhs_two = restrict(rhs_one - padded_stencil(padded_one, 1))
    coarse_padded, tiles_by_step = coarse_solve(rhs_two, inv_tiles)
    center, coupling = level_coeffs(1)
    updated_padded = padded_one + coarse_padded
    updated = updated_padded[1:-1, 1:-1, 1:-1]
    post_one = updated + omega * (rhs_one - padded_stencil(updated_padded, 1)) / center
    return post_smooth(0, corr_zero, faces_zero, rhs_zero, post_one, all_faces(post_one)), tiles_by_step


def body(residuals, patch_box, tile_pairs, inv_tiles):
    size_a, size_b, size_c, orb_count = residuals.shape
    lanes = LANES if orb_count % LANES == 0 else orb_count
    grouped = residuals.reshape(size_a, size_b, size_c, orb_count // lanes, lanes)
    correct, tiles_by_step = vcycle(grouped, inv_tiles)
    correct = correct.reshape(size_a, size_b, size_c, orb_count)
    gram = gram_matrix(tiles_by_step, inv_tiles, tile_pairs, orb_count)
    mask_first = dim_mask(patch_box[0], lax.axis_index("gx") * size_a, size_a)
    mask_second = dim_mask(patch_box[1], lax.axis_index("gy") * size_b, size_b)
    mask_third = dim_mask(patch_box[2], lax.axis_index("gz") * size_c, size_c)
    precond = correct * (
        mask_first[:, None, None, :] * mask_second[None, :, None, :] * mask_third[None, None, :, :]
    )
    cell_count = size_a * size_b * size_c
    rows = lax.optimization_barrier(precond.reshape(cell_count, orb_count))
    mixed = jnp.dot(rows, gram, precision=lax.Precision.HIGH, preferred_element_type=jnp.float32)
    return mixed.reshape(size_a, size_b, size_c, orb_count).astype(jnp.bfloat16)


def solution(mesh):
    return jax.shard_map(
        body,
        mesh=mesh,
        in_specs=(P("gx", "gy", "gz", None), P(), P(), P("gx", None, None)),
        out_specs=P("gx", "gy", "gz", None),
        check_vma=False,
    )
```

```python
import jax
import jax.numpy as jnp
import numpy as np
from jax import lax
from jax.sharding import PartitionSpec as P

LEVELS = 4
COARSE = 4


omega = 0.8
shift_sigma = 0.01

GRID_AXES = (("gx", 0), ("gy", 1), ("gz", 2))
COARSE_HALO = 10
LANES = 128


def shifted(block, axis, offset):
    count = lax.axis_size(axis)
    step = offset % count
    if step == 0:
        return block
    return lax.ppermute(block, axis, [(j, (j - step) % count) for j in range(count)])


def axis_faces(block, axis, dim, prepare=None):
    count = lax.axis_size(axis)
    first = lax.slice_in_dim(block, 0, 1, axis=dim)
    last = lax.slice_in_dim(block, block.shape[dim] - 1, None, axis=dim)
    if prepare is not None:
        first, last = lax.optimization_barrier((prepare(first), prepare(last)))
    if count == 1:
        return last, first
    if count == 2:
        both = lax.ppermute(jnp.concatenate([first, last], axis=dim), axis, [(0, 1), (1, 0)])
        hi = lax.slice_in_dim(both, 0, 1, axis=dim)
        lo = lax.slice_in_dim(both, 1, 2, axis=dim)
        return lo, hi
    lo = shifted(last, axis, -1)
    hi = shifted(first, axis, 1)
    return lo, hi


def all_faces(block, prepare=None):
    return [axis_faces(block, axis, dim, prepare) for axis, dim in GRID_AXES]


def extend_axis(block, axis, dim, halo, extra=None):
    count = lax.axis_size(axis)
    size = block.shape[dim]
    reach = -(-halo // size)
    if 2 * reach + 1 >= count:
        offsets = list(range(count))
        start = 0
    else:
        offsets = list(range(-reach, reach + 1))
        start = reach * size
    cache = {}
    extras = {}
    pieces = []
    for offset in offsets:
        step = offset % count
        if step not in cache:
            if extra is None or step == 0:
                cache[step] = shifted(block, axis, step)
                extras[step] = extra
            else:
                trailing = block.shape[1:]
                if extra.size % int(np.prod(trailing)) == 0:
                    both = jnp.concatenate([block, extra.reshape((-1,) + trailing)], axis=0)
                    both = shifted(both, axis, step)
                    cache[step] = both[: block.shape[0]]
                    extras[step] = both[block.shape[0] :].reshape(extra.shape)
                else:
                    both = jnp.concatenate([block.reshape(-1), extra.reshape(-1)])
                    both = shifted(both, axis, step)
                    cache[step] = both[: block.size].reshape(block.shape)
                    extras[step] = both[block.size :].reshape(extra.shape)
        pieces.append(cache[step])
    return jnp.concatenate(pieces, axis=dim), start, extras


def axis_offsets(count, size, halo):
    reach = -(-halo // size)
    if 2 * reach + 1 >= count:
        return list(range(count)), 0
    return list(range(-reach, reach + 1)), reach * size


def extend_joint(block, axes, dims, halo):
    counts = [lax.axis_size(axis) for axis in axes]
    plans = [axis_offsets(count, block.shape[dim], halo) for count, dim in zip(counts, dims)]
    cache = {}

    def fetch(offset):
        steps = tuple(o % c for o, c in zip(offset, counts))
        if steps not in cache:
            if not any(steps):
                cache[steps] = block
            else:
                pairs = []
                for target in range(_prod(counts)):
                    coords = _unravel(target, counts)
                    source = _ravel([(c + s) % n for c, s, n in zip(coords, steps, counts)], counts)
                    pairs.append((source, target))
                cache[steps] = lax.ppermute(block, tuple(axes), pairs)
        return cache[steps]

    def assemble(level, prefix):
        offsets, start = plans[level]
        if level == len(axes) - 1:
            pieces = [fetch(prefix + (o,)) for o in offsets]
        else:
            pieces = [assemble(level + 1, prefix + (o,)) for o in offsets]
        return jnp.concatenate(pieces, axis=dims[level])

    return assemble(0, ()), [start for offsets, start in plans]


def _prod(values):
    total = 1
    for v in values:
        total *= v
    return total


def _unravel(index, counts):
    coords = []
    for n in reversed(counts):
        coords.append(index % n)
        index //= n
    return list(reversed(coords))


def _ravel(coords, counts):
    index = 0
    for c, n in zip(coords, counts):
        index = index * n + c
    return index


def level_coeffs(level_id):
    coupling = 0.5 / 4.0**level_id
    return (6.0 * coupling + shift_sigma, coupling)


def pad_with(block, faces):
    padded = block
    for dim, (lo, hi) in enumerate(faces):
        widths = [(0, 0)] * block.ndim
        for other in range(dim):
            widths[other] = (1, 1)
        lo = jnp.pad(lo, widths)
        hi = jnp.pad(hi, widths)
        padded = jnp.concatenate([lo, padded, hi], axis=dim)
    return padded


def stencil(block, faces, level_id):
    return padded_stencil(pad_with(block, faces), level_id)


def padded_stencil(padded, level_id):
    center, coupling = level_coeffs(level_id)
    middle = padded[1:-1, 1:-1, 1:-1]
    beside = padded[2:, 1:-1, 1:-1] + padded[:-2, 1:-1, 1:-1]
    beside = beside + padded[1:-1, 2:, 1:-1] + padded[1:-1, :-2, 1:-1]
    beside = beside + padded[1:-1, 1:-1, 2:] + padded[1:-1, 1:-1, :-2]
    return center * middle - coupling * beside


def restrict(field):
    for dim in range(3):
        size = field.shape[dim]
        even = lax.slice_in_dim(field, 0, size, stride=2, axis=dim)
        odd = lax.slice_in_dim(field, 1, size, stride=2, axis=dim)
        field = even + odd
    return field * 0.125


def prolong(field):
    return jnp.repeat(jnp.repeat(jnp.repeat(field, 2, 0), 2, 1), 2, 2)


def coarse_solve(rhs_two, tiles):
    extended = rhs_two
    starts = []
    extended, start, tiles_by_step = extend_axis(extended, "gx", 0, COARSE_HALO, tiles)
    starts.append(start)
    extended, joint_starts = extend_joint(extended, ("gy", "gz"), (1, 2), COARSE_HALO)
    starts.extend(joint_starts)
    grid = extended.shape[:3]
    orbs = extended.shape[3:]
    operator = coarse_matrix(grid, tuple(starts), rhs_two.shape[:3])
    operator = jnp.asarray(operator.reshape((-1,) + tuple(grid)))
    post = jnp.einsum(
        "qxyz,xyzgl->qgl", operator, extended, precision=lax.Precision.HIGHEST, preferred_element_type=jnp.float32
    )
    return post.reshape(tuple(2 * size + 2 for size in rhs_two.shape[:3]) + orbs), tiles_by_step


def coarse_matrix(grid, starts, block):
    cells = int(np.prod(grid))
    field = np.eye(cells).reshape(grid + (cells,))

    def apply(v, level_id):
        center, coupling = level_coeffs(level_id)
        beside = 0.0
        for dim in range(3):
            beside = beside + np.roll(v, -1, dim) + np.roll(v, 1, dim)
        return center * v - coupling * beside

    def shrink(v):
        a, b, c = v.shape[:3]
        return v.reshape(a // 2, 2, b // 2, 2, c // 2, 2, -1).mean(axis=(1, 3, 5))

    def grow(v):
        return np.repeat(np.repeat(np.repeat(v, 2, 0), 2, 1), 2, 2)

    level_two = LEVELS - 2
    center, coupling = level_coeffs(level_two)
    correct_two = omega * field / center
    current = shrink(field - apply(correct_two, level_two))
    top_level = LEVELS - 1
    center_top, coupling_top = level_coeffs(top_level)
    correct = omega * current / center_top
    for sweep_id in range(COARSE - 1):
        correct = correct + omega * (current - apply(correct, top_level)) / center_top
    updated = correct_two + grow(correct)
    post = updated + omega * (field - apply(updated, level_two)) / center
    padded = [2 * size + 2 for size in block]
    for dim in range(3):
        index = [(starts[dim] + (p - 1) // 2) % grid[dim] for p in range(padded[dim])]
        post = np.take(post, index, axis=dim)
    rim = np.zeros(padded, np.int32)
    for dim in range(3):
        edge = np.zeros(padded[dim], np.int32)
        edge[0] = edge[-1] = 1
        rim = rim + edge.reshape([-1 if d == dim else 1 for d in range(3)])
    post = post * (rim <= 1)[..., None]
    post = post.reshape(-1, cells)
    return post.astype(np.float32)


def prolong_face(face, dim):
    for other in range(3):
        if other != dim:
            face = jnp.repeat(face, 2, other)
    return face


def coarse_faces(halo_block, dim):
    inner = halo_block
    for other in range(3):
        if other != dim:
            inner = lax.slice_in_dim(inner, 1, inner.shape[other] - 1, axis=other)
    size = inner.shape[dim]
    lo = lax.slice_in_dim(inner, 0, 1, axis=dim)
    hi = lax.slice_in_dim(inner, size - 1, size, axis=dim)
    return lo, hi


def post_smooth(level_id, corr, corr_faces, rhs, coarse_inner, coarse_face_list):
    center, coupling = level_coeffs(level_id)
    updated = corr + prolong(coarse_inner)
    faces = []
    for dim in range(3):
        lo = corr_faces[dim][0] + prolong_face(coarse_face_list[dim][0], dim)
        hi = corr_faces[dim][1] + prolong_face(coarse_face_list[dim][1], dim)
        faces.append((lo, hi))
    return updated + omega * (rhs - stencil(updated, faces, level_id)) / center


def post_smooth_padded(level_id, corr_padded, rhs, coarse_inner, coarse_face_list):
    center, coupling = level_coeffs(level_id)
    faces = [(prolong_face(lo, dim), prolong_face(hi, dim)) for dim, (lo, hi) in enumerate(coarse_face_list)]
    updated_padded = corr_padded + pad_with(prolong(coarse_inner), faces)
    updated = updated_padded[1:-1, 1:-1, 1:-1]
    return updated + omega * (rhs - padded_stencil(updated_padded, level_id)) / center


def dim_mask(box_part, offset, extent):
    cells = offset + jnp.arange(extent, dtype=jnp.int32)[:, None]
    return ((box_part[0][None, :] <= cells) & (cells < box_part[1][None, :])).astype(jnp.float32)


def gram_matrix(tiles_by_step, inv_tiles, tile_pairs, orb_count):
    count = lax.axis_size("gx")
    local = inv_tiles.shape[0]
    tile_edge = inv_tiles.shape[1]
    blocks = orb_count // tile_edge
    me = lax.axis_index("gx")
    pieces = []
    ids = []
    for step in range(count):
        piece = tiles_by_step.get(step)
        if piece is None:
            piece = inv_tiles if step == 0 else shifted(inv_tiles, "gx", step)
        pieces.append(piece)
        ids.append(((me + step) % count) * local + jnp.arange(local, dtype=jnp.int32))
    tiles = jnp.concatenate(pieces, axis=0)
    pairs = jnp.take(tile_pairs, jnp.concatenate(ids), axis=0)
    block_ids = jnp.arange(blocks, dtype=jnp.int32)
    rows = (pairs[:, 0][:, None] == block_ids[None, :]).astype(jnp.float32)
    cols = (pairs[:, 1][:, None] == block_ids[None, :]).astype(jnp.float32)
    spread = rows[:, :, None, None, None] * cols[:, None, None, :, None] * tiles[:, None, :, None, :]
    return spread.sum(axis=0).reshape(orb_count, orb_count)


def vcycle(residuals, inv_tiles):
    center, coupling = level_coeffs(0)
    faces_zero = all_faces(residuals, lambda part: omega * part.astype(jnp.float32) / center)
    rhs_zero = residuals.astype(jnp.float32)
    corr_zero = omega * rhs_zero / center
    rhs_one = restrict(rhs_zero - stencil(corr_zero, faces_zero, 0))
    center, coupling = level_coeffs(1)
    corr_one = omega * rhs_one / center
    padded_one = pad_with(corr_one, all_faces(corr_one))
    rhs_two = restrict(rhs_one - padded_stencil(padded_one, 1))
    coarse_padded, tiles_by_step = coarse_solve(rhs_two, inv_tiles)
    center, coupling = level_coeffs(1)
    updated_padded = padded_one + coarse_padded
    updated = updated_padded[1:-1, 1:-1, 1:-1]
    post_one = updated + omega * (rhs_one - padded_stencil(updated_padded, 1)) / center
    return post_smooth(0, corr_zero, faces_zero, rhs_zero, post_one, all_faces(post_one)), tiles_by_step


def body(residuals, patch_box, tile_pairs, inv_tiles):
    size_a, size_b, size_c, orb_count = residuals.shape
    lanes = LANES if orb_count % LANES == 0 else orb_count
    grouped = residuals.reshape(size_a, size_b, size_c, orb_count // lanes, lanes)
    correct, tiles_by_step = vcycle(grouped, inv_tiles)
    correct = correct.reshape(size_a, size_b, size_c, orb_count)
    gram = gram_matrix(tiles_by_step, inv_tiles, tile_pairs, orb_count)
    mask_first = dim_mask(patch_box[0], lax.axis_index("gx") * size_a, size_a)
    mask_second = dim_mask(patch_box[1], lax.axis_index("gy") * size_b, size_b)
    mask_third = dim_mask(patch_box[2], lax.axis_index("gz") * size_c, size_c)
    precond = correct * (
        mask_first[:, None, None, :] * mask_second[None, :, None, :] * mask_third[None, None, :, :]
    )
    cell_count = size_a * size_b * size_c
    rows = lax.optimization_barrier(precond.reshape(cell_count, orb_count))
    mixed = jnp.dot(rows, gram, precision=lax.Precision.HIGH, preferred_element_type=jnp.float32)
    return mixed.reshape(size_a, size_b, size_c, orb_count).astype(jnp.bfloat16)


def solution(mesh):
    return jax.shard_map(
        body,
        mesh=mesh,
        in_specs=(P("gx", "gy", "gz", None), P(), P(), P("gx", None, None)),
        out_specs=P("gx", "gy", "gz", None),
        check_vma=False,
    )
```

```python
import jax
import jax.numpy as jnp
import numpy as np
from jax import lax
from jax.sharding import PartitionSpec as P

LEVELS = 4
COARSE = 4


omega = 0.8
shift_sigma = 0.01

GRID_AXES = (("gx", 0), ("gy", 1), ("gz", 2))
COARSE_HALO = 10
LANES = 128


def shifted(block, axis, offset):
    count = lax.axis_size(axis)
    step = offset % count
    if step == 0:
        return block
    return lax.ppermute(block, axis, [(j, (j - step) % count) for j in range(count)])


def axis_faces(block, axis, dim, prepare=None, slabs=None):
    count = lax.axis_size(axis)
    if slabs is not None:
        first, last = slabs
    else:
        first = lax.slice_in_dim(block, 0, 1, axis=dim)
        last = lax.slice_in_dim(block, block.shape[dim] - 1, None, axis=dim)
    if prepare is not None:
        first = prepare(first)
        last = prepare(last)
    if count == 1:
        return last, first
    if count == 2:
        both = lax.ppermute(jnp.concatenate([first, last], axis=dim), axis, [(0, 1), (1, 0)])
        hi = lax.slice_in_dim(both, 0, 1, axis=dim)
        lo = lax.slice_in_dim(both, 1, 2, axis=dim)
        return lo, hi
    lo = shifted(last, axis, -1)
    hi = shifted(first, axis, 1)
    return lo, hi


def all_faces(block, prepare=None):
    return [axis_faces(block, axis, dim, prepare) for axis, dim in GRID_AXES]


def extend_axis(block, axis, dim, halo, extra=None):
    count = lax.axis_size(axis)
    size = block.shape[dim]
    reach = -(-halo // size)
    if 2 * reach + 1 >= count:
        offsets = list(range(count))
        start = 0
    else:
        offsets = list(range(-reach, reach + 1))
        start = reach * size
    cache = {}
    extras = {}
    pieces = []
    for offset in offsets:
        step = offset % count
        if step not in cache:
            if extra is None or step == 0:
                cache[step] = shifted(block, axis, step)
                extras[step] = extra
            else:
                trailing = block.shape[1:]
                if extra.size % int(np.prod(trailing)) == 0:
                    both = jnp.concatenate([block, extra.reshape((-1,) + trailing)], axis=0)
                    both = shifted(both, axis, step)
                    cache[step] = both[: block.shape[0]]
                    extras[step] = both[block.shape[0] :].reshape(extra.shape)
                else:
                    both = jnp.concatenate([block.reshape(-1), extra.reshape(-1)])
                    both = shifted(both, axis, step)
                    cache[step] = both[: block.size].reshape(block.shape)
                    extras[step] = both[block.size :].reshape(extra.shape)
        pieces.append(cache[step])
    return jnp.concatenate(pieces, axis=dim), start, extras


def axis_offsets(count, size, halo):
    reach = -(-halo // size)
    if 2 * reach + 1 >= count:
        return list(range(count)), 0
    return list(range(-reach, reach + 1)), reach * size


def extend_joint(block, axes, dims, halo):
    counts = [lax.axis_size(axis) for axis in axes]
    plans = [axis_offsets(count, block.shape[dim], halo) for count, dim in zip(counts, dims)]
    cache = {}

    def fetch(offset):
        steps = tuple(o % c for o, c in zip(offset, counts))
        if steps not in cache:
            if not any(steps):
                cache[steps] = block
            else:
                pairs = []
                for target in range(_prod(counts)):
                    coords = _unravel(target, counts)
                    source = _ravel([(c + s) % n for c, s, n in zip(coords, steps, counts)], counts)
                    pairs.append((source, target))
                cache[steps] = lax.ppermute(block, tuple(axes), pairs)
        return cache[steps]

    def assemble(level, prefix):
        offsets, start = plans[level]
        if level == len(axes) - 1:
            pieces = [fetch(prefix + (o,)) for o in offsets]
        else:
            pieces = [assemble(level + 1, prefix + (o,)) for o in offsets]
        return jnp.concatenate(pieces, axis=dims[level])

    return assemble(0, ()), [start for offsets, start in plans]


def _prod(values):
    total = 1
    for v in values:
        total *= v
    return total


def _unravel(index, counts):
    coords = []
    for n in reversed(counts):
        coords.append(index % n)
        index //= n
    return list(reversed(coords))


def _ravel(coords, counts):
    index = 0
    for c, n in zip(coords, counts):
        index = index * n + c
    return index


def level_coeffs(level_id):
    coupling = 0.5 / 4.0**level_id
    return (6.0 * coupling + shift_sigma, coupling)


def pad_with(block, faces):
    padded = block
    for dim, (lo, hi) in enumerate(faces):
        widths = [(0, 0)] * block.ndim
        for other in range(dim):
            widths[other] = (1, 1)
        lo = jnp.pad(lo, widths)
        hi = jnp.pad(hi, widths)
        padded = jnp.concatenate([lo, padded, hi], axis=dim)
    return padded


def stencil(block, faces, level_id):
    return padded_stencil(pad_with(block, faces), level_id)


def padded_stencil(padded, level_id):
    center, coupling = level_coeffs(level_id)
    middle = padded[1:-1, 1:-1, 1:-1]
    beside = padded[2:, 1:-1, 1:-1] + padded[:-2, 1:-1, 1:-1]
    beside = beside + padded[1:-1, 2:, 1:-1] + padded[1:-1, :-2, 1:-1]
    beside = beside + padded[1:-1, 1:-1, 2:] + padded[1:-1, 1:-1, :-2]
    return center * middle - coupling * beside


def restrict(field):
    for dim in range(3):
        size = field.shape[dim]
        even = lax.slice_in_dim(field, 0, size, stride=2, axis=dim)
        odd = lax.slice_in_dim(field, 1, size, stride=2, axis=dim)
        field = even + odd
    return field * 0.125


def prolong(field):
    return jnp.repeat(jnp.repeat(jnp.repeat(field, 2, 0), 2, 1), 2, 2)


def coarse_solve(rhs_two, tiles):
    extended = rhs_two
    starts = []
    extended, start, tiles_by_step = extend_axis(extended, "gx", 0, COARSE_HALO, tiles)
    starts.append(start)
    extended, joint_starts = extend_joint(extended, ("gy", "gz"), (1, 2), COARSE_HALO)
    starts.extend(joint_starts)
    grid = extended.shape[:3]
    orbs = extended.shape[3:]
    operator = coarse_matrix(grid, tuple(starts), rhs_two.shape[:3])
    operator = jnp.asarray(operator.reshape((-1,) + tuple(grid)))
    post = jnp.einsum(
        "qxyz,xyzgl->qgl", operator, extended, precision=lax.Precision.HIGHEST, preferred_element_type=jnp.float32
    )
    return post.reshape(tuple(2 * size + 2 for size in rhs_two.shape[:3]) + orbs), tiles_by_step


def coarse_matrix(grid, starts, block):
    cells = int(np.prod(grid))
    field = np.eye(cells).reshape(grid + (cells,))

    def apply(v, level_id):
        center, coupling = level_coeffs(level_id)
        beside = 0.0
        for dim in range(3):
            beside = beside + np.roll(v, -1, dim) + np.roll(v, 1, dim)
        return center * v - coupling * beside

    def shrink(v):
        a, b, c = v.shape[:3]
        return v.reshape(a // 2, 2, b // 2, 2, c // 2, 2, -1).mean(axis=(1, 3, 5))

    def grow(v):
        return np.repeat(np.repeat(np.repeat(v, 2, 0), 2, 1), 2, 2)

    level_two = LEVELS - 2
    center, coupling = level_coeffs(level_two)
    correct_two = omega * field / center
    current = shrink(field - apply(correct_two, level_two))
    top_level = LEVELS - 1
    center_top, coupling_top = level_coeffs(top_level)
    correct = omega * current / center_top
    for sweep_id in range(COARSE - 1):
        correct = correct + omega * (current - apply(correct, top_level)) / center_top
    updated = correct_two + grow(correct)
    post = updated + omega * (field - apply(updated, level_two)) / center
    padded = [2 * size + 2 for size in block]
    for dim in range(3):
        index = [(starts[dim] + (p - 1) // 2) % grid[dim] for p in range(padded[dim])]
        post = np.take(post, index, axis=dim)
    rim = np.zeros(padded, np.int32)
    for dim in range(3):
        edge = np.zeros(padded[dim], np.int32)
        edge[0] = edge[-1] = 1
        rim = rim + edge.reshape([-1 if d == dim else 1 for d in range(3)])
    post = post * (rim <= 1)[..., None]
    post = post.reshape(-1, cells)
    return post.astype(np.float32)


def prolong_face(face, dim):
    for other in range(3):
        if other != dim:
            face = jnp.repeat(face, 2, other)
    return face


def coarse_faces(halo_block, dim):
    inner = halo_block
    for other in range(3):
        if other != dim:
            inner = lax.slice_in_dim(inner, 1, inner.shape[other] - 1, axis=other)
    size = inner.shape[dim]
    lo = lax.slice_in_dim(inner, 0, 1, axis=dim)
    hi = lax.slice_in_dim(inner, size - 1, size, axis=dim)
    return lo, hi


def post_smooth(level_id, corr, corr_faces, rhs, coarse_inner, coarse_face_list):
    center, coupling = level_coeffs(level_id)
    updated = corr + prolong(coarse_inner)
    faces = []
    for dim in range(3):
        lo = corr_faces[dim][0] + prolong_face(coarse_face_list[dim][0], dim)
        hi = corr_faces[dim][1] + prolong_face(coarse_face_list[dim][1], dim)
        faces.append((lo, hi))
    return updated + omega * (rhs - stencil(updated, faces, level_id)) / center


def post_smooth_padded(level_id, corr_padded, rhs, coarse_inner, coarse_face_list):
    center, coupling = level_coeffs(level_id)
    faces = [(prolong_face(lo, dim), prolong_face(hi, dim)) for dim, (lo, hi) in enumerate(coarse_face_list)]
    updated_padded = corr_padded + pad_with(prolong(coarse_inner), faces)
    updated = updated_padded[1:-1, 1:-1, 1:-1]
    return updated + omega * (rhs - padded_stencil(updated_padded, level_id)) / center


def dim_mask(box_part, offset, extent):
    cells = offset + jnp.arange(extent, dtype=jnp.int32)[:, None]
    return ((box_part[0][None, :] <= cells) & (cells < box_part[1][None, :])).astype(jnp.float32)


def gram_matrix(tiles_by_step, inv_tiles, tile_pairs, orb_count):
    count = lax.axis_size("gx")
    local = inv_tiles.shape[0]
    tile_edge = inv_tiles.shape[1]
    blocks = orb_count // tile_edge
    me = lax.axis_index("gx")
    pieces = []
    ids = []
    for step in range(count):
        piece = tiles_by_step.get(step)
        if piece is None:
            piece = inv_tiles if step == 0 else shifted(inv_tiles, "gx", step)
        pieces.append(piece)
        ids.append(((me + step) % count) * local + jnp.arange(local, dtype=jnp.int32))
    tiles = jnp.concatenate(pieces, axis=0)
    pairs = jnp.take(tile_pairs, jnp.concatenate(ids), axis=0)
    block_ids = jnp.arange(blocks, dtype=jnp.int32)
    rows = (pairs[:, 0][:, None] == block_ids[None, :]).astype(jnp.float32)
    cols = (pairs[:, 1][:, None] == block_ids[None, :]).astype(jnp.float32)
    spread = rows[:, :, None, None, None] * cols[:, None, None, :, None] * tiles[:, None, :, None, :]
    return spread.sum(axis=0).reshape(orb_count, orb_count)


def vcycle(residuals, inv_tiles):
    center, coupling = level_coeffs(0)
    faces_zero = all_faces(residuals, lambda part: omega * part.astype(jnp.float32) / center)
    rhs_zero = residuals.astype(jnp.float32)
    corr_zero = omega * rhs_zero / center
    rhs_one = restrict(rhs_zero - stencil(corr_zero, faces_zero, 0))
    center, coupling = level_coeffs(1)
    corr_one = omega * rhs_one / center
    padded_one = pad_with(corr_one, all_faces(corr_one))
    rhs_two = restrict(rhs_one - padded_stencil(padded_one, 1))
    coarse_padded, tiles_by_step = coarse_solve(rhs_two, inv_tiles)
    center, coupling = level_coeffs(1)
    updated_padded = padded_one + coarse_padded
    updated = updated_padded[1:-1, 1:-1, 1:-1]
    post_one = updated + omega * (rhs_one - padded_stencil(updated_padded, 1)) / center
    slabs = []
    for dim in range(3):
        pair = []
        for lo_side in (True, False):
            size = updated_padded.shape[dim]
            part = lax.slice_in_dim(updated_padded, 0 if lo_side else size - 3, 3 if lo_side else size, axis=dim)
            inner = rhs_one.shape[dim]
            rhs = lax.slice_in_dim(rhs_one, 0 if lo_side else inner - 1, 1 if lo_side else inner, axis=dim)
            mid = part[1:-1, 1:-1, 1:-1]
            pair.append(mid + omega * (rhs - padded_stencil(part, 1)) / center)
        slabs.append(tuple(pair))
    faces_one = [axis_faces(None, axis, dim, slabs=slabs[dim]) for axis, dim in GRID_AXES]
    return post_smooth(0, corr_zero, faces_zero, rhs_zero, post_one, faces_one), tiles_by_step


def body(residuals, patch_box, tile_pairs, inv_tiles):
    size_a, size_b, size_c, orb_count = residuals.shape
    lanes = LANES if orb_count % LANES == 0 else orb_count
    grouped = residuals.reshape(size_a, size_b, size_c, orb_count // lanes, lanes)
    correct, tiles_by_step = vcycle(grouped, inv_tiles)
    correct = correct.reshape(size_a, size_b, size_c, orb_count)
    gram = gram_matrix(tiles_by_step, inv_tiles, tile_pairs, orb_count)
    mask_first = dim_mask(patch_box[0], lax.axis_index("gx") * size_a, size_a)
    mask_second = dim_mask(patch_box[1], lax.axis_index("gy") * size_b, size_b)
    mask_third = dim_mask(patch_box[2], lax.axis_index("gz") * size_c, size_c)
    precond = correct * (
        mask_first[:, None, None, :] * mask_second[None, :, None, :] * mask_third[None, None, :, :]
    )
    cell_count = size_a * size_b * size_c
    rows = lax.optimization_barrier(precond.reshape(cell_count, orb_count))
    mixed = jnp.dot(rows, gram, precision=lax.Precision.HIGH, preferred_element_type=jnp.float32)
    return mixed.reshape(size_a, size_b, size_c, orb_count).astype(jnp.bfloat16)


def solution(mesh):
    return jax.shard_map(
        body,
        mesh=mesh,
        in_specs=(P("gx", "gy", "gz", None), P(), P(), P("gx", None, None)),
        out_specs=P("gx", "gy", "gz", None),
        check_vma=False,
    )
```

```python
import jax
import jax.numpy as jnp
import numpy as np
from jax import lax
from jax.sharding import PartitionSpec as P

LEVELS = 4
COARSE = 4


omega = 0.8
shift_sigma = 0.01

GRID_AXES = (("gx", 0), ("gy", 1), ("gz", 2))
COARSE_HALO = 10
LANES = 128


def shifted(block, axis, offset):
    count = lax.axis_size(axis)
    step = offset % count
    if step == 0:
        return block
    return lax.ppermute(block, axis, [(j, (j - step) % count) for j in range(count)])


def axis_faces(block, axis, dim, prepare=None):
    count = lax.axis_size(axis)
    first = lax.slice_in_dim(block, 0, 1, axis=dim)
    last = lax.slice_in_dim(block, block.shape[dim] - 1, None, axis=dim)
    if prepare is not None:
        first = prepare(first)
        last = prepare(last)
    if count == 1:
        return last, first
    if count == 2:
        both = lax.ppermute(jnp.concatenate([first, last], axis=dim), axis, [(0, 1), (1, 0)])
        hi = lax.slice_in_dim(both, 0, 1, axis=dim)
        lo = lax.slice_in_dim(both, 1, 2, axis=dim)
        return lo, hi
    lo = shifted(last, axis, -1)
    hi = shifted(first, axis, 1)
    return lo, hi


def all_faces(block, prepare=None):
    return [axis_faces(block, axis, dim, prepare) for axis, dim in GRID_AXES]


def extend_axis(block, axis, dim, halo, extra=None):
    count = lax.axis_size(axis)
    size = block.shape[dim]
    reach = -(-halo // size)
    if 2 * reach + 1 >= count:
        offsets = list(range(count))
        start = 0
    else:
        offsets = list(range(-reach, reach + 1))
        start = reach * size
    cache = {}
    extras = {}
    pieces = []
    for offset in offsets:
        step = offset % count
        if step not in cache:
            if extra is None or step == 0:
                cache[step] = shifted(block, axis, step)
                extras[step] = extra
            else:
                trailing = block.shape[1:]
                if extra.size % int(np.prod(trailing)) == 0:
                    both = jnp.concatenate([block, extra.reshape((-1,) + trailing)], axis=0)
                    both = shifted(both, axis, step)
                    cache[step] = both[: block.shape[0]]
                    extras[step] = both[block.shape[0] :].reshape(extra.shape)
                else:
                    both = jnp.concatenate([block.reshape(-1), extra.reshape(-1)])
                    both = shifted(both, axis, step)
                    cache[step] = both[: block.size].reshape(block.shape)
                    extras[step] = both[block.size :].reshape(extra.shape)
        pieces.append(cache[step])
    return jnp.concatenate(pieces, axis=dim), start, extras


def axis_offsets(count, size, halo):
    reach = -(-halo // size)
    if 2 * reach + 1 >= count:
        return list(range(count)), 0
    return list(range(-reach, reach + 1)), reach * size


def extend_joint(block, axes, dims, halo):
    counts = [lax.axis_size(axis) for axis in axes]
    plans = [axis_offsets(count, block.shape[dim], halo) for count, dim in zip(counts, dims)]
    cache = {}

    def fetch(offset):
        steps = tuple(o % c for o, c in zip(offset, counts))
        if steps not in cache:
            if not any(steps):
                cache[steps] = block
            else:
                pairs = []
                for target in range(_prod(counts)):
                    coords = _unravel(target, counts)
                    source = _ravel([(c + s) % n for c, s, n in zip(coords, steps, counts)], counts)
                    pairs.append((source, target))
                cache[steps] = lax.ppermute(block, tuple(axes), pairs)
        return cache[steps]

    def assemble(level, prefix):
        offsets, start = plans[level]
        if level == len(axes) - 1:
            pieces = [fetch(prefix + (o,)) for o in offsets]
        else:
            pieces = [assemble(level + 1, prefix + (o,)) for o in offsets]
        return jnp.concatenate(pieces, axis=dims[level])

    return assemble(0, ()), [start for offsets, start in plans]


def _prod(values):
    total = 1
    for v in values:
        total *= v
    return total


def _unravel(index, counts):
    coords = []
    for n in reversed(counts):
        coords.append(index % n)
        index //= n
    return list(reversed(coords))


def _ravel(coords, counts):
    index = 0
    for c, n in zip(coords, counts):
        index = index * n + c
    return index


def level_coeffs(level_id):
    coupling = 0.5 / 4.0**level_id
    return (6.0 * coupling + shift_sigma, coupling)


def pad_with(block, faces):
    padded = block
    for dim, (lo, hi) in enumerate(faces):
        widths = [(0, 0)] * block.ndim
        for other in range(dim):
            widths[other] = (1, 1)
        lo = jnp.pad(lo, widths)
        hi = jnp.pad(hi, widths)
        padded = jnp.concatenate([lo, padded, hi], axis=dim)
    return padded


def stencil(block, faces, level_id):
    return padded_stencil(pad_with(block, faces), level_id)


def padded_stencil(padded, level_id):
    center, coupling = level_coeffs(level_id)
    middle = padded[1:-1, 1:-1, 1:-1]
    beside = padded[2:, 1:-1, 1:-1] + padded[:-2, 1:-1, 1:-1]
    beside = beside + padded[1:-1, 2:, 1:-1] + padded[1:-1, :-2, 1:-1]
    beside = beside + padded[1:-1, 1:-1, 2:] + padded[1:-1, 1:-1, :-2]
    return center * middle - coupling * beside


def restrict(field):
    for dim in range(3):
        size = field.shape[dim]
        even = lax.slice_in_dim(field, 0, size, stride=2, axis=dim)
        odd = lax.slice_in_dim(field, 1, size, stride=2, axis=dim)
        field = even + odd
    return field * 0.125


def prolong(field):
    return jnp.repeat(jnp.repeat(jnp.repeat(field, 2, 0), 2, 1), 2, 2)


def coarse_solve(rhs_two, tiles):
    extended = rhs_two
    starts = []
    extended, start, tiles_by_step = extend_axis(extended, "gx", 0, COARSE_HALO, tiles)
    starts.append(start)
    extended, joint_starts = extend_joint(extended, ("gy", "gz"), (1, 2), COARSE_HALO)
    starts.extend(joint_starts)
    grid = extended.shape[:3]
    orbs = extended.shape[3:]
    operator = coarse_matrix(grid, tuple(starts), rhs_two.shape[:3])
    operator = jnp.asarray(operator.reshape((-1,) + tuple(grid)))
    post = jnp.einsum(
        "qxyz,xyzgl->qgl", operator, extended, precision=lax.Precision.HIGH, preferred_element_type=jnp.float32
    )
    return post.reshape(tuple(2 * size + 2 for size in rhs_two.shape[:3]) + orbs), tiles_by_step


def coarse_matrix(grid, starts, block):
    cells = int(np.prod(grid))
    field = np.eye(cells).reshape(grid + (cells,))

    def apply(v, level_id):
        center, coupling = level_coeffs(level_id)
        beside = 0.0
        for dim in range(3):
            beside = beside + np.roll(v, -1, dim) + np.roll(v, 1, dim)
        return center * v - coupling * beside

    def shrink(v):
        a, b, c = v.shape[:3]
        return v.reshape(a // 2, 2, b // 2, 2, c // 2, 2, -1).mean(axis=(1, 3, 5))

    def grow(v):
        return np.repeat(np.repeat(np.repeat(v, 2, 0), 2, 1), 2, 2)

    level_two = LEVELS - 2
    center, coupling = level_coeffs(level_two)
    correct_two = omega * field / center
    current = shrink(field - apply(correct_two, level_two))
    top_level = LEVELS - 1
    center_top, coupling_top = level_coeffs(top_level)
    correct = omega * current / center_top
    for sweep_id in range(COARSE - 1):
        correct = correct + omega * (current - apply(correct, top_level)) / center_top
    updated = correct_two + grow(correct)
    post = updated + omega * (field - apply(updated, level_two)) / center
    padded = [2 * size + 2 for size in block]
    for dim in range(3):
        index = [(starts[dim] + (p - 1) // 2) % grid[dim] for p in range(padded[dim])]
        post = np.take(post, index, axis=dim)
    rim = np.zeros(padded, np.int32)
    for dim in range(3):
        edge = np.zeros(padded[dim], np.int32)
        edge[0] = edge[-1] = 1
        rim = rim + edge.reshape([-1 if d == dim else 1 for d in range(3)])
    post = post * (rim <= 1)[..., None]
    post = post.reshape(-1, cells)
    return post.astype(np.float32)


def prolong_face(face, dim):
    for other in range(3):
        if other != dim:
            face = jnp.repeat(face, 2, other)
    return face


def coarse_faces(halo_block, dim):
    inner = halo_block
    for other in range(3):
        if other != dim:
            inner = lax.slice_in_dim(inner, 1, inner.shape[other] - 1, axis=other)
    size = inner.shape[dim]
    lo = lax.slice_in_dim(inner, 0, 1, axis=dim)
    hi = lax.slice_in_dim(inner, size - 1, size, axis=dim)
    return lo, hi


def post_smooth(level_id, corr, corr_faces, rhs, coarse_inner, coarse_face_list):
    center, coupling = level_coeffs(level_id)
    updated = corr + prolong(coarse_inner)
    faces = []
    for dim in range(3):
        lo = corr_faces[dim][0] + prolong_face(coarse_face_list[dim][0], dim)
        hi = corr_faces[dim][1] + prolong_face(coarse_face_list[dim][1], dim)
        faces.append((lo, hi))
    return updated + omega * (rhs - stencil(updated, faces, level_id)) / center


def post_smooth_padded(level_id, corr_padded, rhs, coarse_inner, coarse_face_list):
    center, coupling = level_coeffs(level_id)
    faces = [(prolong_face(lo, dim), prolong_face(hi, dim)) for dim, (lo, hi) in enumerate(coarse_face_list)]
    updated_padded = corr_padded + pad_with(prolong(coarse_inner), faces)
    updated = updated_padded[1:-1, 1:-1, 1:-1]
    return updated + omega * (rhs - padded_stencil(updated_padded, level_id)) / center


def dim_mask(box_part, offset, extent):
    cells = offset + jnp.arange(extent, dtype=jnp.int32)[:, None]
    return ((box_part[0][None, :] <= cells) & (cells < box_part[1][None, :])).astype(jnp.float32)


def gram_matrix(tiles_by_step, inv_tiles, tile_pairs, orb_count):
    count = lax.axis_size("gx")
    local = inv_tiles.shape[0]
    tile_edge = inv_tiles.shape[1]
    blocks = orb_count // tile_edge
    me = lax.axis_index("gx")
    pieces = []
    ids = []
    for step in range(count):
        piece = tiles_by_step.get(step)
        if piece is None:
            piece = inv_tiles if step == 0 else shifted(inv_tiles, "gx", step)
        pieces.append(piece)
        ids.append(((me + step) % count) * local + jnp.arange(local, dtype=jnp.int32))
    tiles = jnp.concatenate(pieces, axis=0)
    pairs = jnp.take(tile_pairs, jnp.concatenate(ids), axis=0)
    block_ids = jnp.arange(blocks, dtype=jnp.int32)
    rows = (pairs[:, 0][:, None] == block_ids[None, :]).astype(jnp.float32)
    cols = (pairs[:, 1][:, None] == block_ids[None, :]).astype(jnp.float32)
    spread = rows[:, :, None, None, None] * cols[:, None, None, :, None] * tiles[:, None, :, None, :]
    return spread.sum(axis=0).reshape(orb_count, orb_count)


def vcycle(residuals, inv_tiles):
    center, coupling = level_coeffs(0)
    faces_zero = all_faces(residuals, lambda part: omega * part.astype(jnp.float32) / center)
    rhs_zero = residuals.astype(jnp.float32)
    corr_zero = omega * rhs_zero / center
    rhs_one = restrict(rhs_zero - stencil(corr_zero, faces_zero, 0))
    center, coupling = level_coeffs(1)
    corr_one = omega * rhs_one / center
    padded_one = pad_with(corr_one, all_faces(corr_one))
    rhs_two = restrict(rhs_one - padded_stencil(padded_one, 1))
    coarse_padded, tiles_by_step = coarse_solve(rhs_two, inv_tiles)
    center, coupling = level_coeffs(1)
    updated_padded = padded_one + coarse_padded
    updated = updated_padded[1:-1, 1:-1, 1:-1]
    post_one = updated + omega * (rhs_one - padded_stencil(updated_padded, 1)) / center
    return post_smooth(0, corr_zero, faces_zero, rhs_zero, post_one, all_faces(post_one)), tiles_by_step


def body(residuals, patch_box, tile_pairs, inv_tiles):
    size_a, size_b, size_c, orb_count = residuals.shape
    lanes = LANES if orb_count % LANES == 0 else orb_count
    grouped = residuals.reshape(size_a, size_b, size_c, orb_count // lanes, lanes)
    correct, tiles_by_step = vcycle(grouped, inv_tiles)
    correct = correct.reshape(size_a, size_b, size_c, orb_count)
    gram = gram_matrix(tiles_by_step, inv_tiles, tile_pairs, orb_count)
    mask_first = dim_mask(patch_box[0], lax.axis_index("gx") * size_a, size_a)
    mask_second = dim_mask(patch_box[1], lax.axis_index("gy") * size_b, size_b)
    mask_third = dim_mask(patch_box[2], lax.axis_index("gz") * size_c, size_c)
    precond = correct * (
        mask_first[:, None, None, :] * mask_second[None, :, None, :] * mask_third[None, None, :, :]
    )
    cell_count = size_a * size_b * size_c
    rows = lax.optimization_barrier(precond.reshape(cell_count, orb_count))
    mixed = jnp.dot(rows, gram, precision=lax.Precision.HIGH, preferred_element_type=jnp.float32)
    return mixed.reshape(size_a, size_b, size_c, orb_count).astype(jnp.bfloat16)


def solution(mesh):
    return jax.shard_map(
        body,
        mesh=mesh,
        in_specs=(P("gx", "gy", "gz", None), P(), P(), P("gx", None, None)),
        out_specs=P("gx", "gy", "gz", None),
        check_vma=False,
    )
```
